32 devices in a mesh: req: 16 (over z, x, core), ep: 2 (over y).
Axes of the slice: x: 2, y: 2, z: 4, core: 2. Of those that a mesh axis runs over, the one named last changes fastest.
Arguments:
- hidden: bfloat16 [16, 512, 1536], P('req', None, 'ep'), may hold values from -6 to 6
- key_cache: bfloat16 [16, 8, 2560, 64], P('req', 'ep'), may hold values from -160 to 160
- value_cache: bfloat16 [16, 8, 2560, 64], P('req', 'ep'), may hold values from -6 to 6
- request_order: int32 [16], replicated, may hold values from 0 to 15, each once
- cached_lengths: int32 [16], replicated, may hold values from 1 to 2048, 16384 in all
- expert_ids: int32 [16, 512, 8], P('req'), may hold values from 0 to 39, all different within a row; in each aligned block of 512 rows (0 to 511, 512 to 1023, ..., all dimensions but the last counted through in order) at most 192 rows name the same one
- gate_values: float32 [16, 512, 8], P('req'), may hold values from 0.1 to 1
- attn_gain: float32 [1536], replicated, may hold values from 0.25 to 1.75
- ffn_gain: float32 [1536], replicated, may hold values from 0.25 to 1.75
- w_query: bfloat16 [1536, 1536], P(None, 'ep'), may hold values from -0.15625 to 0.15625
- w_key: bfloat16 [1536, 512], P(None, 'ep'), may hold values from -0.15625 to 0.15625
- w_value: bfloat16 [1536, 512], P(None, 'ep'), may hold values from -0.15625 to 0.15625
- w_out: bfloat16 [1536, 1536], P('ep'), may hold values from -0.15625 to 0.15625
- expert_gate: bfloat16 [4, 1536, 512], P('ep', 'req'), may hold values from -0.15625 to 0.15625
- expert_up: bfloat16 [4, 1536, 512], P('ep', 'req'), may hold values from -0.15625 to 0.15625
- expert_down: bfloat16 [4, 512, 1536], P('ep', 'req'), may hold values from -0.25 to 0.25
Outputs:
- hidden_out: bfloat16 [16, 512, 1536], P('req', None, 'ep')
- key_cache_out: bfloat16 [16, 8, 2560, 64], P('req', 'ep')
- value_cache_out: bfloat16 [16, 8, 2560, 64], P('req', 'ep')
The draws below stay inside these ranges and needn't reach their ends.
Inputs may be any that keep to these rules, and one draw needn't show every extreme that they name: Slot s holds request request_order[s]; every request is held by one slot. `cached_lengths`: the longest cached length is exactly 2048. `expert_ids`: each token names 8 different experts; among the 512 tokens of one slot no expert is named by more than 192 tokens, a bound that some block reaches.
All inputs are finite; a program needn't handle non-finite values.
Results may differ from the reference program's by a relative error of at most 0.012.
The reference program's roundings to bfloat16 on the way count: a program that leaves them out, or rounds other values in their place, can miss the bound.
Values may be sent and summed in bfloat16 or wider, within the bound.
No kernel may reach another device: no remote copies, remote signals or barrier semaphores. Data moves between devices by JAX's collectives and lax.ppermute only.
A program may use at most 128 MiB of HBM per device.

```python
import math
import jax
import jax.numpy as jnp
import numpy as np
from jax import lax

D = 1536
QH = 24
KVH = 8
HD = 64
EXPERTS = 40
FF = 512
TOPK = 8
NEW = 512
MAXLEN = 2048
EXP_DEV = 2
REQUESTS = 16
CAPE = 192
CAPC = 2560
W_EXPERTS = 4
N_EP = 2


def draw_key_cache(key, part):
    base = jax.random.normal(key, (REQUESTS, KVH, CAPC, HD), jnp.float32)
    return jnp.clip(base, -160.0, 160.0).astype(jnp.bfloat16)


def shard_levels(own_key, dims, pieces, low, largest):
    factor_of = 1.0
    for position, shards_of in pieces:
        steps = jax.random.uniform(jax.random.fold_in(jax.random.fold_in(own_key, 6), position), (shards_of,), jnp.float32, low / len(pieces), largest / len(pieces))
        factor_of = factor_of * jnp.repeat(jnp.exp(steps), dims[position] // shards_of).reshape((-1,) + (1,) * (len(dims) - 1 - position))
    return factor_of


def split_up(number_of, total, limit, slope):
    weights = [(1 << 20) // math.isqrt(grade ** slope) + 1 for grade in range(2, number_of + 1)]
    spare, counts = total - limit - (number_of - 1), [1] * (number_of - 1)
    while spare > 0:
        candidates = [i for i in range(number_of - 1) if counts[i] < limit]
        whole, left = sum([weights[i] for i in candidates]), spare
        for i in candidates:
            extra = min(limit - counts[i], max(1, left * weights[i] // whole), spare)
            counts[i] = counts[i] + extra
            spare = spare - extra
    return np.array([limit] + counts)


def uneven(own_key, count, total, bound, slope):
    if count == 2:
        one = jax.random.randint(own_key, (), max(1, total - bound), min(bound, total - 1) + 1)
        return jnp.stack([one, total - one])
    tallies = jnp.asarray(split_up(count, total, bound, slope), jnp.int32)
    pairs = (count - 1) // 2
    giver, sink = tallies[1:1 + 2 * pairs:2], tallies[2:2 + 2 * pairs:2]
    margin = jnp.minimum(giver - 1, bound - sink)
    shifted = jax.random.randint(jax.random.fold_in(own_key, 1), (pairs,), 0, 1 << 20) % (margin + 1)
    tallies = tallies.at[1:1 + 2 * pairs:2].set(giver - shifted).at[2:2 + 2 * pairs:2].set(sink + shifted)
    return tallies[jax.random.permutation(jax.random.fold_in(own_key, 2), count)]


def assign_block(own_key, own, number, rows, count, top, reach, lean):
    ranking = jax.random.permutation(own_key, count)
    packed, common = shares(count, rows * top, reach, lean, True), shares(count, rows * top, reach, lean, False)
    places = jnp.arange(count)

    def named(tallies, rotation):
        used = int((tallies > 0).sum())
        fixed = max(1, used // 4)
        passed = fixed + (places - fixed + rotation * (used - fixed)) % max(1, count - fixed)
        return jnp.zeros((count,), jnp.int32).at[ranking[jnp.where(places < fixed, places, passed)]].set(jnp.asarray(tallies, jnp.int32))

    tallies = jnp.where(number % 4 == 0, named(packed, number // 4), named(common, number - number // 4 - 1))
    mixed = jax.random.permutation(jax.random.fold_in(own, 3), count)
    giver, receiver = mixed[0:count // 2 * 2:2], mixed[1:count // 2 * 2:2]
    room = jnp.minimum(tallies[giver] - 1, reach - tallies[receiver]) // 2
    room = jnp.where((giver == ranking[0]) | (receiver == ranking[0]) | (tallies[receiver] == 0), 0, jnp.maximum(room, 0))
    passed = jax.random.randint(jax.random.fold_in(own, 4), (count // 2,), 0, 1 << 20) % (room + 1)
    tallies = tallies.at[giver].add(-passed).at[receiver].add(passed)
    items = jnp.searchsorted(jnp.cumsum(tallies), jnp.arange(rows * top), side="right").astype(jnp.int32)
    grid = items.reshape(top, rows).T
    grid = grid[jax.random.permutation(jax.random.fold_in(own, 1), rows)]
    rotation = jax.random.randint(jax.random.fold_in(own, 2), (rows, 1), 0, top)
    return jnp.take_along_axis(grid, (jnp.arange(top)[None, :] + rotation) % top, axis=1)


def shares(amount, total, limit, slope, full):
    portions = [(1 << 20) // math.isqrt(standing ** slope) + 1 for standing in range(1, amount + 1)]
    largest = limit if full else min(limit, max(-(-total // amount), total * portions[0] // sum(portions)))
    least = 1 if total - largest >= amount - 1 else 0
    given, spare = [largest] + [least] * (amount - 1), total - largest - least * (amount - 1)
    while spare > 0:
        movable = [i for i in range(1, amount) if given[i] < largest] or [i for i in range(1, amount) if given[i] < limit]
        pool, left = sum([portions[i] for i in movable]), spare
        for i in movable:
            extra = min(limit - given[i], max(1, left * portions[i] // pool), spare)
            given[i] = given[i] + extra
            spare = spare - extra
    return np.array(given)


def centred(stream_key, dims, deviation, reach, shards=(), kind=jnp.bfloat16):
    drawn = jax.random.normal(stream_key, dims, jnp.float32) * deviation
    if len(shards) > 0:
        drawn = shard_levels(stream_key, dims, shards, -0.22, 0.18) * drawn
    return jnp.clip(drawn, min=-reach, max=reach).astype(kind)


def setup_inputs(seed: int = 0) -> dict:
    splits = jax.random.split(jax.random.key(seed), 17)
    hidden = centred(splits[0], (REQUESTS, NEW, D), 1.0, 6.0, ((0, 16), (2, 2)))
    key_cache = draw_key_cache(jax.random.fold_in(splits[16], 71), 0)
    value_cache = centred(splits[2], (REQUESTS, KVH, CAPC, HD), 1.0, 6.0, ((0, 16), (1, 2)))
    request_order = jax.random.permutation(splits[3], REQUESTS).astype(jnp.int32)
    cached_lengths = uneven(splits[4], REQUESTS, REQUESTS * MAXLEN // 2, MAXLEN, 2).astype(jnp.int32)
    expert_ids_keys = jax.random.split(jax.random.fold_in(splits[5], 1), REQUESTS * NEW // NEW)
    expert_ids_turns = jax.random.permutation(jax.random.fold_in(splits[5], 3), REQUESTS * NEW // NEW)
    expert_ids = jax.vmap(lambda own, number: assign_block(jax.random.fold_in(splits[5], 2), own, number, NEW, EXPERTS, TOPK, CAPE, 2))(expert_ids_keys, expert_ids_turns).reshape((REQUESTS, NEW, TOPK))
    gate_values = jnp.clip(0.1 + 0.9 * jax.random.uniform(splits[6], (REQUESTS, NEW, TOPK), jnp.float32) ** shard_levels(splits[6], (REQUESTS, NEW, TOPK), ((0, 16),), -0.2, 0.2), 0.1, 1.0)
    attn_gain = jnp.clip(1.0 + 0.15 * jax.random.normal(splits[7], (D,), jnp.float32), 0.25, 1.75)
    ffn_gain = jnp.clip(1.0 + 0.15 * jax.random.normal(splits[8], (D,), jnp.float32), 0.25, 1.75)
    w_query = centred(splits[9], (D, QH * HD), D ** -0.5, 0.15625, ((1, 2),))
    w_key = centred(splits[10], (D, KVH * HD), D ** -0.5, 0.15625, ((1, 2),))
    w_value = centred(splits[11], (D, KVH * HD), D ** -0.5, 0.15625, ((1, 2),))
    w_out = centred(splits[12], (QH * HD, D), (QH * HD) ** -0.5, 0.15625, ((0, 2),))
    expert_gate = centred(splits[13], (W_EXPERTS, D, FF), D ** -0.5, 0.15625, ((0, 2), (1, 16)))
    expert_up = centred(splits[14], (W_EXPERTS, D, FF), D ** -0.5, 0.15625, ((0, 2), (1, 16)))
    expert_down = centred(splits[15], (W_EXPERTS, FF, D), FF ** -0.5, 0.25, ((0, 2), (1, 16)))
    return {"hidden": hidden, "key_cache": key_cache, "value_cache": value_cache, "request_order": request_order, "cached_lengths": cached_lengths, "expert_ids": expert_ids, "gate_values": gate_values, "attn_gain": attn_gain, "ffn_gain": ffn_gain, "w_query": w_query, "w_key": w_key, "w_value": w_value, "w_out": w_out, "expert_gate": expert_gate, "expert_up": expert_up, "expert_down": expert_down}


epsilon = 1e-06

def normalize(values, gain):
    return values * lax.rsqrt(lax.optimization_barrier(jnp.mean(values * values, -1, keepdims=True)) + epsilon) * gain

def rotate(values, positions):
    half = values.shape[-1] // 2
    freq = 10000.0 ** (-jnp.arange(half, dtype=jnp.float32) * (2.0 / values.shape[-1]))
    angle = positions.astype(jnp.float32)[:, None] * freq[None, :]
    cosine = jnp.cos(angle)
    sine = jnp.sin(angle)
    first = values[..., :half]
    second = values[..., half:]
    return jnp.concatenate([first * cosine - second * sine, second * cosine + first * sine], -1)

def rounded(values):
    return lax.optimization_barrier(values.astype(jnp.bfloat16)).astype(jnp.float32)

def route_table(chosen, gate_rows, expert, capacity):
    hits = chosen == expert
    member = lax.optimization_barrier(jnp.sum(hits.astype(jnp.int32), 1, dtype=jnp.int32))
    weight = lax.optimization_barrier(jnp.sum(jnp.where(hits, gate_rows, 0.0), 1))
    place = jnp.cumsum(member, dtype=jnp.int32) - 1
    slots = jnp.arange(capacity, dtype=jnp.int32)
    table = (member[None, :] == 1) & (place[None, :] == slots[:, None])
    gate_slot = lax.optimization_barrier(jnp.sum(jnp.where(table, weight[None, :], 0.0), 1))
    return (table.astype(jnp.bfloat16), gate_slot)

def reference(hidden, key_cache, value_cache, request_order, cached_lengths, expert_ids, gate_values, attn_gain, ffn_gain, w_query, w_key, w_value, w_out, expert_gate, expert_up, expert_down):
    slot_lengths = cached_lengths[request_order].astype(jnp.int32)
    group = QH // KVH
    per_group = QH * HD // N_EP

    def one_slot(item):
        rows, keys, values, length, chosen, gate_rows = item
        rows_f = rows.astype(jnp.float32)
        normed = normalize(rows_f, attn_gain).astype(jnp.bfloat16)
        query = jnp.dot(normed, w_query, preferred_element_type=jnp.float32).reshape(NEW, QH, HD).transpose(1, 0, 2)
        key_new = jnp.dot(normed, w_key, preferred_element_type=jnp.float32).reshape(NEW, KVH, HD).transpose(1, 0, 2)
        value_new = jnp.dot(normed, w_value, preferred_element_type=jnp.float32).reshape(NEW, KVH, HD).transpose(1, 0, 2)
        positions = length + jnp.arange(NEW, dtype=jnp.int32)
        query = rotate(query, positions).astype(jnp.bfloat16)
        key_new = rotate(key_new, positions).astype(jnp.bfloat16)
        value_new = value_new.astype(jnp.bfloat16)
        zero = jnp.zeros((), jnp.int32)
        keys = lax.dynamic_update_slice(keys, key_new, (zero, length.astype(jnp.int32), zero))
        values = lax.dynamic_update_slice(values, value_new, (zero, length.astype(jnp.int32), zero))
        grouped = query.reshape(KVH, group, NEW, HD).astype(jnp.float32)
        scores = jnp.einsum('kgtd,kjd->kgtj', grouped, keys.astype(jnp.float32)) * HD ** (-0.5)
        visible = jnp.arange(CAPC, dtype=jnp.int32)[None, :] <= positions[:, None]
        scores = jnp.where(visible, scores, -1e+30)
        highest = lax.optimization_barrier(jnp.max(scores, -1, keepdims=True))
        probs = jnp.where(visible, jnp.exp(scores - highest), 0.0)
        total = lax.optimization_barrier(jnp.sum(probs, -1))
        probs_low = rounded(probs)
        attended = jnp.einsum('kgtj,kjd->kgtd', probs_low, values.astype(jnp.float32)) / total[..., None]
        attended = attended.reshape(QH, NEW, HD).transpose(1, 0, 2).reshape(NEW, QH * HD).astype(jnp.bfloat16)
        head_sum = jnp.zeros((NEW, D), jnp.float32)
        for block in range(N_EP):
            part = jnp.dot(attended[:, block * per_group:(block + 1) * per_group], w_out[block * per_group:(block + 1) * per_group], preferred_element_type=jnp.float32)
            head_sum = head_sum + rounded(part)
        mixed = (rows_f + head_sum).astype(jnp.bfloat16)
        ffn_normed = normalize(mixed.astype(jnp.float32), ffn_gain).astype(jnp.bfloat16)
        expert_sum = jnp.zeros((NEW, D), jnp.float32)
        for block in range(N_EP):
            part = jnp.zeros((NEW, D), jnp.float32)
            for inner in range(EXP_DEV):
                expert = block * EXP_DEV + inner
                table, gate_slot = route_table(chosen, gate_rows, expert, CAPE)
                dispatched = jnp.dot(table, ffn_normed, preferred_element_type=jnp.float32).astype(jnp.bfloat16)
                gate_act = jnp.dot(dispatched, expert_gate[expert], preferred_element_type=jnp.float32)
                up_act = jnp.dot(dispatched, expert_up[expert], preferred_element_type=jnp.float32)
                act = (jax.nn.silu(gate_act) * up_act).astype(jnp.bfloat16)
                output = jnp.dot(act, expert_down[expert], preferred_element_type=jnp.float32)
                contrib = (output * gate_slot[:, None]).astype(jnp.bfloat16)
                part = part + jnp.dot(table.T, contrib, preferred_element_type=jnp.float32)
            expert_sum = expert_sum + rounded(part)
        result = (mixed.astype(jnp.float32) + expert_sum).astype(jnp.bfloat16)
        return (result, keys, values)
    return lax.map(one_slot, (hidden, key_cache, value_cache, slot_lengths, expert_ids, gate_values))
```

```python
import jax
import jax.numpy as jnp
from jax import lax
from jax.experimental import pallas as pl
from jax.experimental.pallas import tpu as pltpu
from jax.sharding import PartitionSpec as P

epsilon = 1e-06


def normalize(values, gain):
    return values * lax.rsqrt(jnp.mean(values * values, -1, keepdims=True) + epsilon) * gain


def rotate(values, positions):
    half = values.shape[-1] // 2
    freq = 10000.0 ** (-jnp.arange(half, dtype=jnp.float32) * (2.0 / values.shape[-1]))
    angle = positions.astype(jnp.float32)[:, None] * freq[None, :]
    cosine = jnp.cos(angle)
    sine = jnp.sin(angle)
    first = values[..., :half]
    second = values[..., half:]
    return jnp.concatenate([first * cosine - second * sine, second * cosine + first * sine], -1)


def rounded(values):
    return lax.optimization_barrier(values.astype(jnp.bfloat16)).astype(jnp.float32)


def route_tables(chosen, gate_rows, wanted, capacity):
    hits = chosen[:, :, None] == wanted[None, None, :]
    member = jnp.sum(hits.astype(jnp.int32), 1, dtype=jnp.int32)
    weight = jnp.sum(jnp.where(hits, gate_rows[:, :, None], 0.0), 1)
    place = jnp.cumsum(member, 0, dtype=jnp.int32) - 1
    slots = jnp.arange(capacity, dtype=jnp.int32)
    table = (member.T[:, None, :] == 1) & (place.T[:, None, :] == slots[None, :, None])
    gate_slot = jnp.sum(jnp.where(table, weight.T[:, None, :], 0.0), 2)
    return (table.astype(jnp.bfloat16), gate_slot)


def flash_attend(query, keys, values, length, new_rows):
    kv_heads, rows, head_dim = query.shape
    block = new_rows
    blocks = keys.shape[1] // block
    scale = head_dim ** (-0.5)
    limit = (length + jnp.arange(rows, dtype=jnp.int32) % new_rows)[:, None]

    def last_block(length_ref):
        return (length_ref[0] + new_rows - 1) // block

    def kernel(length_ref, limit_ref, q_ref, k_ref, v_ref, o_ref, m_sc, l_sc, acc_sc):
        step = pl.program_id(1)

        @pl.when(step == 0)
        def _():
            m_sc[...] = jnp.full(m_sc.shape, -1e30, jnp.float32)
            l_sc[...] = jnp.zeros(l_sc.shape, jnp.float32)
            acc_sc[...] = jnp.zeros(acc_sc.shape, jnp.float32)

        def visit(masked):
            scores = (
                lax.dot_general(
                    q_ref[0],
                    k_ref[0],
                    (((1,), (1,)), ((), ())),
                    preferred_element_type=jnp.float32,
                )
                * scale
            )
            if masked:
                column = step * block + lax.broadcasted_iota(jnp.int32, scores.shape, 1)
                visible = column <= limit_ref[...]
                scores = jnp.where(visible, scores, -1e30)
            previous = m_sc[...]
            highest = jnp.maximum(previous, jnp.max(scores, -1, keepdims=True))
            probs = jnp.exp(scores - highest)
            if masked:
                probs = jnp.where(visible, probs, 0.0)
            correction = jnp.exp(previous - highest)
            l_sc[...] = l_sc[...] * correction + jnp.sum(probs, -1, keepdims=True)
            acc_sc[...] = acc_sc[...] * correction + jnp.dot(
                probs.astype(jnp.bfloat16), v_ref[0], preferred_element_type=jnp.float32
            )
            m_sc[...] = highest

        whole = (step + 1) * block - 1 <= length_ref[0]

        @pl.when(whole)
        def _():
            visit(False)

        @pl.when(jnp.logical_not(whole) & (step <= last_block(length_ref)))
        def _():
            visit(True)

        @pl.when(step == blocks - 1)
        def _():
            o_ref[0] = (acc_sc[...] / l_sc[...]).astype(o_ref.dtype)

    def kv_map(head, step, length_ref):
        return (head, jnp.minimum(step, last_block(length_ref)), 0)

    grid_spec = pltpu.PrefetchScalarGridSpec(
        num_scalar_prefetch=1,
        grid=(kv_heads, blocks),
        in_specs=[
            pl.BlockSpec((rows, 1), lambda head, step, length_ref: (0, 0)),
            pl.BlockSpec((1, rows, head_dim), lambda head, step, length_ref: (head, 0, 0)),
            pl.BlockSpec((1, block, head_dim), kv_map),
            pl.BlockSpec((1, block, head_dim), kv_map),
        ],
        out_specs=pl.BlockSpec((1, rows, head_dim), lambda head, step, length_ref: (head, 0, 0)),
        scratch_shapes=[
            pltpu.VMEM((rows, 1), jnp.float32),
            pltpu.VMEM((rows, 1), jnp.float32),
            pltpu.VMEM((rows, head_dim), jnp.float32),
        ],
    )
    flops = 4 * kv_heads * rows * keys.shape[1] * head_dim
    return pl.pallas_call(
        kernel,
        grid_spec=grid_spec,
        out_shape=jax.ShapeDtypeStruct(query.shape, jnp.bfloat16),
        compiler_params=pltpu.CompilerParams(dimension_semantics=("arbitrary", "arbitrary")),
        cost_estimate=pl.CostEstimate(
            flops=flops,
            transcendentals=kv_heads * rows * keys.shape[1],
            bytes_accessed=2 * (query.size + keys.size + values.size + query.size),
        ),
    )(length.reshape(1), limit, query, keys, values)


def shifted(values, shift):
    devices = lax.axis_size("ep")
    return lax.ppermute(values, "ep", [(i, (i + shift) % devices) for i in range(devices)])


def gather_columns(values):
    devices = lax.axis_size("ep")
    me = lax.axis_index("ep")
    width = values.shape[-1]
    whole = jnp.zeros(values.shape[:-1] + (width * devices,), values.dtype)
    for shift in range(devices):
        piece = values if shift == 0 else shifted(values, shift)
        source = (me - shift) % devices
        whole = lax.dynamic_update_slice_in_dim(whole, piece, source * width, values.ndim - 1)
    return whole


def sum_over_ep(part):
    devices = lax.axis_size("ep")
    total = part.astype(jnp.float32)
    for shift in range(1, devices):
        total = total + shifted(part, shift).astype(jnp.float32)
    return total


def scatter_sum_over_ep(part, width):
    devices = lax.axis_size("ep")
    me = lax.axis_index("ep")
    total = lax.dynamic_slice_in_dim(part, me * width, width, 1).astype(jnp.float32)
    for shift in range(1, devices):
        target = (me + shift) % devices
        piece = lax.dynamic_slice_in_dim(part, target * width, width, 1)
        total = total + shifted(piece, shift).astype(jnp.float32)
    return total


def on_device(
    hidden,
    key_cache,
    value_cache,
    request_order,
    cached_lengths,
    expert_ids,
    gate_values,
    attn_gain,
    ffn_gain,
    w_query,
    w_key,
    w_value,
    w_out,
    expert_gate,
    expert_up,
    expert_down,
):
    own_rows = hidden[0]
    new_rows = own_rows.shape[0]
    own_width = own_rows.shape[1]
    head_dim = key_cache.shape[3]
    kv_local = key_cache.shape[1]
    heads_local = w_query.shape[1] // head_dim
    group = heads_local // kv_local
    per_device = expert_gate.shape[0]
    capacity = 3 * new_rows // 8
    me = lax.axis_index("ep")
    gate_whole = lax.all_gather(expert_gate, "req", axis=1, tiled=True)
    up_whole = lax.all_gather(expert_up, "req", axis=1, tiled=True)
    down_whole = lax.all_gather(expert_down, "req", axis=1, tiled=True)
    everyone = jnp.arange(request_order.shape[0], dtype=jnp.int32)
    request = jnp.sum(jnp.where(everyone == lax.axis_index("req"), request_order, 0))
    length = jnp.sum(jnp.where(everyone == request, cached_lengths, 0))
    rows_whole = gather_columns(own_rows)
    rows_f = rows_whole.astype(jnp.float32)
    normed = normalize(rows_f, attn_gain).astype(jnp.bfloat16)
    query = jnp.dot(normed, w_query, preferred_element_type=jnp.float32)
    key_new = jnp.dot(normed, w_key, preferred_element_type=jnp.float32)
    value_new = jnp.dot(normed, w_value, preferred_element_type=jnp.float32)
    positions = length + jnp.arange(new_rows, dtype=jnp.int32)
    query = rotate(
        query.reshape(new_rows, heads_local, head_dim).transpose(1, 0, 2), positions
    ).astype(jnp.bfloat16)
    query = query.reshape(kv_local, group * new_rows, head_dim)
    key_new = rotate(
        key_new.reshape(new_rows, kv_local, head_dim).transpose(1, 0, 2), positions
    ).astype(jnp.bfloat16)
    value_new = (
        value_new.reshape(new_rows, kv_local, head_dim).transpose(1, 0, 2).astype(jnp.bfloat16)
    )
    zero = jnp.zeros((), jnp.int32)
    keys = lax.dynamic_update_slice(key_cache[0], key_new, (zero, length, zero))
    values = lax.dynamic_update_slice(value_cache[0], value_new, (zero, length, zero))
    attended = flash_attend(query, keys, values, length, new_rows)
    gate_whole, up_whole, down_whole, attended = lax.optimization_barrier(
        (gate_whole, up_whole, down_whole, attended)
    )
    attended = (
        attended.reshape(heads_local, new_rows, head_dim)
        .transpose(1, 0, 2)
        .reshape(new_rows, heads_local * head_dim)
    )
    head_part = jnp.dot(attended, w_out, preferred_element_type=jnp.float32).astype(jnp.bfloat16)
    head_sum = sum_over_ep(head_part)
    mixed_f = (rows_f + head_sum).astype(jnp.bfloat16).astype(jnp.float32)
    ffn_normed = normalize(mixed_f, ffn_gain).astype(jnp.bfloat16)
    table, gate_slot = route_tables(
        expert_ids[0],
        gate_values[0],
        me * per_device + jnp.arange(per_device, dtype=jnp.int32),
        capacity,
    )
    dispatched = jnp.einsum(
        "ect,td->ecd", table, ffn_normed, preferred_element_type=jnp.float32
    ).astype(jnp.bfloat16)
    gate_act = jnp.einsum("ecd,edf->ecf", dispatched, gate_whole, preferred_element_type=jnp.float32)
    up_act = jnp.einsum("ecd,edf->ecf", dispatched, up_whole, preferred_element_type=jnp.float32)
    act = (jax.nn.silu(gate_act) * up_act).astype(jnp.bfloat16)
    output = jnp.einsum("ecf,efd->ecd", act, down_whole, preferred_element_type=jnp.float32)
    contrib = (output * gate_slot[..., None]).astype(jnp.bfloat16)
    expert_part = jnp.einsum(
        "ect,ecd->td", table, contrib, preferred_element_type=jnp.float32
    ).astype(jnp.bfloat16)
    expert_sum = scatter_sum_over_ep(expert_part, own_width)
    mixed_own = lax.dynamic_slice_in_dim(mixed_f, me * own_width, own_width, 1)
    result = (mixed_own + expert_sum).astype(jnp.bfloat16)
    return (result[None], keys[None], values[None])


def solution(mesh):
    in_specs = (
        P("req", None, "ep"),
        P("req", "ep", None, None),
        P("req", "ep", None, None),
        P(),
        P(),
        P("req", None, None),
        P("req", None, None),
        P(),
        P(),
        P(None, "ep"),
        P(None, "ep"),
        P(None, "ep"),
        P("ep", None),
        P("ep", "req", None),
        P("ep", "req", None),
        P("ep", "req", None),
    )
    out_specs = (P("req", None, "ep"), P("req", "ep", None, None), P("req", "ep", None, None))
    return jax.shard_map(
        on_device, mesh=mesh, in_specs=in_specs, out_specs=out_specs, check_vma=False
    )
```

```python
import jax
import jax.numpy as jnp
from jax import lax
from jax.experimental import pallas as pl
from jax.experimental.pallas import tpu as pltpu
from jax.sharding import PartitionSpec as P

epsilon = 1e-06


def normalize(values, gain):
    return values * lax.rsqrt(jnp.mean(values * values, -1, keepdims=True) + epsilon) * gain


def rotate(values, positions):
    half = values.shape[-1] // 2
    freq = 10000.0 ** (-jnp.arange(half, dtype=jnp.float32) * (2.0 / values.shape[-1]))
    angle = positions.astype(jnp.float32)[:, None] * freq[None, :]
    cosine = jnp.cos(angle)
    sine = jnp.sin(angle)
    first = values[..., :half]
    second = values[..., half:]
    return jnp.concatenate([first * cosine - second * sine, second * cosine + first * sine], -1)


def rounded(values):
    return lax.optimization_barrier(values.astype(jnp.bfloat16)).astype(jnp.float32)


def route_tables(chosen, gate_rows, wanted, capacity):
    hits = chosen[:, :, None] == wanted[None, None, :]
    member = jnp.sum(hits.astype(jnp.int32), 1, dtype=jnp.int32)
    weight = jnp.sum(jnp.where(hits, gate_rows[:, :, None], 0.0), 1)
    place = jnp.cumsum(member, 0, dtype=jnp.int32) - 1
    slots = jnp.arange(capacity, dtype=jnp.int32)
    table = (member.T[:, None, :] == 1) & (place.T[:, None, :] == slots[None, :, None])
    gate_slot = jnp.sum(jnp.where(table, weight.T[:, None, :], 0.0), 2)
    return (table.astype(jnp.bfloat16), gate_slot)


def flash_attend(query, keys, values, length, new_rows):
    kv_heads, rows, head_dim = query.shape
    block = new_rows
    blocks = keys.shape[1] // block
    scale = head_dim ** (-0.5)
    limit = (length + jnp.arange(rows, dtype=jnp.int32) % new_rows)[:, None]

    def last_block(length_ref):
        return (length_ref[0] + new_rows - 1) // block

    def kernel(length_ref, limit_ref, q_ref, k_ref, v_ref, o_ref, m_sc, l_sc, acc_sc):
        step = pl.program_id(1)

        @pl.when(step == 0)
        def _():
            m_sc[...] = jnp.full(m_sc.shape, -1e30, jnp.float32)
            l_sc[...] = jnp.zeros(l_sc.shape, jnp.float32)
            acc_sc[...] = jnp.zeros(acc_sc.shape, jnp.float32)

        def visit(masked):
            scores = (
                lax.dot_general(
                    q_ref[0],
                    k_ref[0],
                    (((1,), (1,)), ((), ())),
                    preferred_element_type=jnp.float32,
                )
                * scale
            )
            if masked:
                column = step * block + lax.broadcasted_iota(jnp.int32, scores.shape, 1)
                visible = column <= limit_ref[...]
                scores = jnp.where(visible, scores, -1e30)
            previous = m_sc[...]
            highest = jnp.maximum(previous, jnp.max(scores, -1, keepdims=True))
            probs = jnp.exp(scores - highest)
            if masked:
                probs = jnp.where(visible, probs, 0.0)
            correction = jnp.exp(previous - highest)
            l_sc[...] = l_sc[...] * correction + jnp.sum(probs, -1, keepdims=True)
            acc_sc[...] = acc_sc[...] * correction + jnp.dot(
                probs.astype(jnp.bfloat16), v_ref[0], preferred_element_type=jnp.float32
            )
            m_sc[...] = highest

        whole = (step + 1) * block - 1 <= length_ref[0]

        @pl.when(whole)
        def _():
            visit(False)

        @pl.when(jnp.logical_not(whole) & (step <= last_block(length_ref)))
        def _():
            visit(True)

        @pl.when(step == blocks - 1)
        def _():
            o_ref[0] = (acc_sc[...] / l_sc[...]).astype(o_ref.dtype)

    def kv_map(head, step, length_ref):
        return (head, jnp.minimum(step, last_block(length_ref)), 0)

    grid_spec = pltpu.PrefetchScalarGridSpec(
        num_scalar_prefetch=1,
        grid=(kv_heads, blocks),
        in_specs=[
            pl.BlockSpec((rows, 1), lambda head, step, length_ref: (0, 0)),
            pl.BlockSpec((1, rows, head_dim), lambda head, step, length_ref: (head, 0, 0)),
            pl.BlockSpec((1, block, head_dim), kv_map),
            pl.BlockSpec((1, block, head_dim), kv_map),
        ],
        out_specs=pl.BlockSpec((1, rows, head_dim), lambda head, step, length_ref: (head, 0, 0)),
        scratch_shapes=[
            pltpu.VMEM((rows, 1), jnp.float32),
            pltpu.VMEM((rows, 1), jnp.float32),
            pltpu.VMEM((rows, head_dim), jnp.float32),
        ],
    )
    flops = 4 * kv_heads * rows * keys.shape[1] * head_dim
    return pl.pallas_call(
        kernel,
        grid_spec=grid_spec,
        out_shape=jax.ShapeDtypeStruct(query.shape, jnp.bfloat16),
        compiler_params=pltpu.CompilerParams(dimension_semantics=("arbitrary", "arbitrary")),
        cost_estimate=pl.CostEstimate(
            flops=flops,
            transcendentals=kv_heads * rows * keys.shape[1],
            bytes_accessed=2 * (query.size + keys.size + values.size + query.size),
        ),
    )(length.reshape(1), limit, query, keys, values)


def shifted(values, shift):
    devices = lax.axis_size("ep")
    return lax.ppermute(values, "ep", [(i, (i + shift) % devices) for i in range(devices)])


def gather_columns(values):
    devices = lax.axis_size("ep")
    me = lax.axis_index("ep")
    width = values.shape[-1]
    whole = jnp.zeros(values.shape[:-1] + (width * devices,), values.dtype)
    for shift in range(devices):
        piece = values if shift == 0 else shifted(values, shift)
        source = (me - shift) % devices
        whole = lax.dynamic_update_slice_in_dim(whole, piece, source * width, values.ndim - 1)
    return whole


def sum_over_ep(part):
    devices = lax.axis_size("ep")
    total = part.astype(jnp.float32)
    for shift in range(1, devices):
        total = total + shifted(part, shift).astype(jnp.float32)
    return total


def scatter_sum_over_ep(part, width):
    devices = lax.axis_size("ep")
    me = lax.axis_index("ep")
    total = lax.dynamic_slice_in_dim(part, me * width, width, 1).astype(jnp.float32)
    for shift in range(1, devices):
        target = (me + shift) % devices
        piece = lax.dynamic_slice_in_dim(part, target * width, width, 1)
        total = total + shifted(piece, shift).astype(jnp.float32)
    return total


def on_device(
    hidden,
    key_cache,
    value_cache,
    request_order,
    cached_lengths,
    expert_ids,
    gate_values,
    attn_gain,
    ffn_gain,
    w_query,
    w_key,
    w_value,
    w_out,
    expert_gate,
    expert_up,
    expert_down,
):
    own_rows = hidden[0]
    new_rows = own_rows.shape[0]
    own_width = own_rows.shape[1]
    head_dim = key_cache.shape[3]
    kv_local = key_cache.shape[1]
    heads_local = w_query.shape[1] // head_dim
    group = heads_local // kv_local
    per_device = expert_gate.shape[0]
    capacity = 3 * new_rows // 8
    me = lax.axis_index("ep")
    gate_whole = lax.all_gather(expert_gate, "req", axis=1, tiled=True)
    up_whole = lax.all_gather(expert_up, "req", axis=1, tiled=True)
    down_whole = lax.all_gather(expert_down, "req", axis=1, tiled=True)
    everyone = jnp.arange(request_order.shape[0], dtype=jnp.int32)
    request = jnp.sum(jnp.where(everyone == lax.axis_index("req"), request_order, 0))
    length = jnp.sum(jnp.where(everyone == request, cached_lengths, 0))
    rows_whole = gather_columns(own_rows)
    rows_f = rows_whole.astype(jnp.float32)
    normed = normalize(rows_f, attn_gain).astype(jnp.bfloat16)
    query = jnp.dot(normed, w_query, preferred_element_type=jnp.float32)
    key_new = jnp.dot(normed, w_key, preferred_element_type=jnp.float32)
    value_new = jnp.dot(normed, w_value, preferred_element_type=jnp.float32)
    positions = length + jnp.arange(new_rows, dtype=jnp.int32)
    query = rotate(
        query.reshape(new_rows, heads_local, head_dim).transpose(1, 0, 2), positions
    ).astype(jnp.bfloat16)
    query = query.reshape(kv_local, group * new_rows, head_dim)
    key_new = rotate(
        key_new.reshape(new_rows, kv_local, head_dim).transpose(1, 0, 2), positions
    ).astype(jnp.bfloat16)
    value_new = (
        value_new.reshape(new_rows, kv_local, head_dim).transpose(1, 0, 2).astype(jnp.bfloat16)
    )
    zero = jnp.zeros((), jnp.int32)
    keys = lax.dynamic_update_slice(key_cache[0], key_new, (zero, length, zero))
    values = lax.dynamic_update_slice(value_cache[0], value_new, (zero, length, zero))
    attended = flash_attend(query, keys, values, length, new_rows)
    attended = (
        attended.reshape(heads_local, new_rows, head_dim)
        .transpose(1, 0, 2)
        .reshape(new_rows, heads_local * head_dim)
    )
    head_part = jnp.dot(attended, w_out, preferred_element_type=jnp.float32).astype(jnp.bfloat16)
    head_sum = sum_over_ep(head_part)
    mixed_f = (rows_f + head_sum).astype(jnp.bfloat16).astype(jnp.float32)
    ffn_normed = normalize(mixed_f, ffn_gain).astype(jnp.bfloat16)
    table, gate_slot = route_tables(
        expert_ids[0],
        gate_values[0],
        me * per_device + jnp.arange(per_device, dtype=jnp.int32),
        capacity,
    )
    dispatched = jnp.einsum(
        "ect,td->ecd", table, ffn_normed, preferred_element_type=jnp.float32
    ).astype(jnp.bfloat16)
    gate_whole, up_whole, down_whole, dispatched = lax.optimization_barrier(
        (gate_whole, up_whole, down_whole, dispatched)
    )
    gate_act = jnp.einsum("ecd,edf->ecf", dispatched, gate_whole, preferred_element_type=jnp.float32)
    up_act = jnp.einsum("ecd,edf->ecf", dispatched, up_whole, preferred_element_type=jnp.float32)
    act = (jax.nn.silu(gate_act) * up_act).astype(jnp.bfloat16)
    output = jnp.einsum("ecf,efd->ecd", act, down_whole, preferred_element_type=jnp.float32)
    contrib = (output * gate_slot[..., None]).astype(jnp.bfloat16)
    expert_part = jnp.einsum(
        "ect,ecd->td", table, contrib, preferred_element_type=jnp.float32
    ).astype(jnp.bfloat16)
    expert_sum = scatter_sum_over_ep(expert_part, own_width)
    mixed_own = lax.dynamic_slice_in_dim(mixed_f, me * own_width, own_width, 1)
    result = (mixed_own + expert_sum).astype(jnp.bfloat16)
    return (result[None], keys[None], values[None])


def solution(mesh):
    in_specs = (
        P("req", None, "ep"),
        P("req", "ep", None, None),
        P("req", "ep", None, None),
        P(),
        P(),
        P("req", None, None),
        P("req", None, None),
        P(),
        P(),
        P(None, "ep"),
        P(None, "ep"),
        P(None, "ep"),
        P("ep", None),
        P("ep", "req", None),
        P("ep", "req", None),
        P("ep", "req", None),
    )
    out_specs = (P("req", None, "ep"), P("req", "ep", None, None), P("req", "ep", None, None))
    return jax.shard_map(
        on_device, mesh=mesh, in_specs=in_specs, out_specs=out_specs, check_vma=False
    )
```

```python
import jax
import jax.numpy as jnp
from jax import lax
from jax.experimental import pallas as pl
from jax.experimental.pallas import tpu as pltpu
from jax.sharding import PartitionSpec as P

epsilon = 1e-06


def normalize(values, gain):
    return values * lax.rsqrt(jnp.mean(values * values, -1, keepdims=True) + epsilon) * gain


def rotate(values, positions):
    half = values.shape[-1] // 2
    freq = 10000.0 ** (-jnp.arange(half, dtype=jnp.float32) * (2.0 / values.shape[-1]))
    angle = positions.astype(jnp.float32)[:, None] * freq[None, :]
    cosine = jnp.cos(angle)
    sine = jnp.sin(angle)
    first = values[..., :half]
    second = values[..., half:]
    return jnp.concatenate([first * cosine - second * sine, second * cosine + first * sine], -1)


def rounded(values):
    return lax.optimization_barrier(values.astype(jnp.bfloat16)).astype(jnp.float32)


def route_tables(chosen, gate_rows, wanted, capacity):
    hits = chosen[:, :, None] == wanted[None, None, :]
    member = jnp.sum(hits.astype(jnp.int32), 1, dtype=jnp.int32)
    weight = jnp.sum(jnp.where(hits, gate_rows[:, :, None], 0.0), 1)
    place = jnp.cumsum(member, 0, dtype=jnp.int32) - 1
    slots = jnp.arange(capacity, dtype=jnp.int32)
    table = (member.T[:, None, :] == 1) & (place.T[:, None, :] == slots[None, :, None])
    gate_slot = jnp.sum(jnp.where(table, weight.T[:, None, :], 0.0), 2)
    return (table.astype(jnp.bfloat16), gate_slot)


def flash_attend(query, keys, values, length, new_rows):
    kv_heads, rows, head_dim = query.shape
    block = new_rows
    blocks = keys.shape[1] // block
    limit = (length + jnp.arange(rows, dtype=jnp.int32) % new_rows)[:, None]

    def last_block(length_ref):
        return (length_ref[0] + new_rows - 1) // block

    def kernel(length_ref, limit_ref, q_ref, k_ref, v_ref, o_ref, m_sc, l_sc, acc_sc):
        step = pl.program_id(1)

        @pl.when(step == 0)
        def _():
            m_sc[...] = jnp.full(m_sc.shape, -1e30, jnp.float32)
            l_sc[...] = jnp.zeros(l_sc.shape, jnp.float32)
            acc_sc[...] = jnp.zeros(acc_sc.shape, jnp.float32)

        def visit(masked):
            scores = lax.dot_general(
                q_ref[0],
                k_ref[0],
                (((1,), (1,)), ((), ())),
                preferred_element_type=jnp.float32,
            )
            if masked:
                column = step * block + lax.broadcasted_iota(jnp.int32, scores.shape, 1)
                visible = column <= limit_ref[...]
                scores = jnp.where(visible, scores, -1e30)
            previous = m_sc[...]
            highest = jnp.maximum(previous, jnp.max(scores, -1, keepdims=True))
            probs = jnp.exp(scores - highest)
            if masked:
                probs = jnp.where(visible, probs, 0.0)
            correction = jnp.exp(previous - highest)
            l_sc[...] = l_sc[...] * correction + jnp.sum(probs, -1, keepdims=True)
            acc_sc[...] = acc_sc[...] * correction + jnp.dot(
                probs.astype(jnp.bfloat16), v_ref[0], preferred_element_type=jnp.float32
            )
            m_sc[...] = highest

        whole = (step + 1) * block - 1 <= length_ref[0]

        @pl.when(whole)
        def _():
            visit(False)

        @pl.when(jnp.logical_not(whole) & (step <= last_block(length_ref)))
        def _():
            visit(True)

        @pl.when(step == blocks - 1)
        def _():
            o_ref[0] = (acc_sc[...] / l_sc[...]).astype(o_ref.dtype)

    def kv_map(head, step, length_ref):
        return (head, jnp.minimum(step, last_block(length_ref)), 0)

    grid_spec = pltpu.PrefetchScalarGridSpec(
        num_scalar_prefetch=1,
        grid=(kv_heads, blocks),
        in_specs=[
            pl.BlockSpec((rows, 1), lambda head, step, length_ref: (0, 0)),
            pl.BlockSpec((1, rows, head_dim), lambda head, step, length_ref: (head, 0, 0)),
            pl.BlockSpec((1, block, head_dim), kv_map),
            pl.BlockSpec((1, block, head_dim), kv_map),
        ],
        out_specs=pl.BlockSpec((1, rows, head_dim), lambda head, step, length_ref: (head, 0, 0)),
        scratch_shapes=[
            pltpu.VMEM((rows, 1), jnp.float32),
            pltpu.VMEM((rows, 1), jnp.float32),
            pltpu.VMEM((rows, head_dim), jnp.float32),
        ],
    )
    flops = 4 * kv_heads * rows * keys.shape[1] * head_dim
    return pl.pallas_call(
        kernel,
        grid_spec=grid_spec,
        out_shape=jax.ShapeDtypeStruct(query.shape, jnp.bfloat16),
        compiler_params=pltpu.CompilerParams(dimension_semantics=("arbitrary", "arbitrary")),
        cost_estimate=pl.CostEstimate(
            flops=flops,
            transcendentals=kv_heads * rows * keys.shape[1],
            bytes_accessed=2 * (query.size + keys.size + values.size + query.size),
        ),
    )(length.reshape(1), limit, query, keys, values)


def shifted(values, shift):
    devices = lax.axis_size("ep")
    return lax.ppermute(values, "ep", [(i, (i + shift) % devices) for i in range(devices)])


def gather_columns(values):
    devices = lax.axis_size("ep")
    me = lax.axis_index("ep")
    width = values.shape[-1]
    whole = jnp.zeros(values.shape[:-1] + (width * devices,), values.dtype)
    for shift in range(devices):
        piece = values if shift == 0 else shifted(values, shift)
        source = (me - shift) % devices
        whole = lax.dynamic_update_slice_in_dim(whole, piece, source * width, values.ndim - 1)
    return whole


def sum_over_ep(part):
    devices = lax.axis_size("ep")
    half = part.shape[0] // 2
    total = part.astype(jnp.float32)
    for shift in range(1, devices):
        upper = shifted(part[:half], shift)
        lower = shifted(part[half:], shift)
        total = total + jnp.concatenate([upper, lower], 0).astype(jnp.float32)
    return total


def scatter_sum_over_ep(part, width):
    devices = lax.axis_size("ep")
    me = lax.axis_index("ep")
    total = lax.dynamic_slice_in_dim(part, me * width, width, 1).astype(jnp.float32)
    for shift in range(1, devices):
        target = (me + shift) % devices
        piece = lax.dynamic_slice_in_dim(part, target * width, width, 1)
        total = total + shifted(piece, shift).astype(jnp.float32)
    return total


def on_device(
    hidden,
    key_cache,
    value_cache,
    request_order,
    cached_lengths,
    expert_ids,
    gate_values,
    attn_gain,
    ffn_gain,
    w_query,
    w_key,
    w_value,
    w_out,
    expert_gate,
    expert_up,
    expert_down,
):
    own_rows = hidden[0]
    new_rows = own_rows.shape[0]
    own_width = own_rows.shape[1]
    head_dim = key_cache.shape[3]
    kv_local = key_cache.shape[1]
    heads_local = w_query.shape[1] // head_dim
    group = heads_local // kv_local
    per_device = expert_gate.shape[0]
    capacity = 3 * new_rows // 8
    me = lax.axis_index("ep")
    gate_whole = lax.all_gather(expert_gate, "req", axis=1, tiled=True)
    up_whole = lax.all_gather(expert_up, "req", axis=1, tiled=True)
    down_whole = lax.all_gather(expert_down, "req", axis=1, tiled=True)
    everyone = jnp.arange(request_order.shape[0], dtype=jnp.int32)
    request = jnp.sum(jnp.where(everyone == lax.axis_index("req"), request_order, 0))
    length = jnp.sum(jnp.where(everyone == request, cached_lengths, 0))
    rows_whole = gather_columns(own_rows)
    rows_f = rows_whole.astype(jnp.float32)
    normed = normalize(rows_f, attn_gain).astype(jnp.bfloat16)
    query = jnp.dot(normed, w_query, preferred_element_type=jnp.float32)
    key_new = jnp.dot(normed, w_key, preferred_element_type=jnp.float32)
    value_new = jnp.dot(normed, w_value, preferred_element_type=jnp.float32)
    positions = length + jnp.arange(new_rows, dtype=jnp.int32)
    query = rotate(
        query.reshape(new_rows, heads_local, head_dim).transpose(1, 0, 2), positions
    ).astype(jnp.bfloat16) * jnp.asarray(head_dim ** (-0.5), jnp.bfloat16)
    query = query.reshape(kv_local, group * new_rows, head_dim)
    key_new = rotate(
        key_new.reshape(new_rows, kv_local, head_dim).transpose(1, 0, 2), positions
    ).astype(jnp.bfloat16)
    value_new = (
        value_new.reshape(new_rows, kv_local, head_dim).transpose(1, 0, 2).astype(jnp.bfloat16)
    )
    zero = jnp.zeros((), jnp.int32)
    keys = lax.dynamic_update_slice(key_cache[0], key_new, (zero, length, zero))
    values = lax.dynamic_update_slice(value_cache[0], value_new, (zero, length, zero))
    attended = flash_attend(query, keys, values, length, new_rows)
    attended = (
        attended.reshape(heads_local, new_rows, head_dim)
        .transpose(1, 0, 2)
        .reshape(new_rows, heads_local * head_dim)
    )
    head_part = jnp.dot(attended, w_out, preferred_element_type=jnp.float32).astype(jnp.bfloat16)
    head_sum = sum_over_ep(head_part)
    mixed_f = (rows_f + head_sum).astype(jnp.bfloat16).astype(jnp.float32)
    ffn_normed = normalize(mixed_f, ffn_gain).astype(jnp.bfloat16)
    table, gate_slot = route_tables(
        expert_ids[0],
        gate_values[0],
        me * per_device + jnp.arange(per_device, dtype=jnp.int32),
        capacity,
    )
    dispatched = jnp.einsum(
        "ect,td->ecd", table, ffn_normed, preferred_element_type=jnp.float32
    ).astype(jnp.bfloat16)
    gate_whole, up_whole, down_whole, dispatched = lax.optimization_barrier(
        (gate_whole, up_whole, down_whole, dispatched)
    )
    gate_act = jnp.einsum("ecd,edf->ecf", dispatched, gate_whole, preferred_element_type=jnp.float32)
    up_act = jnp.einsum("ecd,edf->ecf", dispatched, up_whole, preferred_element_type=jnp.float32)
    act = (jax.nn.silu(gate_act) * up_act).astype(jnp.bfloat16)
    output = jnp.einsum("ecf,efd->ecd", act, down_whole, preferred_element_type=jnp.float32)
    contrib = (output * gate_slot[..., None]).astype(jnp.bfloat16)
    expert_part = jnp.einsum(
        "ect,ecd->td", table, contrib, preferred_element_type=jnp.float32
    ).astype(jnp.bfloat16)
    expert_sum = scatter_sum_over_ep(expert_part, own_width)
    mixed_own = lax.dynamic_slice_in_dim(mixed_f, me * own_width, own_width, 1)
    result = (mixed_own + expert_sum).astype(jnp.bfloat16)
    return (result[None], keys[None], values[None])


def solution(mesh):
    in_specs = (
        P("req", None, "ep"),
        P("req", "ep", None, None),
        P("req", "ep", None, None),
        P(),
        P(),
        P("req", None, None),
        P("req", None, None),
        P(),
        P(),
        P(None, "ep"),
        P(None, "ep"),
        P(None, "ep"),
        P("ep", None),
        P("ep", "req", None),
        P("ep", "req", None),
        P("ep", "req", None),
    )
    out_specs = (P("req", None, "ep"), P("req", "ep", None, None), P("req", "ep", None, None))
    return jax.shard_map(
        on_device, mesh=mesh, in_specs=in_specs, out_specs=out_specs, check_vma=False
    )
```

```python
import jax
import jax.numpy as jnp
from jax import lax
from jax.experimental import pallas as pl
from jax.experimental.pallas import tpu as pltpu
from jax.sharding import PartitionSpec as P

epsilon = 1e-06


def normalize(values, gain):
    return values * lax.rsqrt(jnp.mean(values * values, -1, keepdims=True) + epsilon) * gain


def rotate(values, positions):
    half = values.shape[-1] // 2
    freq = 10000.0 ** (-jnp.arange(half, dtype=jnp.float32) * (2.0 / values.shape[-1]))
    angle = positions.astype(jnp.float32)[:, None] * freq[None, :]
    cosine = jnp.cos(angle)
    sine = jnp.sin(angle)
    first = values[..., :half]
    second = values[..., half:]
    return jnp.concatenate([first * cosine - second * sine, second * cosine + first * sine], -1)


def rounded(values):
    return lax.optimization_barrier(values.astype(jnp.bfloat16)).astype(jnp.float32)


def route_tables(chosen, gate_rows, wanted, capacity):
    hits = chosen[:, :, None] == wanted[None, None, :]
    member = jnp.sum(hits.astype(jnp.int32), 1, dtype=jnp.int32)
    weight = jnp.sum(jnp.where(hits, gate_rows[:, :, None], 0.0), 1)
    place = jnp.cumsum(member, 0, dtype=jnp.int32) - 1
    slots = jnp.arange(capacity, dtype=jnp.int32)
    table = (member.T[:, None, :] == 1) & (place.T[:, None, :] == slots[None, :, None])
    gate_slot = jnp.sum(jnp.where(table, weight.T[:, None, :], 0.0), 2)
    return (table.astype(jnp.bfloat16), gate_slot)


def flash_attend(query, keys, values, key_new, value_new, length):
    kv_heads, rows, head_dim = query.shape
    block = key_new.shape[2]
    blocks = keys.shape[2] // block

    def cached_blocks(length_ref):
        return (length_ref[0] + block - 1) // block

    def kernel(length_ref, q_ref, kc_ref, vc_ref, kn_ref, vn_ref, o_ref, m_sc, l_sc, acc_sc):
        step = pl.program_id(1)
        length = length_ref[0]

        def visit(key_block, value_block, visible, first):
            scores = jnp.dot(q_ref[0], key_block, preferred_element_type=jnp.float32)
            scores = jnp.where(visible, scores, -1e30)
            if first:
                highest = jnp.max(scores, -1, keepdims=True)
            else:
                previous = m_sc[...]
                highest = jnp.maximum(previous, jnp.max(scores, -1, keepdims=True))
            probs = jnp.where(visible, jnp.exp(scores - highest), 0.0)
            summed = lax.dot_general(
                probs.astype(jnp.bfloat16),
                value_block,
                (((1,), (1,)), ((), ())),
                preferred_element_type=jnp.float32,
            )
            if first:
                l_sc[...] = jnp.sum(probs, -1, keepdims=True)
                acc_sc[...] = summed
            else:
                correction = jnp.exp(previous - highest)
                l_sc[...] = l_sc[...] * correction + jnp.sum(probs, -1, keepdims=True)
                acc_sc[...] = acc_sc[...] * correction + summed
            m_sc[...] = highest

        shape = (rows, block)
        column = lax.broadcasted_iota(jnp.int32, shape, 1)

        @pl.when(step == 0)
        def _():
            token = lax.rem(lax.broadcasted_iota(jnp.int32, shape, 0), block)
            visit(kn_ref[0], vn_ref[0], column <= token, True)

        start = (step - 1) * block

        @pl.when((step > 0) & (start < length))
        def _():
            visit(kc_ref[0], vc_ref[0], column + start < length, False)

        @pl.when(step == blocks - 1)
        def _():
            o_ref[0] = (acc_sc[...] / l_sc[...]).astype(o_ref.dtype)

    def cache_map(head, step, length_ref):
        return (head, 0, jnp.clip(step - 1, 0, cached_blocks(length_ref) - 1))

    def fixed_map(head, step, length_ref):
        return (head, 0, 0)

    grid_spec = pltpu.PrefetchScalarGridSpec(
        num_scalar_prefetch=1,
        grid=(kv_heads, blocks),
        in_specs=[
            pl.BlockSpec((1, rows, head_dim), fixed_map),
            pl.BlockSpec((1, head_dim, block), cache_map),
            pl.BlockSpec((1, head_dim, block), cache_map),
            pl.BlockSpec((1, head_dim, block), fixed_map),
            pl.BlockSpec((1, head_dim, block), fixed_map),
        ],
        out_specs=pl.BlockSpec((1, rows, head_dim), fixed_map),
        scratch_shapes=[
            pltpu.VMEM((rows, 1), jnp.float32),
            pltpu.VMEM((rows, 1), jnp.float32),
            pltpu.VMEM((rows, head_dim), jnp.float32),
        ],
    )
    flops = 4 * kv_heads * rows * keys.shape[2] * head_dim
    return pl.pallas_call(
        kernel,
        grid_spec=grid_spec,
        out_shape=jax.ShapeDtypeStruct(query.shape, jnp.bfloat16),
        compiler_params=pltpu.CompilerParams(dimension_semantics=("arbitrary", "arbitrary")),
        cost_estimate=pl.CostEstimate(
            flops=flops,
            transcendentals=kv_heads * rows * keys.shape[2],
            bytes_accessed=2 * (query.size + keys.size + values.size + query.size),
        ),
    )(length.reshape(1), query, keys, values, key_new, value_new)


def shifted(values, shift):
    devices = lax.axis_size("ep")
    return lax.ppermute(values, "ep", [(i, (i + shift) % devices) for i in range(devices)])


def gather_columns(values):
    devices = lax.axis_size("ep")
    me = lax.axis_index("ep")
    width = values.shape[-1]
    whole = jnp.zeros(values.shape[:-1] + (width * devices,), values.dtype)
    for shift in range(devices):
        piece = values if shift == 0 else shifted(values, shift)
        source = (me - shift) % devices
        whole = lax.dynamic_update_slice_in_dim(whole, piece, source * width, values.ndim - 1)
    return whole


def sum_over_ep(part):
    devices = lax.axis_size("ep")
    half = part.shape[0] // 2
    total = part.astype(jnp.float32)
    for shift in range(1, devices):
        upper = shifted(part[:half], shift)
        lower = shifted(part[half:], shift)
        total = total + jnp.concatenate([upper, lower], 0).astype(jnp.float32)
    return total


def scatter_sum_over_ep(part, width):
    devices = lax.axis_size("ep")
    me = lax.axis_index("ep")
    total = lax.dynamic_slice_in_dim(part, me * width, width, 1).astype(jnp.float32)
    for shift in range(1, devices):
        target = (me + shift) % devices
        piece = lax.dynamic_slice_in_dim(part, target * width, width, 1)
        total = total + shifted(piece, shift).astype(jnp.float32)
    return total


def on_device(
    hidden,
    key_cache,
    value_cache,
    request_order,
    cached_lengths,
    expert_ids,
    gate_values,
    attn_gain,
    ffn_gain,
    w_query,
    w_key,
    w_value,
    w_out,
    expert_gate,
    expert_up,
    expert_down,
):
    own_rows = hidden[0]
    new_rows = own_rows.shape[0]
    own_width = own_rows.shape[1]
    head_dim = key_cache.shape[3]
    kv_local = key_cache.shape[1]
    heads_local = w_query.shape[1] // head_dim
    group = heads_local // kv_local
    per_device = expert_gate.shape[0]
    capacity = 3 * new_rows // 8
    me = lax.axis_index("ep")
    gate_whole = lax.all_gather(expert_gate, "req", axis=1, tiled=True)
    up_whole = lax.all_gather(expert_up, "req", axis=1, tiled=True)
    down_whole = lax.all_gather(expert_down, "req", axis=1, tiled=True)
    everyone = jnp.arange(request_order.shape[0], dtype=jnp.int32)
    request = jnp.sum(jnp.where(everyone == lax.axis_index("req"), request_order, 0))
    length = jnp.sum(jnp.where(everyone == request, cached_lengths, 0))
    rows_whole = gather_columns(own_rows)
    rows_f = rows_whole.astype(jnp.float32)
    normed = normalize(rows_f, attn_gain).astype(jnp.bfloat16)
    query = jnp.dot(normed, w_query, preferred_element_type=jnp.float32)
    key_new = jnp.dot(normed, w_key, preferred_element_type=jnp.float32)
    value_new = jnp.dot(normed, w_value, preferred_element_type=jnp.float32)
    positions = length + jnp.arange(new_rows, dtype=jnp.int32)
    query = rotate(
        query.reshape(new_rows, heads_local, head_dim).transpose(1, 0, 2), positions
    ).astype(jnp.bfloat16) * jnp.asarray(head_dim ** (-0.5), jnp.bfloat16)
    query = query.reshape(kv_local, group * new_rows, head_dim)
    key_new = rotate(
        key_new.reshape(new_rows, kv_local, head_dim).transpose(1, 0, 2), positions
    ).astype(jnp.bfloat16)
    value_new = (
        value_new.reshape(new_rows, kv_local, head_dim).transpose(1, 0, 2).astype(jnp.bfloat16)
    )
    zero = jnp.zeros((), jnp.int32)
    keys = lax.dynamic_update_slice(key_cache[0], key_new, (zero, length, zero))
    values = lax.dynamic_update_slice(value_cache[0], value_new, (zero, length, zero))
    attended = flash_attend(
        query,
        jnp.swapaxes(key_cache[0], 1, 2),
        jnp.swapaxes(value_cache[0], 1, 2),
        jnp.swapaxes(key_new, 1, 2),
        jnp.swapaxes(value_new, 1, 2),
        length,
    )
    attended = (
        attended.reshape(heads_local, new_rows, head_dim)
        .transpose(1, 0, 2)
        .reshape(new_rows, heads_local * head_dim)
    )
    head_part = jnp.dot(attended, w_out, preferred_element_type=jnp.float32).astype(jnp.bfloat16)
    head_sum = sum_over_ep(head_part)
    mixed_f = (rows_f + head_sum).astype(jnp.bfloat16).astype(jnp.float32)
    ffn_normed = normalize(mixed_f, ffn_gain).astype(jnp.bfloat16)
    table, gate_slot = route_tables(
        expert_ids[0],
        gate_values[0],
        me * per_device + jnp.arange(per_device, dtype=jnp.int32),
        capacity,
    )
    dispatched = jnp.einsum(
        "ect,td->ecd", table, ffn_normed, preferred_element_type=jnp.float32
    ).astype(jnp.bfloat16)
    gate_whole, up_whole, down_whole, dispatched = lax.optimization_barrier(
        (gate_whole, up_whole, down_whole, dispatched)
    )
    gate_act = jnp.einsum("ecd,edf->ecf", dispatched, gate_whole, preferred_element_type=jnp.float32)
    up_act = jnp.einsum("ecd,edf->ecf", dispatched, up_whole, preferred_element_type=jnp.float32)
    act = (jax.nn.silu(gate_act) * up_act).astype(jnp.bfloat16)
    output = jnp.einsum("ecf,efd->ecd", act, down_whole, preferred_element_type=jnp.float32)
    contrib = (output * gate_slot[..., None]).astype(jnp.bfloat16)
    expert_part = jnp.einsum(
        "ect,ecd->td", table, contrib, preferred_element_type=jnp.float32
    ).astype(jnp.bfloat16)
    expert_sum = scatter_sum_over_ep(expert_part, own_width)
    mixed_own = lax.dynamic_slice_in_dim(mixed_f, me * own_width, own_width, 1)
    result = (mixed_own + expert_sum).astype(jnp.bfloat16)
    return (result[None], keys[None], values[None])


def solution(mesh):
    in_specs = (
        P("req", None, "ep"),
        P("req", "ep", None, None),
        P("req", "ep", None, None),
        P(),
        P(),
        P("req", None, None),
        P("req", None, None),
        P(),
        P(),
        P(None, "ep"),
        P(None, "ep"),
        P(None, "ep"),
        P("ep", None),
        P("ep", "req", None),
        P("ep", "req", None),
        P("ep", "req", None),
    )
    out_specs = (P("req", None, "ep"), P("req", "ep", None, None), P("req", "ep", None, None))
    return jax.shard_map(
        on_device, mesh=mesh, in_specs=in_specs, out_specs=out_specs, check_vma=False
    )
```

```python
import jax
import jax.numpy as jnp
from jax import lax
from jax.experimental import pallas as pl
from jax.experimental.pallas import tpu as pltpu
from jax.sharding import PartitionSpec as P

epsilon = 1e-06


def normalize(values, gain):
    return values * lax.rsqrt(jnp.mean(values * values, -1, keepdims=True) + epsilon) * gain


def rotate(values, positions):
    half = values.shape[-1] // 2
    freq = 10000.0 ** (-jnp.arange(half, dtype=jnp.float32) * (2.0 / values.shape[-1]))
    angle = positions.astype(jnp.float32)[:, None] * freq[None, :]
    cosine = jnp.cos(angle)
    sine = jnp.sin(angle)
    first = values[..., :half]
    second = values[..., half:]
    return jnp.concatenate([first * cosine - second * sine, second * cosine + first * sine], -1)


def rounded(values):
    return lax.optimization_barrier(values.astype(jnp.bfloat16)).astype(jnp.float32)


def route_tables(chosen, gate_rows, wanted, capacity):
    hits = chosen[:, :, None] == wanted[None, None, :]
    member = jnp.sum(hits.astype(jnp.int32), 1, dtype=jnp.int32)
    weight = jnp.sum(jnp.where(hits, gate_rows[:, :, None], 0.0), 1)
    place = jnp.cumsum(member, 0, dtype=jnp.int32) - 1
    slots = jnp.arange(capacity, dtype=jnp.int32)
    table = (member.T[:, None, :] == 1) & (place.T[:, None, :] == slots[None, :, None])
    gate_slot = jnp.sum(jnp.where(table, weight.T[:, None, :], 0.0), 2)
    return (table.astype(jnp.bfloat16), gate_slot)


def flash_attend(query, keys, values, key_new, value_new, length):
    kv_heads, rows, head_dim = query.shape
    block = key_new.shape[2]
    blocks = keys.shape[2] // block

    def cached_blocks(length_ref):
        return (length_ref[0] + block - 1) // block

    def kernel(length_ref, q_ref, kc_ref, vc_ref, kn_ref, vn_ref, o_ref, m_sc, l_sc, acc_sc):
        step = pl.program_id(1)
        length = length_ref[0]

        def visit(key_block, value_block, visible, first):
            scores = jnp.dot(q_ref[0], key_block, preferred_element_type=jnp.float32)
            if visible is not None:
                scores = jnp.where(visible, scores, -1e30)
            if first:
                highest = jnp.max(scores, -1, keepdims=True)
            else:
                previous = m_sc[...]
                highest = jnp.maximum(previous, jnp.max(scores, -1, keepdims=True))
            probs = jnp.exp(scores - highest)
            if visible is not None:
                probs = jnp.where(visible, probs, 0.0)
            summed = lax.dot_general(
                probs.astype(jnp.bfloat16),
                value_block,
                (((1,), (1,)), ((), ())),
                preferred_element_type=jnp.float32,
            )
            if first:
                l_sc[...] = jnp.sum(probs, -1, keepdims=True)
                acc_sc[...] = summed
            else:
                correction = jnp.exp(previous - highest)
                l_sc[...] = l_sc[...] * correction + jnp.sum(probs, -1, keepdims=True)
                acc_sc[...] = acc_sc[...] * correction + summed
            m_sc[...] = highest

        shape = (rows, block)
        column = lax.broadcasted_iota(jnp.int32, shape, 1)

        @pl.when(step == 0)
        def _():
            token = lax.rem(lax.broadcasted_iota(jnp.int32, shape, 0), block)
            visit(kn_ref[0], vn_ref[0], column <= token, True)

        start = (step - 1) * block

        whole = (step > 0) & (start + block <= length)

        @pl.when(whole)
        def _():
            visit(kc_ref[0], vc_ref[0], None, False)

        @pl.when((step > 0) & jnp.logical_not(whole) & (start < length))
        def _():
            visit(kc_ref[0], vc_ref[0], column + start < length, False)

        @pl.when(step == blocks - 1)
        def _():
            o_ref[0] = (acc_sc[...] / l_sc[...]).astype(o_ref.dtype)

    def cache_map(head, step, length_ref):
        return (head, 0, jnp.clip(step - 1, 0, cached_blocks(length_ref) - 1))

    def fixed_map(head, step, length_ref):
        return (head, 0, 0)

    grid_spec = pltpu.PrefetchScalarGridSpec(
        num_scalar_prefetch=1,
        grid=(kv_heads, blocks),
        in_specs=[
            pl.BlockSpec((1, rows, head_dim), fixed_map),
            pl.BlockSpec((1, head_dim, block), cache_map),
            pl.BlockSpec((1, head_dim, block), cache_map),
            pl.BlockSpec((1, head_dim, block), fixed_map),
            pl.BlockSpec((1, head_dim, block), fixed_map),
        ],
        out_specs=pl.BlockSpec((1, rows, head_dim), fixed_map),
        scratch_shapes=[
            pltpu.VMEM((rows, 1), jnp.float32),
            pltpu.VMEM((rows, 1), jnp.float32),
            pltpu.VMEM((rows, head_dim), jnp.float32),
        ],
    )
    flops = 4 * kv_heads * rows * keys.shape[2] * head_dim
    return pl.pallas_call(
        kernel,
        grid_spec=grid_spec,
        out_shape=jax.ShapeDtypeStruct(query.shape, jnp.bfloat16),
        compiler_params=pltpu.CompilerParams(dimension_semantics=("arbitrary", "arbitrary")),
        cost_estimate=pl.CostEstimate(
            flops=flops,
            transcendentals=kv_heads * rows * keys.shape[2],
            bytes_accessed=2 * (query.size + keys.size + values.size + query.size),
        ),
    )(length.reshape(1), query, keys, values, key_new, value_new)


def shifted(values, shift):
    devices = lax.axis_size("ep")
    return lax.ppermute(values, "ep", [(i, (i + shift) % devices) for i in range(devices)])


def gather_columns(values):
    devices = lax.axis_size("ep")
    me = lax.axis_index("ep")
    width = values.shape[-1]
    whole = jnp.zeros(values.shape[:-1] + (width * devices,), values.dtype)
    for shift in range(devices):
        piece = values if shift == 0 else shifted(values, shift)
        source = (me - shift) % devices
        whole = lax.dynamic_update_slice_in_dim(whole, piece, source * width, values.ndim - 1)
    return whole


def sum_over_ep(part):
    devices = lax.axis_size("ep")
    half = part.shape[0] // 2
    total = part.astype(jnp.float32)
    for shift in range(1, devices):
        upper = shifted(part[:half], shift)
        lower = shifted(part[half:], shift)
        total = total + jnp.concatenate([upper, lower], 0).astype(jnp.float32)
    return total


def scatter_sum_over_ep(part, width):
    devices = lax.axis_size("ep")
    me = lax.axis_index("ep")
    total = lax.dynamic_slice_in_dim(part, me * width, width, 1).astype(jnp.float32)
    for shift in range(1, devices):
        target = (me + shift) % devices
        piece = lax.dynamic_slice_in_dim(part, target * width, width, 1)
        total = total + shifted(piece, shift).astype(jnp.float32)
    return total


def on_device(
    hidden,
    key_cache,
    value_cache,
    request_order,
    cached_lengths,
    expert_ids,
    gate_values,
    attn_gain,
    ffn_gain,
    w_query,
    w_key,
    w_value,
    w_out,
    expert_gate,
    expert_up,
    expert_down,
):
    own_rows = hidden[0]
    new_rows = own_rows.shape[0]
    own_width = own_rows.shape[1]
    head_dim = key_cache.shape[3]
    kv_local = key_cache.shape[1]
    heads_local = w_query.shape[1] // head_dim
    group = heads_local // kv_local
    per_device = expert_gate.shape[0]
    capacity = 3 * new_rows // 8
    me = lax.axis_index("ep")
    gate_whole = lax.all_gather(expert_gate, "req", axis=1, tiled=True)
    up_whole = lax.all_gather(expert_up, "req", axis=1, tiled=True)
    down_whole = lax.all_gather(expert_down, "req", axis=1, tiled=True)
    everyone = jnp.arange(request_order.shape[0], dtype=jnp.int32)
    request = jnp.sum(jnp.where(everyone == lax.axis_index("req"), request_order, 0))
    length = jnp.sum(jnp.where(everyone == request, cached_lengths, 0))
    rows_whole = gather_columns(own_rows)
    rows_f = rows_whole.astype(jnp.float32)
    normed = normalize(rows_f, attn_gain).astype(jnp.bfloat16)
    query = jnp.dot(normed, w_query, preferred_element_type=jnp.float32)
    key_new = jnp.dot(normed, w_key, preferred_element_type=jnp.float32)
    value_new = jnp.dot(normed, w_value, preferred_element_type=jnp.float32)
    positions = length + jnp.arange(new_rows, dtype=jnp.int32)
    query = rotate(
        query.reshape(new_rows, heads_local, head_dim).transpose(1, 0, 2), positions
    ).astype(jnp.bfloat16) * jnp.asarray(head_dim ** (-0.5), jnp.bfloat16)
    query = query.reshape(kv_local, group * new_rows, head_dim)
    key_new = rotate(
        key_new.reshape(new_rows, kv_local, head_dim).transpose(1, 0, 2), positions
    ).astype(jnp.bfloat16)
    value_new = (
        value_new.reshape(new_rows, kv_local, head_dim).transpose(1, 0, 2).astype(jnp.bfloat16)
    )
    zero = jnp.zeros((), jnp.int32)
    keys = lax.dynamic_update_slice(key_cache[0], key_new, (zero, length, zero))
    values = lax.dynamic_update_slice(value_cache[0], value_new, (zero, length, zero))
    attended = flash_attend(
        query,
        jnp.swapaxes(key_cache[0], 1, 2),
        jnp.swapaxes(value_cache[0], 1, 2),
        jnp.swapaxes(key_new, 1, 2),
        jnp.swapaxes(value_new, 1, 2),
        length,
    )
    attended = (
        attended.reshape(heads_local, new_rows, head_dim)
        .transpose(1, 0, 2)
        .reshape(new_rows, heads_local * head_dim)
    )
    head_part = jnp.dot(attended, w_out, preferred_element_type=jnp.float32).astype(jnp.bfloat16)
    head_sum = sum_over_ep(head_part)
    mixed_f = (rows_f + head_sum).astype(jnp.bfloat16).astype(jnp.float32)
    ffn_normed = normalize(mixed_f, ffn_gain).astype(jnp.bfloat16)
    table, gate_slot = route_tables(
        expert_ids[0],
        gate_values[0],
        me * per_device + jnp.arange(per_device, dtype=jnp.int32),
        capacity,
    )
    dispatched = jnp.einsum(
        "ect,td->ecd", table, ffn_normed, preferred_element_type=jnp.float32
    ).astype(jnp.bfloat16)
    gate_whole, up_whole, dispatched = lax.optimization_barrier((gate_whole, up_whole, dispatched))
    gate_act = jnp.einsum("ecd,edf->ecf", dispatched, gate_whole, preferred_element_type=jnp.float32)
    up_act = jnp.einsum("ecd,edf->ecf", dispatched, up_whole, preferred_element_type=jnp.float32)
    act = (jax.nn.silu(gate_act) * up_act).astype(jnp.bfloat16)
    down_whole, act = lax.optimization_barrier((down_whole, act))
    output = jnp.einsum("ecf,efd->ecd", act, down_whole, preferred_element_type=jnp.float32)
    contrib = (output * gate_slot[..., None]).astype(jnp.bfloat16)
    expert_part = jnp.einsum(
        "ect,ecd->td", table, contrib, preferred_element_type=jnp.float32
    ).astype(jnp.bfloat16)
    expert_sum = scatter_sum_over_ep(expert_part, own_width)
    mixed_own = lax.dynamic_slice_in_dim(mixed_f, me * own_width, own_width, 1)
    result = (mixed_own + expert_sum).astype(jnp.bfloat16)
    return (result[None], keys[None], values[None])


def solution(mesh):
    in_specs = (
        P("req", None, "ep"),
        P("req", "ep", None, None),
        P("req", "ep", None, None),
        P(),
        P(),
        P("req", None, None),
        P("req", None, None),
        P(),
        P(),
        P(None, "ep"),
        P(None, "ep"),
        P(None, "ep"),
        P("ep", None),
        P("ep", "req", None),
        P("ep", "req", None),
        P("ep", "req", None),
    )
    out_specs = (P("req", None, "ep"), P("req", "ep", None, None), P("req", "ep", None, None))
    return jax.shard_map(
        on_device, mesh=mesh, in_specs=in_specs, out_specs=out_specs, check_vma=False
    )
```

```python
import jax
import jax.numpy as jnp
from jax import lax
from jax.experimental import pallas as pl
from jax.experimental.pallas import tpu as pltpu
from jax.sharding import PartitionSpec as P

epsilon = 1e-06


def normalize(values, gain):
    return values * lax.rsqrt(jnp.mean(values * values, -1, keepdims=True) + epsilon) * gain


def rotate(values, positions):
    half = values.shape[-1] // 2
    freq = 10000.0 ** (-jnp.arange(half, dtype=jnp.float32) * (2.0 / values.shape[-1]))
    angle = positions.astype(jnp.float32)[:, None] * freq[None, :]
    cosine = jnp.cos(angle)
    sine = jnp.sin(angle)
    first = values[..., :half]
    second = values[..., half:]
    return jnp.concatenate([first * cosine - second * sine, second * cosine + first * sine], -1)


def rounded(values):
    return lax.optimization_barrier(values.astype(jnp.bfloat16)).astype(jnp.float32)


def route_tables(chosen, gate_rows, wanted, capacity):
    hits = chosen[:, :, None] == wanted[None, None, :]
    member = jnp.sum(hits.astype(jnp.int32), 1, dtype=jnp.int32)
    weight = jnp.sum(jnp.where(hits, gate_rows[:, :, None], 0.0), 1)
    place = jnp.cumsum(member, 0, dtype=jnp.int32) - 1
    slots = jnp.arange(capacity, dtype=jnp.int32)
    table = (member.T[:, None, :] == 1) & (place.T[:, None, :] == slots[None, :, None])
    gate_slot = jnp.sum(jnp.where(table, weight.T[:, None, :], 0.0), 2)
    return (table.astype(jnp.bfloat16), gate_slot)


def flash_attend(query, keys, values, key_new, value_new, length):
    kv_heads, rows, head_dim = query.shape
    block = key_new.shape[2]
    blocks = keys.shape[2] // block

    def cached_blocks(length_ref):
        return (length_ref[0] + block - 1) // block

    def kernel(length_ref, q_ref, kc_ref, vc_ref, kn_ref, vn_ref, o_ref, m_sc, l_sc, acc_sc):
        step = pl.program_id(1)
        length = length_ref[0]

        def visit(key_block, value_block, visible, first):
            scores = jnp.dot(q_ref[0], key_block, preferred_element_type=jnp.float32)
            if visible is not None:
                scores = jnp.where(visible, scores, -1e30)
            if first:
                highest = jnp.max(scores, -1, keepdims=True)
            else:
                previous = m_sc[...]
                highest = jnp.maximum(previous, jnp.max(scores, -1, keepdims=True))
            probs = jnp.exp(scores - highest)
            if visible is not None:
                probs = jnp.where(visible, probs, 0.0)
            summed = lax.dot_general(
                probs.astype(jnp.bfloat16),
                value_block,
                (((1,), (1,)), ((), ())),
                preferred_element_type=jnp.float32,
            )
            if first:
                l_sc[...] = jnp.sum(probs, -1, keepdims=True)
                acc_sc[...] = summed
            else:
                correction = jnp.exp(previous - highest)
                l_sc[...] = l_sc[...] * correction + jnp.sum(probs, -1, keepdims=True)
                acc_sc[...] = acc_sc[...] * correction + summed
            m_sc[...] = highest

        shape = (rows, block)
        column = lax.broadcasted_iota(jnp.int32, shape, 1)

        @pl.when(step == 0)
        def _():
            token = lax.rem(lax.broadcasted_iota(jnp.int32, shape, 0), block)
            visit(kn_ref[0], vn_ref[0], column <= token, True)

        start = (step - 1) * block

        whole = (step > 0) & (start + block <= length)

        @pl.when(whole)
        def _():
            visit(kc_ref[0], vc_ref[0], None, False)

        @pl.when((step > 0) & jnp.logical_not(whole) & (start < length))
        def _():
            visit(kc_ref[0], vc_ref[0], column + start < length, False)

        @pl.when(step == blocks - 1)
        def _():
            o_ref[0] = (acc_sc[...] / l_sc[...]).astype(o_ref.dtype)

    def cache_map(head, step, length_ref):
        return (head, 0, jnp.clip(step - 1, 0, cached_blocks(length_ref) - 1))

    def fixed_map(head, step, length_ref):
        return (head, 0, 0)

    grid_spec = pltpu.PrefetchScalarGridSpec(
        num_scalar_prefetch=1,
        grid=(kv_heads, blocks),
        in_specs=[
            pl.BlockSpec((1, rows, head_dim), fixed_map),
            pl.BlockSpec((1, head_dim, block), cache_map),
            pl.BlockSpec((1, head_dim, block), cache_map),
            pl.BlockSpec((1, head_dim, block), fixed_map),
            pl.BlockSpec((1, head_dim, block), fixed_map),
        ],
        out_specs=pl.BlockSpec((1, rows, head_dim), fixed_map),
        scratch_shapes=[
            pltpu.VMEM((rows, 1), jnp.float32),
            pltpu.VMEM((rows, 1), jnp.float32),
            pltpu.VMEM((rows, head_dim), jnp.float32),
        ],
    )
    flops = 4 * kv_heads * rows * keys.shape[2] * head_dim
    return pl.pallas_call(
        kernel,
        grid_spec=grid_spec,
        out_shape=jax.ShapeDtypeStruct(query.shape, jnp.bfloat16),
        compiler_params=pltpu.CompilerParams(dimension_semantics=("arbitrary", "arbitrary")),
        cost_estimate=pl.CostEstimate(
            flops=flops,
            transcendentals=kv_heads * rows * keys.shape[2],
            bytes_accessed=2 * (query.size + keys.size + values.size + query.size),
        ),
    )(length.reshape(1), query, keys, values, key_new, value_new)


def gather_rows(values, axis_name):
    devices = lax.axis_size(axis_name)
    me = lax.axis_index(axis_name)
    rows = values.shape[1]
    whole = jnp.zeros((values.shape[0], rows * devices) + values.shape[2:], values.dtype)
    for shift in range(devices):
        if shift == 0:
            piece = values
        else:
            pairs = [(i, (i + shift) % devices) for i in range(devices)]
            piece = lax.ppermute(values, axis_name, pairs)
        source = (me - shift) % devices
        whole = lax.dynamic_update_slice_in_dim(whole, piece, source * rows, 1)
    return whole


def shifted(values, shift):
    devices = lax.axis_size("ep")
    return lax.ppermute(values, "ep", [(i, (i + shift) % devices) for i in range(devices)])


def gather_columns(values):
    devices = lax.axis_size("ep")
    me = lax.axis_index("ep")
    width = values.shape[-1]
    whole = jnp.zeros(values.shape[:-1] + (width * devices,), values.dtype)
    for shift in range(devices):
        piece = values if shift == 0 else shifted(values, shift)
        source = (me - shift) % devices
        whole = lax.dynamic_update_slice_in_dim(whole, piece, source * width, values.ndim - 1)
    return whole


def sum_over_ep(part):
    devices = lax.axis_size("ep")
    half = part.shape[0] // 2
    total = part.astype(jnp.float32)
    for shift in range(1, devices):
        upper = shifted(part[:half], shift)
        lower = shifted(part[half:], shift)
        total = total + jnp.concatenate([upper, lower], 0).astype(jnp.float32)
    return total


def scatter_sum_over_ep(part, width):
    devices = lax.axis_size("ep")
    me = lax.axis_index("ep")
    total = lax.dynamic_slice_in_dim(part, me * width, width, 1).astype(jnp.float32)
    for shift in range(1, devices):
        target = (me + shift) % devices
        piece = lax.dynamic_slice_in_dim(part, target * width, width, 1)
        total = total + shifted(piece, shift).astype(jnp.float32)
    return total


def on_device(
    hidden,
    key_cache,
    value_cache,
    request_order,
    cached_lengths,
    expert_ids,
    gate_values,
    attn_gain,
    ffn_gain,
    w_query,
    w_key,
    w_value,
    w_out,
    expert_gate,
    expert_up,
    expert_down,
):
    own_rows = hidden[0]
    new_rows = own_rows.shape[0]
    own_width = own_rows.shape[1]
    head_dim = key_cache.shape[3]
    kv_local = key_cache.shape[1]
    heads_local = w_query.shape[1] // head_dim
    group = heads_local // kv_local
    per_device = expert_gate.shape[0]
    capacity = 3 * new_rows // 8
    me = lax.axis_index("ep")
    gate_whole = lax.all_gather(expert_gate, "req", axis=1, tiled=True)
    up_whole = lax.all_gather(expert_up, "req", axis=1, tiled=True)
    everyone = jnp.arange(request_order.shape[0], dtype=jnp.int32)
    request = jnp.sum(jnp.where(everyone == lax.axis_index("req"), request_order, 0))
    length = jnp.sum(jnp.where(everyone == request, cached_lengths, 0))
    rows_whole = gather_columns(own_rows)
    expert_down, rows_whole = lax.optimization_barrier((expert_down, rows_whole))
    down_whole = gather_rows(expert_down, "req")
    rows_f = rows_whole.astype(jnp.float32)
    normed = normalize(rows_f, attn_gain).astype(jnp.bfloat16)
    query = jnp.dot(normed, w_query, preferred_element_type=jnp.float32)
    key_new = jnp.dot(normed, w_key, preferred_element_type=jnp.float32)
    value_new = jnp.dot(normed, w_value, preferred_element_type=jnp.float32)
    positions = length + jnp.arange(new_rows, dtype=jnp.int32)
    query = rotate(
        query.reshape(new_rows, heads_local, head_dim).transpose(1, 0, 2), positions
    ).astype(jnp.bfloat16) * jnp.asarray(head_dim ** (-0.5), jnp.bfloat16)
    query = query.reshape(kv_local, group * new_rows, head_dim)
    key_new = rotate(
        key_new.reshape(new_rows, kv_local, head_dim).transpose(1, 0, 2), positions
    ).astype(jnp.bfloat16)
    value_new = (
        value_new.reshape(new_rows, kv_local, head_dim).transpose(1, 0, 2).astype(jnp.bfloat16)
    )
    zero = jnp.zeros((), jnp.int32)
    keys = lax.dynamic_update_slice(key_cache[0], key_new, (zero, length, zero))
    values = lax.dynamic_update_slice(value_cache[0], value_new, (zero, length, zero))
    attended = flash_attend(
        query,
        jnp.swapaxes(key_cache[0], 1, 2),
        jnp.swapaxes(value_cache[0], 1, 2),
        jnp.swapaxes(key_new, 1, 2),
        jnp.swapaxes(value_new, 1, 2),
        length,
    )
    attended = (
        attended.reshape(heads_local, new_rows, head_dim)
        .transpose(1, 0, 2)
        .reshape(new_rows, heads_local * head_dim)
    )
    head_part = jnp.dot(attended, w_out, preferred_element_type=jnp.float32).astype(jnp.bfloat16)
    head_sum = sum_over_ep(head_part)
    mixed_f = (rows_f + head_sum).astype(jnp.bfloat16).astype(jnp.float32)
    ffn_normed = normalize(mixed_f, ffn_gain).astype(jnp.bfloat16)
    table, gate_slot = route_tables(
        expert_ids[0],
        gate_values[0],
        me * per_device + jnp.arange(per_device, dtype=jnp.int32),
        capacity,
    )
    dispatched = jnp.einsum(
        "ect,td->ecd", table, ffn_normed, preferred_element_type=jnp.float32
    ).astype(jnp.bfloat16)
    gate_whole, up_whole, dispatched = lax.optimization_barrier((gate_whole, up_whole, dispatched))
    gate_act = jnp.einsum("ecd,edf->ecf", dispatched, gate_whole, preferred_element_type=jnp.float32)
    up_act = jnp.einsum("ecd,edf->ecf", dispatched, up_whole, preferred_element_type=jnp.float32)
    act = (jax.nn.silu(gate_act) * up_act).astype(jnp.bfloat16)
    down_whole, act = lax.optimization_barrier((down_whole, act))
    output = jnp.einsum("ecf,efd->ecd", act, down_whole, preferred_element_type=jnp.float32)
    contrib = (output * gate_slot[..., None]).astype(jnp.bfloat16)
    expert_part = jnp.einsum(
        "ect,ecd->td", table, contrib, preferred_element_type=jnp.float32
    ).astype(jnp.bfloat16)
    expert_sum = scatter_sum_over_ep(expert_part, own_width)
    mixed_own = lax.dynamic_slice_in_dim(mixed_f, me * own_width, own_width, 1)
    result = (mixed_own + expert_sum).astype(jnp.bfloat16)
    return (result[None], keys[None], values[None])


def solution(mesh):
    in_specs = (
        P("req", None, "ep"),
        P("req", "ep", None, None),
        P("req", "ep", None, None),
        P(),
        P(),
        P("req", None, None),
        P("req", None, None),
        P(),
        P(),
        P(None, "ep"),
        P(None, "ep"),
        P(None, "ep"),
        P("ep", None),
        P("ep", "req", None),
        P("ep", "req", None),
        P("ep", "req", None),
    )
    out_specs = (P("req", None, "ep"), P("req", "ep", None, None), P("req", "ep", None, None))
    return jax.shard_map(
        on_device, mesh=mesh, in_specs=in_specs, out_specs=out_specs, check_vma=False
    )
```

```python
import jax
import jax.numpy as jnp
from jax import lax
from jax.experimental import pallas as pl
from jax.experimental.pallas import tpu as pltpu
from jax.sharding import PartitionSpec as P

epsilon = 1e-06


def normalize(values, gain):
    return values * lax.rsqrt(jnp.mean(values * values, -1, keepdims=True) + epsilon) * gain


def rotate(values, positions):
    half = values.shape[-1] // 2
    freq = 10000.0 ** (-jnp.arange(half, dtype=jnp.float32) * (2.0 / values.shape[-1]))
    angle = positions.astype(jnp.float32)[:, None] * freq[None, :]
    cosine = jnp.cos(angle)
    sine = jnp.sin(angle)
    first = values[..., :half]
    second = values[..., half:]
    return jnp.concatenate([first * cosine - second * sine, second * cosine + first * sine], -1)


def rounded(values):
    return lax.optimization_barrier(values.astype(jnp.bfloat16)).astype(jnp.float32)


def route_tables(chosen, gate_rows, wanted, capacity):
    hits = chosen[:, :, None] == wanted[None, None, :]
    member = jnp.sum(hits.astype(jnp.int32), 1, dtype=jnp.int32)
    weight = jnp.sum(jnp.where(hits, gate_rows[:, :, None], 0.0), 1)
    place = jnp.cumsum(member, 0, dtype=jnp.int32) - 1
    slots = jnp.arange(capacity, dtype=jnp.int32)
    table = (member.T[:, None, :] == 1) & (place.T[:, None, :] == slots[None, :, None])
    gate_slot = jnp.sum(jnp.where(table, weight.T[:, None, :], 0.0), 2)
    return (table.astype(jnp.bfloat16), gate_slot)


def flash_attend(query, keys, values, key_new, value_new, length):
    kv_heads, rows, head_dim = query.shape
    block = key_new.shape[2]
    blocks = keys.shape[2] // block

    def cached_blocks(length_ref):
        return (length_ref[0] + block - 1) // block

    def kernel(length_ref, q_ref, kc_ref, vc_ref, kn_ref, vn_ref, o_ref, m_sc, l_sc, acc_sc):
        step = pl.program_id(1)
        length = length_ref[0]

        def visit(key_block, value_block, visible, first):
            scores = jnp.dot(q_ref[0], key_block, preferred_element_type=jnp.float32)
            if visible is not None:
                scores = jnp.where(visible, scores, -1e30)
            if first:
                highest = jnp.max(scores, -1, keepdims=True)
            else:
                previous = m_sc[...]
                highest = jnp.maximum(previous, jnp.max(scores, -1, keepdims=True))
            probs = jnp.exp(scores - highest)
            if visible is not None:
                probs = jnp.where(visible, probs, 0.0)
            summed = lax.dot_general(
                probs.astype(jnp.bfloat16),
                value_block,
                (((1,), (1,)), ((), ())),
                preferred_element_type=jnp.float32,
            )
            if first:
                l_sc[...] = jnp.sum(probs, -1, keepdims=True)
                acc_sc[...] = summed
            else:
                correction = jnp.exp(previous - highest)
                l_sc[...] = l_sc[...] * correction + jnp.sum(probs, -1, keepdims=True)
                acc_sc[...] = acc_sc[...] * correction + summed
            m_sc[...] = highest

        shape = (rows, block)
        column = lax.broadcasted_iota(jnp.int32, shape, 1)

        @pl.when(step == 0)
        def _():
            token = lax.rem(lax.broadcasted_iota(jnp.int32, shape, 0), block)
            visit(kn_ref[0], vn_ref[0], column <= token, True)

        start = (step - 1) * block

        whole = (step > 0) & (start + block <= length)

        @pl.when(whole)
        def _():
            visit(kc_ref[0], vc_ref[0], None, False)

        @pl.when((step > 0) & jnp.logical_not(whole) & (start < length))
        def _():
            visit(kc_ref[0], vc_ref[0], column + start < length, False)

        @pl.when(step == blocks - 1)
        def _():
            o_ref[0] = (acc_sc[...] / l_sc[...]).astype(o_ref.dtype)

    def cache_map(head, step, length_ref):
        return (head, 0, jnp.clip(step - 1, 0, cached_blocks(length_ref) - 1))

    def fixed_map(head, step, length_ref):
        return (head, 0, 0)

    grid_spec = pltpu.PrefetchScalarGridSpec(
        num_scalar_prefetch=1,
        grid=(kv_heads, blocks),
        in_specs=[
            pl.BlockSpec((1, rows, head_dim), fixed_map),
            pl.BlockSpec((1, head_dim, block), cache_map),
            pl.BlockSpec((1, head_dim, block), cache_map),
            pl.BlockSpec((1, head_dim, block), fixed_map),
            pl.BlockSpec((1, head_dim, block), fixed_map),
        ],
        out_specs=pl.BlockSpec((1, rows, head_dim), fixed_map),
        scratch_shapes=[
            pltpu.VMEM((rows, 1), jnp.float32),
            pltpu.VMEM((rows, 1), jnp.float32),
            pltpu.VMEM((rows, head_dim), jnp.float32),
        ],
    )
    flops = 4 * kv_heads * rows * keys.shape[2] * head_dim
    return pl.pallas_call(
        kernel,
        grid_spec=grid_spec,
        out_shape=jax.ShapeDtypeStruct(query.shape, jnp.bfloat16),
        compiler_params=pltpu.CompilerParams(dimension_semantics=("arbitrary", "arbitrary")),
        cost_estimate=pl.CostEstimate(
            flops=flops,
            transcendentals=kv_heads * rows * keys.shape[2],
            bytes_accessed=2 * (query.size + keys.size + values.size + query.size),
        ),
    )(length.reshape(1), query, keys, values, key_new, value_new)


def shifted(values, shift):
    devices = lax.axis_size("ep")
    return lax.ppermute(values, "ep", [(i, (i + shift) % devices) for i in range(devices)])


def gather_columns(values):
    devices = lax.axis_size("ep")
    me = lax.axis_index("ep")
    width = values.shape[-1]
    whole = jnp.zeros(values.shape[:-1] + (width * devices,), values.dtype)
    for shift in range(devices):
        piece = values if shift == 0 else shifted(values, shift)
        source = (me - shift) % devices
        whole = lax.dynamic_update_slice_in_dim(whole, piece, source * width, values.ndim - 1)
    return whole


def sum_over_ep(part):
    devices = lax.axis_size("ep")
    half = part.shape[0] // 2
    total = part.astype(jnp.float32)
    for shift in range(1, devices):
        upper = shifted(part[:half], shift)
        lower = shifted(part[half:], shift)
        total = total + jnp.concatenate([upper, lower], 0).astype(jnp.float32)
    return total


def on_device(
    hidden,
    key_cache,
    value_cache,
    request_order,
    cached_lengths,
    expert_ids,
    gate_values,
    attn_gain,
    ffn_gain,
    w_query,
    w_key,
    w_value,
    w_out,
    expert_gate,
    expert_up,
    expert_down,
):
    own_rows = hidden[0]
    new_rows = own_rows.shape[0]
    own_width = own_rows.shape[1]
    head_dim = key_cache.shape[3]
    kv_local = key_cache.shape[1]
    heads_local = w_query.shape[1] // head_dim
    group = heads_local // kv_local
    per_device = expert_gate.shape[0]
    capacity = 3 * new_rows // 8
    me = lax.axis_index("ep")
    gate_up = lax.all_gather(jnp.stack([expert_gate, expert_up]), "req", axis=2, tiled=True)
    gate_whole = gate_up[0]
    up_whole = gate_up[1]
    down_whole = lax.all_gather(expert_down, "req", axis=1, tiled=True)
    everyone = jnp.arange(request_order.shape[0], dtype=jnp.int32)
    request = jnp.sum(jnp.where(everyone == lax.axis_index("req"), request_order, 0))
    length = jnp.sum(jnp.where(everyone == request, cached_lengths, 0))
    rows_whole = gather_columns(own_rows)
    rows_f = rows_whole.astype(jnp.float32)
    normed = normalize(rows_f, attn_gain).astype(jnp.bfloat16)
    query = jnp.dot(normed, w_query, preferred_element_type=jnp.float32)
    key_new = jnp.dot(normed, w_key, preferred_element_type=jnp.float32)
    value_new = jnp.dot(normed, w_value, preferred_element_type=jnp.float32)
    positions = length + jnp.arange(new_rows, dtype=jnp.int32)
    query = rotate(
        query.reshape(new_rows, heads_local, head_dim).transpose(1, 0, 2), positions
    ).astype(jnp.bfloat16) * jnp.asarray(head_dim ** (-0.5), jnp.bfloat16)
    query = query.reshape(kv_local, group * new_rows, head_dim)
    key_new = rotate(
        key_new.reshape(new_rows, kv_local, head_dim).transpose(1, 0, 2), positions
    ).astype(jnp.bfloat16)
    value_new = (
        value_new.reshape(new_rows, kv_local, head_dim).transpose(1, 0, 2).astype(jnp.bfloat16)
    )
    zero = jnp.zeros((), jnp.int32)
    keys = lax.dynamic_update_slice(key_cache[0], key_new, (zero, length, zero))
    values = lax.dynamic_update_slice(value_cache[0], value_new, (zero, length, zero))
    attended = flash_attend(
        query,
        jnp.swapaxes(key_cache[0], 1, 2),
        jnp.swapaxes(value_cache[0], 1, 2),
        jnp.swapaxes(key_new, 1, 2),
        jnp.swapaxes(value_new, 1, 2),
        length,
    )
    attended = (
        attended.reshape(heads_local, new_rows, head_dim)
        .transpose(1, 0, 2)
        .reshape(new_rows, heads_local * head_dim)
    )
    head_part = jnp.dot(attended, w_out, preferred_element_type=jnp.float32).astype(jnp.bfloat16)
    head_sum = sum_over_ep(head_part)
    mixed_f = (rows_f + head_sum).astype(jnp.bfloat16).astype(jnp.float32)
    ffn_normed = normalize(mixed_f, ffn_gain).astype(jnp.bfloat16)
    table, gate_slot = route_tables(
        expert_ids[0],
        gate_values[0],
        me * per_device + jnp.arange(per_device, dtype=jnp.int32),
        capacity,
    )
    dispatched = jnp.einsum(
        "ect,td->ecd", table, ffn_normed, preferred_element_type=jnp.float32
    ).astype(jnp.bfloat16)
    gate_whole, up_whole, dispatched = lax.optimization_barrier((gate_whole, up_whole, dispatched))
    gate_act = jnp.einsum("ecd,edf->ecf", dispatched, gate_whole, preferred_element_type=jnp.float32)
    up_act = jnp.einsum("ecd,edf->ecf", dispatched, up_whole, preferred_element_type=jnp.float32)
    act = (jax.nn.silu(gate_act) * up_act).astype(jnp.bfloat16)
    down_whole, act = lax.optimization_barrier((down_whole, act))
    devices = lax.axis_size("ep")

    def expert_block(target):
        down_block = lax.dynamic_slice_in_dim(down_whole, target * own_width, own_width, 2)
        output = jnp.einsum("ecf,efd->ecd", act, down_block, preferred_element_type=jnp.float32)
        contrib = (output * gate_slot[..., None]).astype(jnp.bfloat16)
        return jnp.einsum(
            "ect,ecd->td", table, contrib, preferred_element_type=jnp.float32
        ).astype(jnp.bfloat16)

    received = [shifted(expert_block((me + shift) % devices), shift) for shift in range(1, devices)]
    expert_sum = expert_block(me).astype(jnp.float32)
    for piece in received:
        expert_sum = expert_sum + piece.astype(jnp.float32)
    mixed_own = lax.dynamic_slice_in_dim(mixed_f, me * own_width, own_width, 1)
    result = (mixed_own + expert_sum).astype(jnp.bfloat16)
    return (result[None], keys[None], values[None])


def solution(mesh):
    in_specs = (
        P("req", None, "ep"),
        P("req", "ep", None, None),
        P("req", "ep", None, None),
        P(),
        P(),
        P("req", None, None),
        P("req", None, None),
        P(),
        P(),
        P(None, "ep"),
        P(None, "ep"),
        P(None, "ep"),
        P("ep", None),
        P("ep", "req", None),
        P("ep", "req", None),
        P("ep", "req", None),
    )
    out_specs = (P("req", None, "ep"), P("req", "ep", None, None), P("req", "ep", None, None))
    return jax.shard_map(
        on_device, mesh=mesh, in_specs=in_specs, out_specs=out_specs, check_vma=False
    )
```

```python
import jax
import jax.numpy as jnp
from jax import lax
from jax.experimental import pallas as pl
from jax.experimental.pallas import tpu as pltpu
from jax.sharding import PartitionSpec as P

epsilon = 1e-06


def normalize(values, gain):
    return values * lax.rsqrt(jnp.mean(values * values, -1, keepdims=True) + epsilon) * gain


def rotate(values, positions):
    half = values.shape[-1] // 2
    freq = 10000.0 ** (-jnp.arange(half, dtype=jnp.float32) * (2.0 / values.shape[-1]))
    angle = positions.astype(jnp.float32)[:, None] * freq[None, :]
    cosine = jnp.cos(angle)
    sine = jnp.sin(angle)
    first = values[..., :half]
    second = values[..., half:]
    return jnp.concatenate([first * cosine - second * sine, second * cosine + first * sine], -1)


def rounded(values):
    return lax.optimization_barrier(values.astype(jnp.bfloat16)).astype(jnp.float32)


def route_tables(chosen, gate_rows, wanted, capacity):
    hits = chosen[:, :, None] == wanted[None, None, :]
    member = jnp.sum(hits.astype(jnp.int32), 1, dtype=jnp.int32)
    weight = jnp.sum(jnp.where(hits, gate_rows[:, :, None], 0.0), 1)
    place = jnp.cumsum(member, 0, dtype=jnp.int32) - 1
    slots = jnp.arange(capacity, dtype=jnp.int32)
    table = (member.T[:, None, :] == 1) & (place.T[:, None, :] == slots[None, :, None])
    gate_slot = jnp.sum(jnp.where(table, weight.T[:, None, :], 0.0), 2)
    return (table.astype(jnp.bfloat16), gate_slot)


def flash_attend(query, keys, values, key_new, value_new, length, first_token, tokens):
    kv_heads, rows, head_dim = query.shape
    block = key_new.shape[2]
    blocks = keys.shape[2] // block

    def cached_blocks(length_ref):
        return (length_ref[0] + block - 1) // block

    def kernel(length_ref, q_ref, kc_ref, vc_ref, kn_ref, vn_ref, o_ref, m_sc, l_sc, acc_sc):
        step = pl.program_id(1)
        length = length_ref[0]

        def visit(key_block, value_block, visible, first):
            scores = jnp.dot(q_ref[0], key_block, preferred_element_type=jnp.float32)
            if visible is not None:
                scores = jnp.where(visible, scores, -1e30)
            if first:
                highest = jnp.max(scores, -1, keepdims=True)
            else:
                previous = m_sc[...]
                highest = jnp.maximum(previous, jnp.max(scores, -1, keepdims=True))
            probs = jnp.exp(scores - highest)
            if visible is not None:
                probs = jnp.where(visible, probs, 0.0)
            summed = lax.dot_general(
                probs.astype(jnp.bfloat16),
                value_block,
                (((1,), (1,)), ((), ())),
                preferred_element_type=jnp.float32,
            )
            if first:
                l_sc[...] = jnp.sum(probs, -1, keepdims=True)
                acc_sc[...] = summed
            else:
                correction = jnp.exp(previous - highest)
                l_sc[...] = l_sc[...] * correction + jnp.sum(probs, -1, keepdims=True)
                acc_sc[...] = acc_sc[...] * correction + summed
            m_sc[...] = highest

        shape = (rows, block)
        column = lax.broadcasted_iota(jnp.int32, shape, 1)

        @pl.when(step == 0)
        def _():
            token = first_token + lax.rem(lax.broadcasted_iota(jnp.int32, shape, 0), tokens)
            visit(kn_ref[0], vn_ref[0], column <= token, True)

        start = (step - 1) * block

        whole = (step > 0) & (start + block <= length)

        @pl.when(whole)
        def _():
            visit(kc_ref[0], vc_ref[0], None, False)

        @pl.when((step > 0) & jnp.logical_not(whole) & (start < length))
        def _():
            visit(kc_ref[0], vc_ref[0], column + start < length, False)

        @pl.when(step == blocks - 1)
        def _():
            o_ref[0] = (acc_sc[...] / l_sc[...]).astype(o_ref.dtype)

    def cache_map(head, step, length_ref):
        return (head, 0, jnp.clip(step - 1, 0, cached_blocks(length_ref) - 1))

    def fixed_map(head, step, length_ref):
        return (head, 0, 0)

    grid_spec = pltpu.PrefetchScalarGridSpec(
        num_scalar_prefetch=1,
        grid=(kv_heads, blocks),
        in_specs=[
            pl.BlockSpec((1, rows, head_dim), fixed_map),
            pl.BlockSpec((1, head_dim, block), cache_map),
            pl.BlockSpec((1, head_dim, block), cache_map),
            pl.BlockSpec((1, head_dim, block), fixed_map),
            pl.BlockSpec((1, head_dim, block), fixed_map),
        ],
        out_specs=pl.BlockSpec((1, rows, head_dim), fixed_map),
        scratch_shapes=[
            pltpu.VMEM((rows, 1), jnp.float32),
            pltpu.VMEM((rows, 1), jnp.float32),
            pltpu.VMEM((rows, head_dim), jnp.float32),
        ],
    )
    flops = 4 * kv_heads * rows * keys.shape[2] * head_dim
    return pl.pallas_call(
        kernel,
        grid_spec=grid_spec,
        out_shape=jax.ShapeDtypeStruct(query.shape, jnp.bfloat16),
        compiler_params=pltpu.CompilerParams(dimension_semantics=("arbitrary", "arbitrary")),
        cost_estimate=pl.CostEstimate(
            flops=flops,
            transcendentals=kv_heads * rows * keys.shape[2],
            bytes_accessed=2 * (query.size + keys.size + values.size + query.size),
        ),
    )(length.reshape(1), query, keys, values, key_new, value_new)


def shifted(values, shift):
    devices = lax.axis_size("ep")
    return lax.ppermute(values, "ep", [(i, (i + shift) % devices) for i in range(devices)])


def gather_columns(values):
    devices = lax.axis_size("ep")
    me = lax.axis_index("ep")
    width = values.shape[-1]
    whole = jnp.zeros(values.shape[:-1] + (width * devices,), values.dtype)
    for shift in range(devices):
        piece = values if shift == 0 else shifted(values, shift)
        source = (me - shift) % devices
        whole = lax.dynamic_update_slice_in_dim(whole, piece, source * width, values.ndim - 1)
    return whole


def sum_over_ep(part):
    devices = lax.axis_size("ep")
    total = part.astype(jnp.float32)
    for shift in range(1, devices):
        total = total + shifted(part, shift).astype(jnp.float32)
    return total


def on_device(
    hidden,
    key_cache,
    value_cache,
    request_order,
    cached_lengths,
    expert_ids,
    gate_values,
    attn_gain,
    ffn_gain,
    w_query,
    w_key,
    w_value,
    w_out,
    expert_gate,
    expert_up,
    expert_down,
):
    own_rows = hidden[0]
    new_rows = own_rows.shape[0]
    own_width = own_rows.shape[1]
    head_dim = key_cache.shape[3]
    kv_local = key_cache.shape[1]
    heads_local = w_query.shape[1] // head_dim
    group = heads_local // kv_local
    per_device = expert_gate.shape[0]
    capacity = 3 * new_rows // 8
    me = lax.axis_index("ep")
    gate_up = lax.all_gather(jnp.stack([expert_gate, expert_up]), "req", axis=2, tiled=True)
    gate_whole = gate_up[0]
    up_whole = gate_up[1]
    down_whole = lax.all_gather(expert_down, "req", axis=1, tiled=True)
    everyone = jnp.arange(request_order.shape[0], dtype=jnp.int32)
    request = jnp.sum(jnp.where(everyone == lax.axis_index("req"), request_order, 0))
    length = jnp.sum(jnp.where(everyone == request, cached_lengths, 0))
    rows_whole = gather_columns(own_rows)
    rows_f = rows_whole.astype(jnp.float32)
    normed = normalize(rows_f, attn_gain).astype(jnp.bfloat16)
    query = jnp.dot(normed, w_query, preferred_element_type=jnp.float32)
    key_new = jnp.dot(normed, w_key, preferred_element_type=jnp.float32)
    value_new = jnp.dot(normed, w_value, preferred_element_type=jnp.float32)
    positions = length + jnp.arange(new_rows, dtype=jnp.int32)
    query = rotate(
        query.reshape(new_rows, heads_local, head_dim).transpose(1, 0, 2), positions
    ).astype(jnp.bfloat16) * jnp.asarray(head_dim ** (-0.5), jnp.bfloat16)
    key_new = rotate(
        key_new.reshape(new_rows, kv_local, head_dim).transpose(1, 0, 2), positions
    ).astype(jnp.bfloat16)
    value_new = (
        value_new.reshape(new_rows, kv_local, head_dim).transpose(1, 0, 2).astype(jnp.bfloat16)
    )
    zero = jnp.zeros((), jnp.int32)
    keys = lax.dynamic_update_slice(key_cache[0], key_new, (zero, length, zero))
    values = lax.dynamic_update_slice(value_cache[0], value_new, (zero, length, zero))
    half = new_rows // 2
    query = query.reshape(kv_local, group, new_rows, head_dim)
    key_cache_t = jnp.swapaxes(key_cache[0], 1, 2)
    value_cache_t = jnp.swapaxes(value_cache[0], 1, 2)
    key_new_t = jnp.swapaxes(key_new, 1, 2)
    value_new_t = jnp.swapaxes(value_new, 1, 2)
    head_sums = []
    for first in (0, half):
        part_query = query[:, :, first : first + half].reshape(kv_local, group * half, head_dim)
        attended = flash_attend(
            part_query,
            key_cache_t,
            value_cache_t,
            key_new_t,
            value_new_t,
            length,
            first,
            half,
        )
        attended = (
            attended.reshape(heads_local, half, head_dim)
            .transpose(1, 0, 2)
            .reshape(half, heads_local * head_dim)
        )
        head_part = jnp.dot(attended, w_out, preferred_element_type=jnp.float32).astype(
            jnp.bfloat16
        )
        head_sums.append(sum_over_ep(head_part))
    head_sum = jnp.concatenate(head_sums, 0)
    mixed_f = (rows_f + head_sum).astype(jnp.bfloat16).astype(jnp.float32)
    ffn_normed = normalize(mixed_f, ffn_gain).astype(jnp.bfloat16)
    table, gate_slot = route_tables(
        expert_ids[0],
        gate_values[0],
        me * per_device + jnp.arange(per_device, dtype=jnp.int32),
        capacity,
    )
    dispatched = jnp.einsum(
        "ect,td->ecd", table, ffn_normed, preferred_element_type=jnp.float32
    ).astype(jnp.bfloat16)
    gate_whole, up_whole, dispatched = lax.optimization_barrier((gate_whole, up_whole, dispatched))
    gate_act = jnp.einsum("ecd,edf->ecf", dispatched, gate_whole, preferred_element_type=jnp.float32)
    up_act = jnp.einsum("ecd,edf->ecf", dispatched, up_whole, preferred_element_type=jnp.float32)
    act = (jax.nn.silu(gate_act) * up_act).astype(jnp.bfloat16)
    down_whole, act = lax.optimization_barrier((down_whole, act))
    devices = lax.axis_size("ep")

    def expert_block(target):
        down_block = lax.dynamic_slice_in_dim(down_whole, target * own_width, own_width, 2)
        output = jnp.einsum("ecf,efd->ecd", act, down_block, preferred_element_type=jnp.float32)
        contrib = (output * gate_slot[..., None]).astype(jnp.bfloat16)
        return jnp.einsum(
            "ect,ecd->td", table, contrib, preferred_element_type=jnp.float32
        ).astype(jnp.bfloat16)

    received = [shifted(expert_block((me + shift) % devices), shift) for shift in range(1, devices)]
    expert_sum = expert_block(me).astype(jnp.float32)
    for piece in received:
        expert_sum = expert_sum + piece.astype(jnp.float32)
    mixed_own = lax.dynamic_slice_in_dim(mixed_f, me * own_width, own_width, 1)
    result = (mixed_own + expert_sum).astype(jnp.bfloat16)
    return (result[None], keys[None], values[None])


def solution(mesh):
    in_specs = (
        P("req", None, "ep"),
        P("req", "ep", None, None),
        P("req", "ep", None, None),
        P(),
        P(),
        P("req", None, None),
        P("req", None, None),
        P(),
        P(),
        P(None, "ep"),
        P(None, "ep"),
        P(None, "ep"),
        P("ep", None),
        P("ep", "req", None),
        P("ep", "req", None),
        P("ep", "req", None),
    )
    out_specs = (P("req", None, "ep"), P("req", "ep", None, None), P("req", "ep", None, None))
    return jax.shard_map(
        on_device, mesh=mesh, in_specs=in_specs, out_specs=out_specs, check_vma=False
    )
```

```python
import jax
import jax.numpy as jnp
from jax import lax
from jax.experimental import pallas as pl
from jax.experimental.pallas import tpu as pltpu
from jax.sharding import PartitionSpec as P

epsilon = 1e-06


def normalize(values, gain):
    return values * lax.rsqrt(jnp.mean(values * values, -1, keepdims=True) + epsilon) * gain


def rotate(values, positions):
    half = values.shape[-1] // 2
    freq = 10000.0 ** (-jnp.arange(half, dtype=jnp.float32) * (2.0 / values.shape[-1]))
    angle = positions.astype(jnp.float32)[:, None] * freq[None, :]
    cosine = jnp.cos(angle)
    sine = jnp.sin(angle)
    first = values[..., :half]
    second = values[..., half:]
    return jnp.concatenate([first * cosine - second * sine, second * cosine + first * sine], -1)


def rounded(values):
    return lax.optimization_barrier(values.astype(jnp.bfloat16)).astype(jnp.float32)


def route_tables(chosen, gate_rows, wanted, capacity):
    hits = chosen[:, :, None] == wanted[None, None, :]
    member = jnp.sum(hits.astype(jnp.int32), 1, dtype=jnp.int32)
    weight = jnp.sum(jnp.where(hits, gate_rows[:, :, None], 0.0), 1)
    place = jnp.cumsum(member, 0, dtype=jnp.int32) - 1
    slots = jnp.arange(capacity, dtype=jnp.int32)
    table = (member.T[:, None, :] == 1) & (place.T[:, None, :] == slots[None, :, None])
    gate_slot = jnp.sum(jnp.where(table, weight.T[:, None, :], 0.0), 2)
    return (table.astype(jnp.bfloat16), gate_slot)


def flash_attend(query, keys, values, key_new, value_new, length, first_token, tokens):
    kv_heads, rows, head_dim = query.shape
    block = key_new.shape[2]
    blocks = keys.shape[2] // block

    def cached_blocks(length_ref):
        return (length_ref[0] + block - 1) // block

    def kernel(length_ref, q_ref, kc_ref, vc_ref, kn_ref, vn_ref, o_ref, m_sc, l_sc, acc_sc):
        step = pl.program_id(1)
        length = length_ref[0]

        def visit(key_block, value_block, visible, first):
            scores = jnp.dot(q_ref[0], key_block, preferred_element_type=jnp.float32)
            if visible is not None:
                scores = jnp.where(visible, scores, -1e30)
            if first:
                highest = jnp.max(scores, -1, keepdims=True)
            else:
                previous = m_sc[...]
                highest = jnp.maximum(previous, jnp.max(scores, -1, keepdims=True))
            probs = jnp.exp(scores - highest)
            if visible is not None:
                probs = jnp.where(visible, probs, 0.0)
            summed = lax.dot_general(
                probs.astype(jnp.bfloat16),
                value_block,
                (((1,), (1,)), ((), ())),
                preferred_element_type=jnp.float32,
            )
            if first:
                l_sc[...] = jnp.sum(probs, -1, keepdims=True)
                acc_sc[...] = summed
            else:
                correction = jnp.exp(previous - highest)
                l_sc[...] = l_sc[...] * correction + jnp.sum(probs, -1, keepdims=True)
                acc_sc[...] = acc_sc[...] * correction + summed
            m_sc[...] = highest

        shape = (rows, block)
        column = lax.broadcasted_iota(jnp.int32, shape, 1)

        @pl.when(step == 0)
        def _():
            token = first_token + lax.rem(lax.broadcasted_iota(jnp.int32, shape, 0), tokens)
            visit(kn_ref[0], vn_ref[0], column <= token, True)

        start = (step - 1) * block

        whole = (step > 0) & (start + block <= length)

        @pl.when(whole)
        def _():
            visit(kc_ref[0], vc_ref[0], None, False)

        @pl.when((step > 0) & jnp.logical_not(whole) & (start < length))
        def _():
            visit(kc_ref[0], vc_ref[0], column + start < length, False)

        @pl.when(step == blocks - 1)
        def _():
            o_ref[0] = (acc_sc[...] / l_sc[...]).astype(o_ref.dtype)

    def cache_map(head, step, length_ref):
        return (head, 0, jnp.clip(step - 1, 0, cached_blocks(length_ref) - 1))

    def fixed_map(head, step, length_ref):
        return (head, 0, 0)

    grid_spec = pltpu.PrefetchScalarGridSpec(
        num_scalar_prefetch=1,
        grid=(kv_heads, blocks),
        in_specs=[
            pl.BlockSpec((1, rows, head_dim), fixed_map),
            pl.BlockSpec((1, head_dim, block), cache_map),
            pl.BlockSpec((1, head_dim, block), cache_map),
            pl.BlockSpec((1, head_dim, block), fixed_map),
            pl.BlockSpec((1, head_dim, block), fixed_map),
        ],
        out_specs=pl.BlockSpec((1, rows, head_dim), fixed_map),
        scratch_shapes=[
            pltpu.VMEM((rows, 1), jnp.float32),
            pltpu.VMEM((rows, 1), jnp.float32),
            pltpu.VMEM((rows, head_dim), jnp.float32),
        ],
    )
    flops = 4 * kv_heads * rows * keys.shape[2] * head_dim
    return pl.pallas_call(
        kernel,
        grid_spec=grid_spec,
        out_shape=jax.ShapeDtypeStruct(query.shape, jnp.bfloat16),
        compiler_params=pltpu.CompilerParams(dimension_semantics=("arbitrary", "arbitrary")),
        cost_estimate=pl.CostEstimate(
            flops=flops,
            transcendentals=kv_heads * rows * keys.shape[2],
            bytes_accessed=2 * (query.size + keys.size + values.size + query.size),
        ),
    )(length.reshape(1), query, keys, values, key_new, value_new)


def shifted(values, shift):
    devices = lax.axis_size("ep")
    return lax.ppermute(values, "ep", [(i, (i + shift) % devices) for i in range(devices)])


def gather_columns(values):
    devices = lax.axis_size("ep")
    me = lax.axis_index("ep")
    width = values.shape[-1]
    whole = jnp.zeros(values.shape[:-1] + (width * devices,), values.dtype)
    for shift in range(devices):
        piece = values if shift == 0 else shifted(values, shift)
        source = (me - shift) % devices
        whole = lax.dynamic_update_slice_in_dim(whole, piece, source * width, values.ndim - 1)
    return whole


def sum_over_ep(part):
    devices = lax.axis_size("ep")
    total = part.astype(jnp.float32)
    for shift in range(1, devices):
        total = total + shifted(part, shift).astype(jnp.float32)
    return total


def on_device(
    hidden,
    key_cache,
    value_cache,
    request_order,
    cached_lengths,
    expert_ids,
    gate_values,
    attn_gain,
    ffn_gain,
    w_query,
    w_key,
    w_value,
    w_out,
    expert_gate,
    expert_up,
    expert_down,
):
    own_rows = hidden[0]
    new_rows = own_rows.shape[0]
    own_width = own_rows.shape[1]
    head_dim = key_cache.shape[3]
    kv_local = key_cache.shape[1]
    heads_local = w_query.shape[1] // head_dim
    group = heads_local // kv_local
    per_device = expert_gate.shape[0]
    capacity = 3 * new_rows // 8
    me = lax.axis_index("ep")
    gate_up = lax.all_gather(jnp.stack([expert_gate, expert_up]), "req", axis=2, tiled=True)
    down_whole = lax.all_gather(expert_down, "req", axis=1, tiled=True)
    everyone = jnp.arange(request_order.shape[0], dtype=jnp.int32)
    request = jnp.sum(jnp.where(everyone == lax.axis_index("req"), request_order, 0))
    length = jnp.sum(jnp.where(everyone == request, cached_lengths, 0))
    rows_whole = gather_columns(own_rows)
    rows_f = rows_whole.astype(jnp.float32)
    normed = normalize(rows_f, attn_gain).astype(jnp.bfloat16)
    query = jnp.dot(normed, w_query, preferred_element_type=jnp.float32)
    key_new = jnp.dot(normed, w_key, preferred_element_type=jnp.float32)
    value_new = jnp.dot(normed, w_value, preferred_element_type=jnp.float32)
    positions = length + jnp.arange(new_rows, dtype=jnp.int32)
    query = rotate(
        query.reshape(new_rows, heads_local, head_dim).transpose(1, 0, 2), positions
    ).astype(jnp.bfloat16) * jnp.asarray(head_dim ** (-0.5), jnp.bfloat16)
    key_new = rotate(
        key_new.reshape(new_rows, kv_local, head_dim).transpose(1, 0, 2), positions
    ).astype(jnp.bfloat16)
    value_new = (
        value_new.reshape(new_rows, kv_local, head_dim).transpose(1, 0, 2).astype(jnp.bfloat16)
    )
    zero = jnp.zeros((), jnp.int32)
    keys = lax.dynamic_update_slice(key_cache[0], key_new, (zero, length, zero))
    values = lax.dynamic_update_slice(value_cache[0], value_new, (zero, length, zero))
    half = new_rows // 2
    query = query.reshape(kv_local, group, new_rows, head_dim)
    key_cache_t = jnp.swapaxes(key_cache[0], 1, 2)
    value_cache_t = jnp.swapaxes(value_cache[0], 1, 2)
    key_new_t = jnp.swapaxes(key_new, 1, 2)
    value_new_t = jnp.swapaxes(value_new, 1, 2)
    head_sums = []
    for first in (0, half):
        part_query = query[:, :, first : first + half].reshape(kv_local, group * half, head_dim)
        attended = flash_attend(
            part_query,
            key_cache_t,
            value_cache_t,
            key_new_t,
            value_new_t,
            length,
            first,
            half,
        )
        attended = (
            attended.reshape(heads_local, half, head_dim)
            .transpose(1, 0, 2)
            .reshape(half, heads_local * head_dim)
        )
        head_part = jnp.dot(attended, w_out, preferred_element_type=jnp.float32).astype(
            jnp.bfloat16
        )
        head_sums.append(sum_over_ep(head_part))
    head_sum = jnp.concatenate(head_sums, 0)
    mixed_f = (rows_f + head_sum).astype(jnp.bfloat16).astype(jnp.float32)
    ffn_normed = normalize(mixed_f, ffn_gain).astype(jnp.bfloat16)
    table, gate_slot = route_tables(
        expert_ids[0],
        gate_values[0],
        me * per_device + jnp.arange(per_device, dtype=jnp.int32),
        capacity,
    )
    dispatched = jnp.einsum(
        "ect,td->ecd", table, ffn_normed, preferred_element_type=jnp.float32
    ).astype(jnp.bfloat16)
    gate_up, dispatched = lax.optimization_barrier((gate_up, dispatched))
    both = jnp.einsum("ecd,kedf->kecf", dispatched, gate_up, preferred_element_type=jnp.float32)
    act = (jax.nn.silu(both[0]) * both[1]).astype(jnp.bfloat16)
    down_whole, act = lax.optimization_barrier((down_whole, act))
    devices = lax.axis_size("ep")

    def expert_block(target):
        down_block = lax.dynamic_slice_in_dim(down_whole, target * own_width, own_width, 2)
        output = jnp.einsum("ecf,efd->ecd", act, down_block, preferred_element_type=jnp.float32)
        contrib = (output * gate_slot[..., None]).astype(jnp.bfloat16)
        return jnp.einsum(
            "ect,ecd->td", table, contrib, preferred_element_type=jnp.float32
        ).astype(jnp.bfloat16)

    received = [shifted(expert_block((me + shift) % devices), shift) for shift in range(1, devices)]
    expert_sum = expert_block(me).astype(jnp.float32)
    for piece in received:
        expert_sum = expert_sum + piece.astype(jnp.float32)
    mixed_own = lax.dynamic_slice_in_dim(mixed_f, me * own_width, own_width, 1)
    result = (mixed_own + expert_sum).astype(jnp.bfloat16)
    return (result[None], keys[None], values[None])


def solution(mesh):
    in_specs = (
        P("req", None, "ep"),
        P("req", "ep", None, None),
        P("req", "ep", None, None),
        P(),
        P(),
        P("req", None, None),
        P("req", None, None),
        P(),
        P(),
        P(None, "ep"),
        P(None, "ep"),
        P(None, "ep"),
        P("ep", None),
        P("ep", "req", None),
        P("ep", "req", None),
        P("ep", "req", None),
    )
    out_specs = (P("req", None, "ep"), P("req", "ep", None, None), P("req", "ep", None, None))
    return jax.shard_map(
        on_device, mesh=mesh, in_specs=in_specs, out_specs=out_specs, check_vma=False
    )
```

```python
import jax
import jax.numpy as jnp
from jax import lax
from jax.experimental import pallas as pl
from jax.experimental.pallas import tpu as pltpu
from jax.sharding import PartitionSpec as P

epsilon = 1e-06


def normalize(values, gain):
    return values * lax.rsqrt(jnp.mean(values * values, -1, keepdims=True) + epsilon) * gain


def rotate(values, positions):
    half = values.shape[-1] // 2
    freq = 10000.0 ** (-jnp.arange(half, dtype=jnp.float32) * (2.0 / values.shape[-1]))
    angle = positions.astype(jnp.float32)[:, None] * freq[None, :]
    cosine = jnp.cos(angle)
    sine = jnp.sin(angle)
    first = values[..., :half]
    second = values[..., half:]
    return jnp.concatenate([first * cosine - second * sine, second * cosine + first * sine], -1)


def rounded(values):
    return lax.optimization_barrier(values.astype(jnp.bfloat16)).astype(jnp.float32)


def route_tables(chosen, gate_rows, wanted, capacity):
    hits = chosen[:, :, None] == wanted[None, None, :]
    member = jnp.sum(hits.astype(jnp.int32), 1, dtype=jnp.int32)
    weight = jnp.sum(jnp.where(hits, gate_rows[:, :, None], 0.0), 1)
    place = jnp.cumsum(member, 0, dtype=jnp.int32) - 1
    slots = jnp.arange(capacity, dtype=jnp.int32)
    table = (member.T[:, None, :] == 1) & (place.T[:, None, :] == slots[None, :, None])
    gate_slot = jnp.sum(jnp.where(table, weight.T[:, None, :], 0.0), 2)
    return (table.astype(jnp.bfloat16), gate_slot)


def flash_attend(query, keys, values, key_new, value_new, length, first_token, tokens):
    kv_heads, rows, head_dim = query.shape
    block = key_new.shape[2]
    blocks = keys.shape[2] // block

    def cached_blocks(length_ref):
        return (length_ref[0] + block - 1) // block

    def kernel(length_ref, q_ref, kc_ref, vc_ref, kn_ref, vn_ref, o_ref, m_sc, l_sc, acc_sc):
        step = pl.program_id(0)
        length = length_ref[0]

        def visit(key_ref, value_ref, visible, first):
            for head in range(kv_heads):
                scores = jnp.dot(q_ref[head], key_ref[head], preferred_element_type=jnp.float32)
                if visible is not None:
                    scores = jnp.where(visible, scores, -1e30)
                if first:
                    highest = jnp.max(scores, -1, keepdims=True)
                else:
                    previous = m_sc[head]
                    highest = jnp.maximum(previous, jnp.max(scores, -1, keepdims=True))
                probs = jnp.exp(scores - highest)
                if visible is not None:
                    probs = jnp.where(visible, probs, 0.0)
                summed = lax.dot_general(
                    probs.astype(jnp.bfloat16),
                    value_ref[head],
                    (((1,), (1,)), ((), ())),
                    preferred_element_type=jnp.float32,
                )
                if first:
                    l_sc[head] = jnp.sum(probs, -1, keepdims=True)
                    acc_sc[head] = summed
                else:
                    correction = jnp.exp(previous - highest)
                    l_sc[head] = l_sc[head] * correction + jnp.sum(probs, -1, keepdims=True)
                    acc_sc[head] = acc_sc[head] * correction + summed
                m_sc[head] = highest

        shape = (rows, block)
        column = lax.broadcasted_iota(jnp.int32, shape, 1)

        @pl.when(step == 0)
        def _():
            token = first_token + lax.rem(lax.broadcasted_iota(jnp.int32, shape, 0), tokens)
            visit(kn_ref, vn_ref, column <= token, True)

        start = (step - 1) * block

        whole = (step > 0) & (start + block <= length)

        @pl.when(whole)
        def _():
            visit(kc_ref, vc_ref, None, False)

        @pl.when((step > 0) & jnp.logical_not(whole) & (start < length))
        def _():
            visit(kc_ref, vc_ref, column + start < length, False)

        @pl.when(step == blocks - 1)
        def _():
            for head in range(kv_heads):
                o_ref[head] = (acc_sc[head] / l_sc[head]).astype(o_ref.dtype)

    def cache_map(step, length_ref):
        return (0, 0, jnp.clip(step - 1, 0, cached_blocks(length_ref) - 1))

    def fixed_map(step, length_ref):
        return (0, 0, 0)

    grid_spec = pltpu.PrefetchScalarGridSpec(
        num_scalar_prefetch=1,
        grid=(blocks,),
        in_specs=[
            pl.BlockSpec((kv_heads, rows, head_dim), fixed_map),
            pl.BlockSpec((kv_heads, head_dim, block), cache_map),
            pl.BlockSpec((kv_heads, head_dim, block), cache_map),
            pl.BlockSpec((kv_heads, head_dim, block), fixed_map),
            pl.BlockSpec((kv_heads, head_dim, block), fixed_map),
        ],
        out_specs=pl.BlockSpec((kv_heads, rows, head_dim), fixed_map),
        scratch_shapes=[
            pltpu.VMEM((kv_heads, rows, 1), jnp.float32),
            pltpu.VMEM((kv_heads, rows, 1), jnp.float32),
            pltpu.VMEM((kv_heads, rows, head_dim), jnp.float32),
        ],
    )
    flops = 4 * kv_heads * rows * keys.shape[2] * head_dim
    return pl.pallas_call(
        kernel,
        grid_spec=grid_spec,
        out_shape=jax.ShapeDtypeStruct(query.shape, jnp.bfloat16),
        compiler_params=pltpu.CompilerParams(dimension_semantics=("arbitrary",)),
        cost_estimate=pl.CostEstimate(
            flops=flops,
            transcendentals=kv_heads * rows * keys.shape[2],
            bytes_accessed=2 * (query.size + keys.size + values.size + query.size),
        ),
    )(length.reshape(1), query, keys, values, key_new, value_new)


def shifted(values, shift):
    devices = lax.axis_size("ep")
    return lax.ppermute(values, "ep", [(i, (i + shift) % devices) for i in range(devices)])


def gather_columns(values):
    devices = lax.axis_size("ep")
    me = lax.axis_index("ep")
    width = values.shape[-1]
    whole = jnp.zeros(values.shape[:-1] + (width * devices,), values.dtype)
    for shift in range(devices):
        piece = values if shift == 0 else shifted(values, shift)
        source = (me - shift) % devices
        whole = lax.dynamic_update_slice_in_dim(whole, piece, source * width, values.ndim - 1)
    return whole


def sum_over_ep(part):
    devices = lax.axis_size("ep")
    total = part.astype(jnp.float32)
    for shift in range(1, devices):
        total = total + shifted(part, shift).astype(jnp.float32)
    return total


def on_device(
    hidden,
    key_cache,
    value_cache,
    request_order,
    cached_lengths,
    expert_ids,
    gate_values,
    attn_gain,
    ffn_gain,
    w_query,
    w_key,
    w_value,
    w_out,
    expert_gate,
    expert_up,
    expert_down,
):
    own_rows = hidden[0]
    new_rows = own_rows.shape[0]
    own_width = own_rows.shape[1]
    head_dim = key_cache.shape[3]
    kv_local = key_cache.shape[1]
    heads_local = w_query.shape[1] // head_dim
    group = heads_local // kv_local
    per_device = expert_gate.shape[0]
    capacity = 3 * new_rows // 8
    me = lax.axis_index("ep")
    gate_up = lax.all_gather(jnp.stack([expert_gate, expert_up]), "req", axis=2, tiled=True)
    down_whole = lax.all_gather(expert_down, "req", axis=1, tiled=True)
    everyone = jnp.arange(request_order.shape[0], dtype=jnp.int32)
    request = jnp.sum(jnp.where(everyone == lax.axis_index("req"), request_order, 0))
    length = jnp.sum(jnp.where(everyone == request, cached_lengths, 0))
    rows_whole = gather_columns(own_rows)
    rows_f = rows_whole.astype(jnp.float32)
    normed = normalize(rows_f, attn_gain).astype(jnp.bfloat16)
    query = jnp.dot(normed, w_query, preferred_element_type=jnp.float32)
    key_new = jnp.dot(normed, w_key, preferred_element_type=jnp.float32)
    value_new = jnp.dot(normed, w_value, preferred_element_type=jnp.float32)
    positions = length + jnp.arange(new_rows, dtype=jnp.int32)
    query = rotate(
        query.reshape(new_rows, heads_local, head_dim).transpose(1, 0, 2), positions
    ).astype(jnp.bfloat16) * jnp.asarray(head_dim ** (-0.5), jnp.bfloat16)
    key_new = rotate(
        key_new.reshape(new_rows, kv_local, head_dim).transpose(1, 0, 2), positions
    ).astype(jnp.bfloat16)
    value_new = (
        value_new.reshape(new_rows, kv_local, head_dim).transpose(1, 0, 2).astype(jnp.bfloat16)
    )
    zero = jnp.zeros((), jnp.int32)
    keys = lax.dynamic_update_slice(key_cache[0], key_new, (zero, length, zero))
    values = lax.dynamic_update_slice(value_cache[0], value_new, (zero, length, zero))
    half = new_rows // 2
    query = query.reshape(kv_local, group, new_rows, head_dim)
    key_cache_t = jnp.swapaxes(key_cache[0], 1, 2)
    value_cache_t = jnp.swapaxes(value_cache[0], 1, 2)
    key_new_t = jnp.swapaxes(key_new, 1, 2)
    value_new_t = jnp.swapaxes(value_new, 1, 2)
    head_sums = []
    for first in (0, half):
        part_query = query[:, :, first : first + half].reshape(kv_local, group * half, head_dim)
        attended = flash_attend(
            part_query,
            key_cache_t,
            value_cache_t,
            key_new_t,
            value_new_t,
            length,
            first,
            half,
        )
        attended = (
            attended.reshape(heads_local, half, head_dim)
            .transpose(1, 0, 2)
            .reshape(half, heads_local * head_dim)
        )
        head_part = jnp.dot(attended, w_out, preferred_element_type=jnp.float32).astype(
            jnp.bfloat16
        )
        head_sums.append(sum_over_ep(head_part))
    head_sum = jnp.concatenate(head_sums, 0)
    mixed_f = (rows_f + head_sum).astype(jnp.bfloat16).astype(jnp.float32)
    ffn_normed = normalize(mixed_f, ffn_gain).astype(jnp.bfloat16)
    table, gate_slot = route_tables(
        expert_ids[0],
        gate_values[0],
        me * per_device + jnp.arange(per_device, dtype=jnp.int32),
        capacity,
    )
    dispatched = jnp.einsum(
        "ect,td->ecd", table, ffn_normed, preferred_element_type=jnp.float32
    ).astype(jnp.bfloat16)
    gate_up, dispatched = lax.optimization_barrier((gate_up, dispatched))
    both = jnp.einsum("ecd,kedf->kecf", dispatched, gate_up, preferred_element_type=jnp.float32)
    act = (jax.nn.silu(both[0]) * both[1]).astype(jnp.bfloat16)
    down_whole, act = lax.optimization_barrier((down_whole, act))
    devices = lax.axis_size("ep")

    def expert_block(target):
        down_block = lax.dynamic_slice_in_dim(down_whole, target * own_width, own_width, 2)
        output = jnp.einsum("ecf,efd->ecd", act, down_block, preferred_element_type=jnp.float32)
        contrib = (output * gate_slot[..., None]).astype(jnp.bfloat16)
        return jnp.einsum(
            "ect,ecd->td", table, contrib, preferred_element_type=jnp.float32
        ).astype(jnp.bfloat16)

    received = [shifted(expert_block((me + shift) % devices), shift) for shift in range(1, devices)]
    expert_sum = expert_block(me).astype(jnp.float32)
    for piece in received:
        expert_sum = expert_sum + piece.astype(jnp.float32)
    mixed_own = lax.dynamic_slice_in_dim(mixed_f, me * own_width, own_width, 1)
    result = (mixed_own + expert_sum).astype(jnp.bfloat16)
    return (result[None], keys[None], values[None])


def solution(mesh):
    in_specs = (
        P("req", None, "ep"),
        P("req", "ep", None, None),
        P("req", "ep", None, None),
        P(),
        P(),
        P("req", None, None),
        P("req", None, None),
        P(),
        P(),
        P(None, "ep"),
        P(None, "ep"),
        P(None, "ep"),
        P("ep", None),
        P("ep", "req", None),
        P("ep", "req", None),
        P("ep", "req", None),
    )
    out_specs = (P("req", None, "ep"), P("req", "ep", None, None), P("req", "ep", None, None))
    return jax.shard_map(
        on_device, mesh=mesh, in_specs=in_specs, out_specs=out_specs, check_vma=False
    )
```

```python
import jax
import jax.numpy as jnp
from jax import lax
from jax.experimental import pallas as pl
from jax.experimental.pallas import tpu as pltpu
from jax.sharding import PartitionSpec as P

epsilon = 1e-06


def normalize(values, gain):
    return values * lax.rsqrt(jnp.mean(values * values, -1, keepdims=True) + epsilon) * gain


def rotate(values, positions):
    half = values.shape[-1] // 2
    freq = 10000.0 ** (-jnp.arange(half, dtype=jnp.float32) * (2.0 / values.shape[-1]))
    angle = positions.astype(jnp.float32)[:, None] * freq[None, :]
    cosine = jnp.cos(angle)
    sine = jnp.sin(angle)
    first = values[..., :half]
    second = values[..., half:]
    return jnp.concatenate([first * cosine - second * sine, second * cosine + first * sine], -1)


def rounded(values):
    return lax.optimization_barrier(values.astype(jnp.bfloat16)).astype(jnp.float32)


def route_tables(chosen, gate_rows, wanted, capacity):
    hits = chosen[:, :, None] == wanted[None, None, :]
    member = jnp.sum(hits.astype(jnp.int32), 1, dtype=jnp.int32)
    weight = jnp.sum(jnp.where(hits, gate_rows[:, :, None], 0.0), 1)
    place = jnp.cumsum(member, 0, dtype=jnp.int32) - 1
    slots = jnp.arange(capacity, dtype=jnp.int32)
    table = (member.T[:, None, :] == 1) & (place.T[:, None, :] == slots[None, :, None])
    gate_slot = jnp.sum(jnp.where(table, weight.T[:, None, :], 0.0), 2)
    return (table.astype(jnp.bfloat16), gate_slot)


def flash_attend(query, keys, values, key_new, value_new, length, first_token, tokens):
    kv_heads, rows, head_dim = query.shape
    block = key_new.shape[2]
    blocks = keys.shape[2] // block

    def cached_blocks(length_ref):
        return (length_ref[0] + block - 1) // block

    def kernel(length_ref, q_ref, kc_ref, vc_ref, kn_ref, vn_ref, o_ref, m_sc, l_sc, acc_sc):
        step = pl.program_id(1)
        length = length_ref[0]

        def visit(key_block, value_block, visible, first):
            scores = jnp.dot(q_ref[0], key_block, preferred_element_type=jnp.float32)
            if visible is not None:
                scores = jnp.where(visible, scores, -1e30)
            if first:
                highest = jnp.max(scores, -1, keepdims=True)
            else:
                previous = m_sc[...]
                highest = jnp.maximum(previous, jnp.max(scores, -1, keepdims=True))
            probs = jnp.exp(scores - highest)
            if visible is not None:
                probs = jnp.where(visible, probs, 0.0)
            summed = lax.dot_general(
                probs.astype(jnp.bfloat16),
                value_block,
                (((1,), (1,)), ((), ())),
                preferred_element_type=jnp.float32,
            )
            if first:
                l_sc[...] = jnp.sum(probs, -1, keepdims=True)
                acc_sc[...] = summed
            else:
                correction = jnp.exp(previous - highest)
                l_sc[...] = l_sc[...] * correction + jnp.sum(probs, -1, keepdims=True)
                acc_sc[...] = acc_sc[...] * correction + summed
            m_sc[...] = highest

        shape = (rows, block)
        column = lax.broadcasted_iota(jnp.int32, shape, 1)

        @pl.when(step == 0)
        def _():
            token = first_token + lax.rem(lax.broadcasted_iota(jnp.int32, shape, 0), tokens)
            visit(kn_ref[0], vn_ref[0], column <= token, True)

        start = (step - 1) * block

        whole = (step > 0) & (start + block <= length)

        @pl.when(whole)
        def _():
            visit(kc_ref[0], vc_ref[0], None, False)

        @pl.when((step > 0) & jnp.logical_not(whole) & (start < length))
        def _():
            visit(kc_ref[0], vc_ref[0], column + start < length, False)

        @pl.when(step == blocks - 1)
        def _():
            o_ref[0] = (acc_sc[...] / l_sc[...]).astype(o_ref.dtype)

    def cache_map(head, step, length_ref):
        return (head, 0, jnp.clip(step - 1, 0, cached_blocks(length_ref) - 1))

    def fixed_map(head, step, length_ref):
        return (head, 0, 0)

    grid_spec = pltpu.PrefetchScalarGridSpec(
        num_scalar_prefetch=1,
        grid=(kv_heads, blocks),
        in_specs=[
            pl.BlockSpec((1, rows, head_dim), fixed_map),
            pl.BlockSpec((1, head_dim, block), cache_map),
            pl.BlockSpec((1, head_dim, block), cache_map),
            pl.BlockSpec((1, head_dim, block), fixed_map),
            pl.BlockSpec((1, head_dim, block), fixed_map),
        ],
        out_specs=pl.BlockSpec((1, rows, head_dim), fixed_map),
        scratch_shapes=[
            pltpu.VMEM((rows, 1), jnp.float32),
            pltpu.VMEM((rows, 1), jnp.float32),
            pltpu.VMEM((rows, head_dim), jnp.float32),
        ],
    )
    flops = 4 * kv_heads * rows * keys.shape[2] * head_dim
    return pl.pallas_call(
        kernel,
        grid_spec=grid_spec,
        out_shape=jax.ShapeDtypeStruct(query.shape, jnp.bfloat16),
        compiler_params=pltpu.CompilerParams(dimension_semantics=("arbitrary", "arbitrary")),
        cost_estimate=pl.CostEstimate(
            flops=flops,
            transcendentals=kv_heads * rows * keys.shape[2],
            bytes_accessed=2 * (query.size + keys.size + values.size + query.size),
        ),
    )(length.reshape(1), query, keys, values, key_new, value_new)


def shifted(values, shift):
    devices = lax.axis_size("ep")
    return lax.ppermute(values, "ep", [(i, (i + shift) % devices) for i in range(devices)])


def gather_columns(values):
    devices = lax.axis_size("ep")
    me = lax.axis_index("ep")
    width = values.shape[-1]
    whole = jnp.zeros(values.shape[:-1] + (width * devices,), values.dtype)
    for shift in range(devices):
        piece = values if shift == 0 else shifted(values, shift)
        source = (me - shift) % devices
        whole = lax.dynamic_update_slice_in_dim(whole, piece, source * width, values.ndim - 1)
    return whole


def sum_over_ep(part):
    devices = lax.axis_size("ep")
    total = part.astype(jnp.float32)
    for shift in range(1, devices):
        total = total + shifted(part, shift).astype(jnp.float32)
    return total


def on_device(
    hidden,
    key_cache,
    value_cache,
    request_order,
    cached_lengths,
    expert_ids,
    gate_values,
    attn_gain,
    ffn_gain,
    w_query,
    w_key,
    w_value,
    w_out,
    expert_gate,
    expert_up,
    expert_down,
):
    own_rows = hidden[0]
    new_rows = own_rows.shape[0]
    own_width = own_rows.shape[1]
    head_dim = key_cache.shape[3]
    kv_local = key_cache.shape[1]
    heads_local = w_query.shape[1] // head_dim
    group = heads_local // kv_local
    per_device = expert_gate.shape[0]
    capacity = 3 * new_rows // 8
    me = lax.axis_index("ep")
    gate_up = lax.all_gather(jnp.stack([expert_gate, expert_up]), "req", axis=2, tiled=True)
    gate_whole = gate_up[0]
    up_whole = gate_up[1]
    down_whole = lax.all_gather(expert_down, "req", axis=1, tiled=True)
    everyone = jnp.arange(request_order.shape[0], dtype=jnp.int32)
    request = jnp.sum(jnp.where(everyone == lax.axis_index("req"), request_order, 0))
    length = jnp.sum(jnp.where(everyone == request, cached_lengths, 0))
    rows_whole = gather_columns(own_rows)
    rows_f = rows_whole.astype(jnp.float32)
    normed = normalize(rows_f, attn_gain).astype(jnp.bfloat16)
    query = jnp.dot(normed, w_query, preferred_element_type=jnp.float32)
    key_new = jnp.dot(normed, w_key, preferred_element_type=jnp.float32)
    value_new = jnp.dot(normed, w_value, preferred_element_type=jnp.float32)
    positions = length + jnp.arange(new_rows, dtype=jnp.int32)
    query = rotate(
        query.reshape(new_rows, heads_local, head_dim).transpose(1, 0, 2), positions
    ).astype(jnp.bfloat16) * jnp.asarray(head_dim ** (-0.5), jnp.bfloat16)
    key_new = rotate(
        key_new.reshape(new_rows, kv_local, head_dim).transpose(1, 0, 2), positions
    ).astype(jnp.bfloat16)
    value_new = (
        value_new.reshape(new_rows, kv_local, head_dim).transpose(1, 0, 2).astype(jnp.bfloat16)
    )
    zero = jnp.zeros((), jnp.int32)
    keys = lax.dynamic_update_slice(key_cache[0], key_new, (zero, length, zero))
    values = lax.dynamic_update_slice(value_cache[0], value_new, (zero, length, zero))
    half = new_rows // 2
    query = query.reshape(kv_local, group, new_rows, head_dim)
    key_cache_t = jnp.swapaxes(key_cache[0], 1, 2)
    value_cache_t = jnp.swapaxes(value_cache[0], 1, 2)
    key_new_t = jnp.swapaxes(key_new, 1, 2)
    value_new_t = jnp.swapaxes(value_new, 1, 2)
    head_sums = []
    for first in (0, half):
        part_query = query[:, :, first : first + half].reshape(kv_local, group * half, head_dim)
        attended = flash_attend(
            part_query,
            key_cache_t,
            value_cache_t,
            key_new_t,
            value_new_t,
            length,
            first,
            half,
        )
        attended = (
            attended.reshape(heads_local, half, head_dim)
            .transpose(1, 0, 2)
            .reshape(half, heads_local * head_dim)
        )
        head_part = jnp.dot(attended, w_out, preferred_element_type=jnp.float32).astype(
            jnp.bfloat16
        )
        head_sums.append(sum_over_ep(head_part))
    keys, values, head_sums[0] = lax.optimization_barrier((keys, values, head_sums[0]))
    head_sum = jnp.concatenate(head_sums, 0)
    mixed_f = (rows_f + head_sum).astype(jnp.bfloat16).astype(jnp.float32)
    ffn_normed = normalize(mixed_f, ffn_gain).astype(jnp.bfloat16)
    table, gate_slot = route_tables(
        expert_ids[0],
        gate_values[0],
        me * per_device + jnp.arange(per_device, dtype=jnp.int32),
        capacity,
    )
    dispatched = jnp.einsum(
        "ect,td->ecd", table, ffn_normed, preferred_element_type=jnp.float32
    ).astype(jnp.bfloat16)
    gate_whole, up_whole, dispatched = lax.optimization_barrier((gate_whole, up_whole, dispatched))
    gate_act = jnp.einsum("ecd,edf->ecf", dispatched, gate_whole, preferred_element_type=jnp.float32)
    up_act = jnp.einsum("ecd,edf->ecf", dispatched, up_whole, preferred_element_type=jnp.float32)
    act = (jax.nn.silu(gate_act) * up_act).astype(jnp.bfloat16)
    down_whole, act = lax.optimization_barrier((down_whole, act))
    devices = lax.axis_size("ep")

    def expert_block(target):
        down_block = lax.dynamic_slice_in_dim(down_whole, target * own_width, own_width, 2)
        output = jnp.einsum("ecf,efd->ecd", act, down_block, preferred_element_type=jnp.float32)
        contrib = (output * gate_slot[..., None]).astype(jnp.bfloat16)
        return jnp.einsum(
            "ect,ecd->td", table, contrib, preferred_element_type=jnp.float32
        ).astype(jnp.bfloat16)

    received = [shifted(expert_block((me + shift) % devices), shift) for shift in range(1, devices)]
    expert_sum = expert_block(me).astype(jnp.float32)
    for piece in received:
        expert_sum = expert_sum + piece.astype(jnp.float32)
    mixed_own = lax.dynamic_slice_in_dim(mixed_f, me * own_width, own_width, 1)
    result = (mixed_own + expert_sum).astype(jnp.bfloat16)
    return (result[None], keys[None], values[None])


def solution(mesh):
    in_specs = (
        P("req", None, "ep"),
        P("req", "ep", None, None),
        P("req", "ep", None, None),
        P(),
        P(),
        P("req", None, None),
        P("req", None, None),
        P(),
        P(),
        P(None, "ep"),
        P(None, "ep"),
        P(None, "ep"),
        P("ep", None),
        P("ep", "req", None),
        P("ep", "req", None),
        P("ep", "req", None),
    )
    out_specs = (P("req", None, "ep"), P("req", "ep", None, None), P("req", "ep", None, None))
    return jax.shard_map(
        on_device, mesh=mesh, in_specs=in_specs, out_specs=out_specs, check_vma=False
    )
```

```python
import jax
import jax.numpy as jnp
from jax import lax
from jax.experimental import pallas as pl
from jax.experimental.pallas import tpu as pltpu
from jax.sharding import PartitionSpec as P

epsilon = 1e-06


def normalize(values, gain):
    return values * lax.rsqrt(jnp.mean(values * values, -1, keepdims=True) + epsilon) * gain


def rotate(values, positions):
    half = values.shape[-1] // 2
    freq = 10000.0 ** (-jnp.arange(half, dtype=jnp.float32) * (2.0 / values.shape[-1]))
    angle = positions.astype(jnp.float32)[:, None] * freq[None, :]
    cosine = jnp.cos(angle)
    sine = jnp.sin(angle)
    first = values[..., :half]
    second = values[..., half:]
    return jnp.concatenate([first * cosine - second * sine, second * cosine + first * sine], -1)


def rounded(values):
    return lax.optimization_barrier(values.astype(jnp.bfloat16)).astype(jnp.float32)


def route_tables(chosen, gate_rows, wanted, capacity):
    hits = chosen[:, :, None] == wanted[None, None, :]
    member = jnp.sum(hits.astype(jnp.int32), 1, dtype=jnp.int32)
    weight = jnp.sum(jnp.where(hits, gate_rows[:, :, None], 0.0), 1)
    place = jnp.cumsum(member, 0, dtype=jnp.int32) - 1
    slots = jnp.arange(capacity, dtype=jnp.int32)
    table = (member.T[:, None, :] == 1) & (place.T[:, None, :] == slots[None, :, None])
    gate_slot = jnp.sum(jnp.where(table, weight.T[:, None, :], 0.0), 2)
    return (table.astype(jnp.bfloat16), gate_slot)


def flash_attend(query, keys, values, key_new, value_new, length, first_token, tokens):
    kv_heads, rows, head_dim = query.shape
    block = key_new.shape[2]
    blocks = keys.shape[2] // block

    def cached_blocks(length_ref):
        return (length_ref[0] + block - 1) // block

    def kernel(length_ref, q_ref, kc_ref, vc_ref, kn_ref, vn_ref, o_ref, m_sc, l_sc, acc_sc):
        step = pl.program_id(1)
        length = length_ref[0]

        def visit(key_block, value_block, visible, first):
            scores = jnp.dot(q_ref[0], key_block, preferred_element_type=jnp.float32)
            if visible is not None:
                scores = jnp.where(visible, scores, -1e30)
            if first:
                highest = jnp.max(scores, -1, keepdims=True)
            else:
                previous = m_sc[...]
                highest = jnp.maximum(previous, jnp.max(scores, -1, keepdims=True))
            probs = jnp.exp(scores - highest)
            if visible is not None:
                probs = jnp.where(visible, probs, 0.0)
            summed = lax.dot_general(
                probs.astype(jnp.bfloat16),
                value_block,
                (((1,), (1,)), ((), ())),
                preferred_element_type=jnp.float32,
            )
            if first:
                l_sc[...] = jnp.sum(probs, -1, keepdims=True)
                acc_sc[...] = summed
            else:
                correction = jnp.exp(previous - highest)
                l_sc[...] = l_sc[...] * correction + jnp.sum(probs, -1, keepdims=True)
                acc_sc[...] = acc_sc[...] * correction + summed
            m_sc[...] = highest

        shape = (rows, block)
        column = lax.broadcasted_iota(jnp.int32, shape, 1)

        @pl.when(step == 0)
        def _():
            token = first_token + lax.rem(lax.broadcasted_iota(jnp.int32, shape, 0), tokens)
            visit(kn_ref[0], vn_ref[0], column <= token, True)

        start = (step - 1) * block

        whole = (step > 0) & (start + block <= length)

        @pl.when(whole)
        def _():
            visit(kc_ref[0], vc_ref[0], None, False)

        @pl.when((step > 0) & jnp.logical_not(whole) & (start < length))
        def _():
            visit(kc_ref[0], vc_ref[0], column + start < length, False)

        @pl.when(step == blocks - 1)
        def _():
            o_ref[0] = (acc_sc[...] / l_sc[...]).astype(o_ref.dtype)

    def cache_map(head, step, length_ref):
        return (head, 0, jnp.clip(step - 1, 0, cached_blocks(length_ref) - 1))

    def fixed_map(head, step, length_ref):
        return (head, 0, 0)

    grid_spec = pltpu.PrefetchScalarGridSpec(
        num_scalar_prefetch=1,
        grid=(kv_heads, blocks),
        in_specs=[
            pl.BlockSpec((1, rows, head_dim), fixed_map),
            pl.BlockSpec((1, head_dim, block), cache_map),
            pl.BlockSpec((1, head_dim, block), cache_map),
            pl.BlockSpec((1, head_dim, block), fixed_map),
            pl.BlockSpec((1, head_dim, block), fixed_map),
        ],
        out_specs=pl.BlockSpec((1, rows, head_dim), fixed_map),
        scratch_shapes=[
            pltpu.VMEM((rows, 1), jnp.float32),
            pltpu.VMEM((rows, 1), jnp.float32),
            pltpu.VMEM((rows, head_dim), jnp.float32),
        ],
    )
    flops = 4 * kv_heads * rows * keys.shape[2] * head_dim
    return pl.pallas_call(
        kernel,
        grid_spec=grid_spec,
        out_shape=jax.ShapeDtypeStruct(query.shape, jnp.bfloat16),
        compiler_params=pltpu.CompilerParams(dimension_semantics=("arbitrary", "arbitrary")),
        cost_estimate=pl.CostEstimate(
            flops=flops,
            transcendentals=kv_heads * rows * keys.shape[2],
            bytes_accessed=2 * (query.size + keys.size + values.size + query.size),
        ),
    )(length.reshape(1), query, keys, values, key_new, value_new)


def shifted(values, shift):
    devices = lax.axis_size("ep")
    return lax.ppermute(values, "ep", [(i, (i + shift) % devices) for i in range(devices)])


def gather_columns(values):
    devices = lax.axis_size("ep")
    me = lax.axis_index("ep")
    width = values.shape[-1]
    whole = jnp.zeros(values.shape[:-1] + (width * devices,), values.dtype)
    for shift in range(devices):
        piece = values if shift == 0 else shifted(values, shift)
        source = (me - shift) % devices
        whole = lax.dynamic_update_slice_in_dim(whole, piece, source * width, values.ndim - 1)
    return whole


def sum_over_ep(part):
    devices = lax.axis_size("ep")
    total = part.astype(jnp.float32)
    for shift in range(1, devices):
        total = total + shifted(part, shift).astype(jnp.float32)
    return total


def on_device(
    hidden,
    key_cache,
    value_cache,
    request_order,
    cached_lengths,
    expert_ids,
    gate_values,
    attn_gain,
    ffn_gain,
    w_query,
    w_key,
    w_value,
    w_out,
    expert_gate,
    expert_up,
    expert_down,
):
    own_rows = hidden[0]
    new_rows = own_rows.shape[0]
    own_width = own_rows.shape[1]
    head_dim = key_cache.shape[3]
    kv_local = key_cache.shape[1]
    heads_local = w_query.shape[1] // head_dim
    group = heads_local // kv_local
    per_device = expert_gate.shape[0]
    capacity = 3 * new_rows // 8
    me = lax.axis_index("ep")
    gate_up = lax.all_gather(jnp.stack([expert_gate, expert_up]), "req", axis=2, tiled=True)
    gate_whole = gate_up[0]
    up_whole = gate_up[1]
    down_whole = lax.all_gather(expert_down, "req", axis=1, tiled=True)
    everyone = jnp.arange(request_order.shape[0], dtype=jnp.int32)
    request = jnp.sum(jnp.where(everyone == lax.axis_index("req"), request_order, 0))
    length = jnp.sum(jnp.where(everyone == request, cached_lengths, 0))
    pieces = []
    for rows_part in (own_rows[: new_rows // 2], own_rows[new_rows // 2 :]):
        part_f = gather_columns(rows_part).astype(jnp.float32)
        if pieces:
            part_f, pieces[0] = lax.optimization_barrier((part_f, pieces[0]))
        part_normed = normalize(part_f, attn_gain).astype(jnp.bfloat16)
        pieces.append(
            (
                part_f,
                jnp.dot(part_normed, w_query, preferred_element_type=jnp.float32),
                jnp.dot(part_normed, w_key, preferred_element_type=jnp.float32),
                jnp.dot(part_normed, w_value, preferred_element_type=jnp.float32),
            )
        )
    rows_f, query, key_new, value_new = [
        jnp.concatenate(list(column), 0) for column in zip(*pieces)
    ]
    positions = length + jnp.arange(new_rows, dtype=jnp.int32)
    query = rotate(
        query.reshape(new_rows, heads_local, head_dim).transpose(1, 0, 2), positions
    ).astype(jnp.bfloat16) * jnp.asarray(head_dim ** (-0.5), jnp.bfloat16)
    key_new = rotate(
        key_new.reshape(new_rows, kv_local, head_dim).transpose(1, 0, 2), positions
    ).astype(jnp.bfloat16)
    value_new = (
        value_new.reshape(new_rows, kv_local, head_dim).transpose(1, 0, 2).astype(jnp.bfloat16)
    )
    zero = jnp.zeros((), jnp.int32)
    keys = lax.dynamic_update_slice(key_cache[0], key_new, (zero, length, zero))
    values = lax.dynamic_update_slice(value_cache[0], value_new, (zero, length, zero))
    half = new_rows // 2
    query = query.reshape(kv_local, group, new_rows, head_dim)
    key_cache_t = jnp.swapaxes(key_cache[0], 1, 2)
    value_cache_t = jnp.swapaxes(value_cache[0], 1, 2)
    key_new_t = jnp.swapaxes(key_new, 1, 2)
    value_new_t = jnp.swapaxes(value_new, 1, 2)
    head_sums = []
    for first in (0, half):
        part_query = query[:, :, first : first + half].reshape(kv_local, group * half, head_dim)
        attended = flash_attend(
            part_query,
            key_cache_t,
            value_cache_t,
            key_new_t,
            value_new_t,
            length,
            first,
            half,
        )
        attended = (
            attended.reshape(heads_local, half, head_dim)
            .transpose(1, 0, 2)
            .reshape(half, heads_local * head_dim)
        )
        head_part = jnp.dot(attended, w_out, preferred_element_type=jnp.float32).astype(
            jnp.bfloat16
        )
        head_sums.append(sum_over_ep(head_part))
    head_sum = jnp.concatenate(head_sums, 0)
    mixed_f = (rows_f + head_sum).astype(jnp.bfloat16).astype(jnp.float32)
    ffn_normed = normalize(mixed_f, ffn_gain).astype(jnp.bfloat16)
    table, gate_slot = route_tables(
        expert_ids[0],
        gate_values[0],
        me * per_device + jnp.arange(per_device, dtype=jnp.int32),
        capacity,
    )
    dispatched = jnp.einsum(
        "ect,td->ecd", table, ffn_normed, preferred_element_type=jnp.float32
    ).astype(jnp.bfloat16)
    gate_whole, up_whole, dispatched = lax.optimization_barrier((gate_whole, up_whole, dispatched))
    gate_act = jnp.einsum("ecd,edf->ecf", dispatched, gate_whole, preferred_element_type=jnp.float32)
    up_act = jnp.einsum("ecd,edf->ecf", dispatched, up_whole, preferred_element_type=jnp.float32)
    act = (jax.nn.silu(gate_act) * up_act).astype(jnp.bfloat16)
    down_whole, act = lax.optimization_barrier((down_whole, act))
    devices = lax.axis_size("ep")

    def expert_block(target):
        down_block = lax.dynamic_slice_in_dim(down_whole, target * own_width, own_width, 2)
        output = jnp.einsum("ecf,efd->ecd", act, down_block, preferred_element_type=jnp.float32)
        contrib = (output * gate_slot[..., None]).astype(jnp.bfloat16)
        return jnp.einsum(
            "ect,ecd->td", table, contrib, preferred_element_type=jnp.float32
        ).astype(jnp.bfloat16)

    received = [shifted(expert_block((me + shift) % devices), shift) for shift in range(1, devices)]
    expert_sum = expert_block(me).astype(jnp.float32)
    for piece in received:
        expert_sum = expert_sum + piece.astype(jnp.float32)
    mixed_own = lax.dynamic_slice_in_dim(mixed_f, me * own_width, own_width, 1)
    result = (mixed_own + expert_sum).astype(jnp.bfloat16)
    return (result[None], keys[None], values[None])


def solution(mesh):
    in_specs = (
        P("req", None, "ep"),
        P("req", "ep", None, None),
        P("req", "ep", None, None),
        P(),
        P(),
        P("req", None, None),
        P("req", None, None),
        P(),
        P(),
        P(None, "ep"),
        P(None, "ep"),
        P(None, "ep"),
        P("ep", None),
        P("ep", "req", None),
        P("ep", "req", None),
        P("ep", "req", None),
    )
    out_specs = (P("req", None, "ep"), P("req", "ep", None, None), P("req", "ep", None, None))
    return jax.shard_map(
        on_device, mesh=mesh, in_specs=in_specs, out_specs=out_specs, check_vma=False
    )
```

```python
import jax
import jax.numpy as jnp
from jax import lax
from jax.experimental import pallas as pl
from jax.experimental.pallas import tpu as pltpu
from jax.sharding import PartitionSpec as P

epsilon = 1e-06


def normalize(values, gain):
    return values * lax.rsqrt(jnp.mean(values * values, -1, keepdims=True) + epsilon) * gain


def rotate(values, positions):
    half = values.shape[-1] // 2
    freq = 10000.0 ** (-jnp.arange(half, dtype=jnp.float32) * (2.0 / values.shape[-1]))
    angle = positions.astype(jnp.float32)[:, None] * freq[None, :]
    cosine = jnp.cos(angle)
    sine = jnp.sin(angle)
    first = values[..., :half]
    second = values[..., half:]
    return jnp.concatenate([first * cosine - second * sine, second * cosine + first * sine], -1)


def rounded(values):
    return lax.optimization_barrier(values.astype(jnp.bfloat16)).astype(jnp.float32)


def route_tables(chosen, gate_rows, wanted, capacity):
    hits = chosen[:, :, None] == wanted[None, None, :]
    member = jnp.sum(hits.astype(jnp.int32), 1, dtype=jnp.int32)
    weight = jnp.sum(jnp.where(hits, gate_rows[:, :, None], 0.0), 1)
    place = jnp.cumsum(member, 0, dtype=jnp.int32) - 1
    slots = jnp.arange(capacity, dtype=jnp.int32)
    table = (member.T[:, None, :] == 1) & (place.T[:, None, :] == slots[None, :, None])
    gate_slot = jnp.sum(jnp.where(table, weight.T[:, None, :], 0.0), 2)
    return (table.astype(jnp.bfloat16), gate_slot)


def flash_attend(query, keys, values, key_new, value_new, length, first_token, tokens):
    kv_heads, rows, head_dim = query.shape
    block = key_new.shape[2]
    cached = keys.shape[2] - block
    wide = 2 * block if cached % (2 * block) == 0 else block
    blocks = 1 + cached // wide

    def cached_blocks(length_ref):
        return (length_ref[0] + wide - 1) // wide

    def kernel(length_ref, q_ref, kc_ref, vc_ref, kn_ref, vn_ref, o_ref, m_sc, l_sc, acc_sc):
        step = pl.program_id(1)
        length = length_ref[0]

        def visit(key_block, value_block, visible, first):
            scores = jnp.dot(q_ref[0], key_block, preferred_element_type=jnp.float32)
            if visible is not None:
                scores = jnp.where(visible, scores, -1e30)
            if first:
                highest = jnp.max(scores, -1, keepdims=True)
            else:
                previous = m_sc[...]
                highest = jnp.maximum(previous, jnp.max(scores, -1, keepdims=True))
            probs = jnp.exp(scores - highest)
            if visible is not None:
                probs = jnp.where(visible, probs, 0.0)
            summed = lax.dot_general(
                probs.astype(jnp.bfloat16),
                value_block,
                (((1,), (1,)), ((), ())),
                preferred_element_type=jnp.float32,
            )
            if first:
                l_sc[...] = jnp.sum(probs, -1, keepdims=True)
                acc_sc[...] = summed
            else:
                correction = jnp.exp(previous - highest)
                l_sc[...] = l_sc[...] * correction + jnp.sum(probs, -1, keepdims=True)
                acc_sc[...] = acc_sc[...] * correction + summed
            m_sc[...] = highest

        @pl.when(step == 0)
        def _():
            shape = (rows, block)
            column = lax.broadcasted_iota(jnp.int32, shape, 1)
            token = first_token + lax.rem(lax.broadcasted_iota(jnp.int32, shape, 0), tokens)
            visit(kn_ref[0], vn_ref[0], column <= token, True)

        column = lax.broadcasted_iota(jnp.int32, (rows, wide), 1)
        start = (step - 1) * wide

        whole = (step > 0) & (start + wide <= length)

        @pl.when(whole)
        def _():
            visit(kc_ref[0], vc_ref[0], None, False)

        @pl.when((step > 0) & jnp.logical_not(whole) & (start < length))
        def _():
            visit(kc_ref[0], vc_ref[0], column + start < length, False)

        @pl.when(step == blocks - 1)
        def _():
            o_ref[0] = (acc_sc[...] / l_sc[...]).astype(o_ref.dtype)

    def cache_map(head, step, length_ref):
        return (head, 0, jnp.clip(step - 1, 0, cached_blocks(length_ref) - 1))

    def fixed_map(head, step, length_ref):
        return (head, 0, 0)

    grid_spec = pltpu.PrefetchScalarGridSpec(
        num_scalar_prefetch=1,
        grid=(kv_heads, blocks),
        in_specs=[
            pl.BlockSpec((1, rows, head_dim), fixed_map),
            pl.BlockSpec((1, head_dim, wide), cache_map),
            pl.BlockSpec((1, head_dim, wide), cache_map),
            pl.BlockSpec((1, head_dim, block), fixed_map),
            pl.BlockSpec((1, head_dim, block), fixed_map),
        ],
        out_specs=pl.BlockSpec((1, rows, head_dim), fixed_map),
        scratch_shapes=[
            pltpu.VMEM((rows, 1), jnp.float32),
            pltpu.VMEM((rows, 1), jnp.float32),
            pltpu.VMEM((rows, head_dim), jnp.float32),
        ],
    )
    flops = 4 * kv_heads * rows * keys.shape[2] * head_dim
    return pl.pallas_call(
        kernel,
        grid_spec=grid_spec,
        out_shape=jax.ShapeDtypeStruct(query.shape, jnp.bfloat16),
        compiler_params=pltpu.CompilerParams(dimension_semantics=("arbitrary", "arbitrary")),
        cost_estimate=pl.CostEstimate(
            flops=flops,
            transcendentals=kv_heads * rows * keys.shape[2],
            bytes_accessed=2 * (query.size + keys.size + values.size + query.size),
        ),
    )(length.reshape(1), query, keys, values, key_new, value_new)


def shifted(values, shift):
    devices = lax.axis_size("ep")
    return lax.ppermute(values, "ep", [(i, (i + shift) % devices) for i in range(devices)])


def gather_columns(values):
    devices = lax.axis_size("ep")
    me = lax.axis_index("ep")
    width = values.shape[-1]
    whole = jnp.zeros(values.shape[:-1] + (width * devices,), values.dtype)
    for shift in range(devices):
        piece = values if shift == 0 else shifted(values, shift)
        source = (me - shift) % devices
        whole = lax.dynamic_update_slice_in_dim(whole, piece, source * width, values.ndim - 1)
    return whole


def sum_over_ep(part):
    devices = lax.axis_size("ep")
    total = part.astype(jnp.float32)
    for shift in range(1, devices):
        total = total + shifted(part, shift).astype(jnp.float32)
    return total


def on_device(
    hidden,
    key_cache,
    value_cache,
    request_order,
    cached_lengths,
    expert_ids,
    gate_values,
    attn_gain,
    ffn_gain,
    w_query,
    w_key,
    w_value,
    w_out,
    expert_gate,
    expert_up,
    expert_down,
):
    own_rows = hidden[0]
    new_rows = own_rows.shape[0]
    own_width = own_rows.shape[1]
    head_dim = key_cache.shape[3]
    kv_local = key_cache.shape[1]
    heads_local = w_query.shape[1] // head_dim
    group = heads_local // kv_local
    per_device = expert_gate.shape[0]
    capacity = 3 * new_rows // 8
    me = lax.axis_index("ep")
    gate_up = lax.all_gather(jnp.stack([expert_gate, expert_up]), "req", axis=2, tiled=True)
    gate_whole = gate_up[0]
    up_whole = gate_up[1]
    down_whole = lax.all_gather(expert_down, "req", axis=1, tiled=True)
    everyone = jnp.arange(request_order.shape[0], dtype=jnp.int32)
    request = jnp.sum(jnp.where(everyone == lax.axis_index("req"), request_order, 0))
    length = jnp.sum(jnp.where(everyone == request, cached_lengths, 0))
    rows_whole = gather_columns(own_rows)
    rows_f = rows_whole.astype(jnp.float32)
    normed = normalize(rows_f, attn_gain).astype(jnp.bfloat16)
    query = jnp.dot(normed, w_query, preferred_element_type=jnp.float32)
    key_new = jnp.dot(normed, w_key, preferred_element_type=jnp.float32)
    value_new = jnp.dot(normed, w_value, preferred_element_type=jnp.float32)
    positions = length + jnp.arange(new_rows, dtype=jnp.int32)
    query = rotate(
        query.reshape(new_rows, heads_local, head_dim).transpose(1, 0, 2), positions
    ).astype(jnp.bfloat16) * jnp.asarray(head_dim ** (-0.5), jnp.bfloat16)
    key_new = rotate(
        key_new.reshape(new_rows, kv_local, head_dim).transpose(1, 0, 2), positions
    ).astype(jnp.bfloat16)
    value_new = (
        value_new.reshape(new_rows, kv_local, head_dim).transpose(1, 0, 2).astype(jnp.bfloat16)
    )
    zero = jnp.zeros((), jnp.int32)
    keys = lax.dynamic_update_slice(key_cache[0], key_new, (zero, length, zero))
    values = lax.dynamic_update_slice(value_cache[0], value_new, (zero, length, zero))
    half = new_rows // 2
    query = query.reshape(kv_local, group, new_rows, head_dim)
    key_cache_t = jnp.swapaxes(key_cache[0], 1, 2)
    value_cache_t = jnp.swapaxes(value_cache[0], 1, 2)
    key_new_t = jnp.swapaxes(key_new, 1, 2)
    value_new_t = jnp.swapaxes(value_new, 1, 2)
    head_sums = []
    for first in (0, half):
        part_query = query[:, :, first : first + half].reshape(kv_local, group * half, head_dim)
        attended = flash_attend(
            part_query,
            key_cache_t,
            value_cache_t,
            key_new_t,
            value_new_t,
            length,
            first,
            half,
        )
        attended = (
            attended.reshape(heads_local, half, head_dim)
            .transpose(1, 0, 2)
            .reshape(half, heads_local * head_dim)
        )
        head_part = jnp.dot(attended, w_out, preferred_element_type=jnp.float32).astype(
            jnp.bfloat16
        )
        head_sums.append(sum_over_ep(head_part))
    head_sum = jnp.concatenate(head_sums, 0)
    mixed_f = (rows_f + head_sum).astype(jnp.bfloat16).astype(jnp.float32)
    ffn_normed = normalize(mixed_f, ffn_gain).astype(jnp.bfloat16)
    table, gate_slot = route_tables(
        expert_ids[0],
        gate_values[0],
        me * per_device + jnp.arange(per_device, dtype=jnp.int32),
        capacity,
    )
    dispatched = jnp.einsum(
        "ect,td->ecd", table, ffn_normed, preferred_element_type=jnp.float32
    ).astype(jnp.bfloat16)
    gate_whole, up_whole, dispatched = lax.optimization_barrier((gate_whole, up_whole, dispatched))
    gate_act = jnp.einsum("ecd,edf->ecf", dispatched, gate_whole, preferred_element_type=jnp.float32)
    up_act = jnp.einsum("ecd,edf->ecf", dispatched, up_whole, preferred_element_type=jnp.float32)
    act = (jax.nn.silu(gate_act) * up_act).astype(jnp.bfloat16)
    down_whole, act = lax.optimization_barrier((down_whole, act))
    devices = lax.axis_size("ep")

    def expert_block(target):
        down_block = lax.dynamic_slice_in_dim(down_whole, target * own_width, own_width, 2)
        output = jnp.einsum("ecf,efd->ecd", act, down_block, preferred_element_type=jnp.float32)
        contrib = (output * gate_slot[..., None]).astype(jnp.bfloat16)
        return jnp.einsum(
            "ect,ecd->td", table, contrib, preferred_element_type=jnp.float32
        ).astype(jnp.bfloat16)

    received = [shifted(expert_block((me + shift) % devices), shift) for shift in range(1, devices)]
    expert_sum = expert_block(me).astype(jnp.float32)
    for piece in received:
        expert_sum = expert_sum + piece.astype(jnp.float32)
    mixed_own = lax.dynamic_slice_in_dim(mixed_f, me * own_width, own_width, 1)
    result = (mixed_own + expert_sum).astype(jnp.bfloat16)
    return (result[None], keys[None], values[None])


def solution(mesh):
    in_specs = (
        P("req", None, "ep"),
        P("req", "ep", None, None),
        P("req", "ep", None, None),
        P(),
        P(),
        P("req", None, None),
        P("req", None, None),
        P(),
        P(),
        P(None, "ep"),
        P(None, "ep"),
        P(None, "ep"),
        P("ep", None),
        P("ep", "req", None),
        P("ep", "req", None),
        P("ep", "req", None),
    )
    out_specs = (P("req", None, "ep"), P("req", "ep", None, None), P("req", "ep", None, None))
    return jax.shard_map(
        on_device, mesh=mesh, in_specs=in_specs, out_specs=out_specs, check_vma=False
    )
```

```python
import jax
import jax.numpy as jnp
from jax import lax
from jax.experimental import pallas as pl
from jax.experimental.pallas import tpu as pltpu
from jax.sharding import PartitionSpec as P

epsilon = 1e-06


def normalize(values, gain):
    return values * lax.rsqrt(jnp.mean(values * values, -1, keepdims=True) + epsilon) * gain


def rotate(values, positions):
    half = values.shape[-1] // 2
    freq = 10000.0 ** (-jnp.arange(half, dtype=jnp.float32) * (2.0 / values.shape[-1]))
    angle = positions.astype(jnp.float32)[:, None] * freq[None, :]
    cosine = jnp.cos(angle)
    sine = jnp.sin(angle)
    first = values[..., :half]
    second = values[..., half:]
    return jnp.concatenate([first * cosine - second * sine, second * cosine + first * sine], -1)


def rounded(values):
    return lax.optimization_barrier(values.astype(jnp.bfloat16)).astype(jnp.float32)


def route_tables(chosen, gate_rows, wanted, capacity):
    hits = chosen[:, :, None] == wanted[None, None, :]
    member = jnp.sum(hits.astype(jnp.int32), 1, dtype=jnp.int32)
    weight = jnp.sum(jnp.where(hits, gate_rows[:, :, None], 0.0), 1)
    place = jnp.cumsum(member, 0, dtype=jnp.int32) - 1
    slots = jnp.arange(capacity, dtype=jnp.int32)
    table = (member.T[:, None, :] == 1) & (place.T[:, None, :] == slots[None, :, None])
    gate_slot = jnp.sum(jnp.where(table, weight.T[:, None, :], 0.0), 2)
    return (table.astype(jnp.bfloat16), gate_slot)


def flash_attend(query, keys, values, key_new, value_new, length, first_token, tokens):
    kv_heads, rows, head_dim = query.shape
    block = key_new.shape[2]
    cached = keys.shape[2] - block
    wide = cached if cached % block == 0 else block
    blocks = 1 + cached // wide

    def cached_blocks(length_ref):
        return (length_ref[0] + wide - 1) // wide

    def kernel(length_ref, q_ref, kc_ref, vc_ref, kn_ref, vn_ref, o_ref, m_sc, l_sc, acc_sc):
        step = pl.program_id(1)
        length = length_ref[0]

        def visit(key_block, value_block, visible, first):
            scores = jnp.dot(q_ref[0], key_block, preferred_element_type=jnp.float32)
            if visible is not None:
                scores = jnp.where(visible, scores, -1e30)
            if first:
                highest = jnp.max(scores, -1, keepdims=True)
            else:
                previous = m_sc[...]
                highest = jnp.maximum(previous, jnp.max(scores, -1, keepdims=True))
            probs = jnp.exp(scores - highest)
            if visible is not None:
                probs = jnp.where(visible, probs, 0.0)
            summed = lax.dot_general(
                probs.astype(jnp.bfloat16),
                value_block,
                (((1,), (1,)), ((), ())),
                preferred_element_type=jnp.float32,
            )
            if first:
                l_sc[...] = jnp.sum(probs, -1, keepdims=True)
                acc_sc[...] = summed
            else:
                correction = jnp.exp(previous - highest)
                l_sc[...] = l_sc[...] * correction + jnp.sum(probs, -1, keepdims=True)
                acc_sc[...] = acc_sc[...] * correction + summed
            m_sc[...] = highest

        @pl.when(step == 0)
        def _():
            shape = (rows, block)
            column = lax.broadcasted_iota(jnp.int32, shape, 1)
            token = first_token + lax.rem(lax.broadcasted_iota(jnp.int32, shape, 0), tokens)
            visit(kn_ref[0], vn_ref[0], column <= token, True)

        column = lax.broadcasted_iota(jnp.int32, (rows, wide), 1)
        start = (step - 1) * wide

        whole = (step > 0) & (start + wide <= length)

        @pl.when(whole)
        def _():
            visit(kc_ref[0], vc_ref[0], None, False)

        @pl.when((step > 0) & jnp.logical_not(whole) & (start < length))
        def _():
            visit(kc_ref[0], vc_ref[0], column + start < length, False)

        @pl.when(step == blocks - 1)
        def _():
            o_ref[0] = (acc_sc[...] / l_sc[...]).astype(o_ref.dtype)

    def cache_map(head, step, length_ref):
        return (head, 0, jnp.clip(step - 1, 0, cached_blocks(length_ref) - 1))

    def fixed_map(head, step, length_ref):
        return (head, 0, 0)

    grid_spec = pltpu.PrefetchScalarGridSpec(
        num_scalar_prefetch=1,
        grid=(kv_heads, blocks),
        in_specs=[
            pl.BlockSpec((1, rows, head_dim), fixed_map),
            pl.BlockSpec((1, head_dim, wide), cache_map),
            pl.BlockSpec((1, head_dim, wide), cache_map),
            pl.BlockSpec((1, head_dim, block), fixed_map),
            pl.BlockSpec((1, head_dim, block), fixed_map),
        ],
        out_specs=pl.BlockSpec((1, rows, head_dim), fixed_map),
        scratch_shapes=[
            pltpu.VMEM((rows, 1), jnp.float32),
            pltpu.VMEM((rows, 1), jnp.float32),
            pltpu.VMEM((rows, head_dim), jnp.float32),
        ],
    )
    flops = 4 * kv_heads * rows * keys.shape[2] * head_dim
    return pl.pallas_call(
        kernel,
        grid_spec=grid_spec,
        out_shape=jax.ShapeDtypeStruct(query.shape, jnp.bfloat16),
        compiler_params=pltpu.CompilerParams(dimension_semantics=("arbitrary", "arbitrary")),
        cost_estimate=pl.CostEstimate(
            flops=flops,
            transcendentals=kv_heads * rows * keys.shape[2],
            bytes_accessed=2 * (query.size + keys.size + values.size + query.size),
        ),
    )(length.reshape(1), query, keys, values, key_new, value_new)


def shifted(values, shift):
    devices = lax.axis_size("ep")
    return lax.ppermute(values, "ep", [(i, (i + shift) % devices) for i in range(devices)])


def gather_columns(values):
    devices = lax.axis_size("ep")
    me = lax.axis_index("ep")
    width = values.shape[-1]
    whole = jnp.zeros(values.shape[:-1] + (width * devices,), values.dtype)
    for shift in range(devices):
        piece = values if shift == 0 else shifted(values, shift)
        source = (me - shift) % devices
        whole = lax.dynamic_update_slice_in_dim(whole, piece, source * width, values.ndim - 1)
    return whole


def sum_over_ep(part):
    devices = lax.axis_size("ep")
    total = part.astype(jnp.float32)
    for shift in range(1, devices):
        total = total + shifted(part, shift).astype(jnp.float32)
    return total


def on_device(
    hidden,
    key_cache,
    value_cache,
    request_order,
    cached_lengths,
    expert_ids,
    gate_values,
    attn_gain,
    ffn_gain,
    w_query,
    w_key,
    w_value,
    w_out,
    expert_gate,
    expert_up,
    expert_down,
):
    own_rows = hidden[0]
    new_rows = own_rows.shape[0]
    own_width = own_rows.shape[1]
    head_dim = key_cache.shape[3]
    kv_local = key_cache.shape[1]
    heads_local = w_query.shape[1] // head_dim
    group = heads_local // kv_local
    per_device = expert_gate.shape[0]
    capacity = 3 * new_rows // 8
    me = lax.axis_index("ep")
    gate_up = lax.all_gather(jnp.stack([expert_gate, expert_up]), "req", axis=2, tiled=True)
    gate_whole = gate_up[0]
    up_whole = gate_up[1]
    down_whole = lax.all_gather(expert_down, "req", axis=1, tiled=True)
    everyone = jnp.arange(request_order.shape[0], dtype=jnp.int32)
    request = jnp.sum(jnp.where(everyone == lax.axis_index("req"), request_order, 0))
    length = jnp.sum(jnp.where(everyone == request, cached_lengths, 0))
    rows_whole = gather_columns(own_rows)
    rows_f = rows_whole.astype(jnp.float32)
    normed = normalize(rows_f, attn_gain).astype(jnp.bfloat16)
    query = jnp.dot(normed, w_query, preferred_element_type=jnp.float32)
    key_new = jnp.dot(normed, w_key, preferred_element_type=jnp.float32)
    value_new = jnp.dot(normed, w_value, preferred_element_type=jnp.float32)
    positions = length + jnp.arange(new_rows, dtype=jnp.int32)
    query = rotate(
        query.reshape(new_rows, heads_local, head_dim).transpose(1, 0, 2), positions
    ).astype(jnp.bfloat16) * jnp.asarray(head_dim ** (-0.5), jnp.bfloat16)
    key_new = rotate(
        key_new.reshape(new_rows, kv_local, head_dim).transpose(1, 0, 2), positions
    ).astype(jnp.bfloat16)
    value_new = (
        value_new.reshape(new_rows, kv_local, head_dim).transpose(1, 0, 2).astype(jnp.bfloat16)
    )
    zero = jnp.zeros((), jnp.int32)
    keys = lax.dynamic_update_slice(key_cache[0], key_new, (zero, length, zero))
    values = lax.dynamic_update_slice(value_cache[0], value_new, (zero, length, zero))
    half = new_rows // 2
    query = query.reshape(kv_local, group, new_rows, head_dim)
    key_cache_t = jnp.swapaxes(key_cache[0], 1, 2)
    value_cache_t = jnp.swapaxes(value_cache[0], 1, 2)
    key_new_t = jnp.swapaxes(key_new, 1, 2)
    value_new_t = jnp.swapaxes(value_new, 1, 2)
    head_sums = []
    for first in (0, half):
        part_query = query[:, :, first : first + half].reshape(kv_local, group * half, head_dim)
        attended = flash_attend(
            part_query,
            key_cache_t,
            value_cache_t,
            key_new_t,
            value_new_t,
            length,
            first,
            half,
        )
        attended = (
            attended.reshape(heads_local, half, head_dim)
            .transpose(1, 0, 2)
            .reshape(half, heads_local * head_dim)
        )
        head_part = jnp.dot(attended, w_out, preferred_element_type=jnp.float32).astype(
            jnp.bfloat16
        )
        head_sums.append(sum_over_ep(head_part))
    head_sum = jnp.concatenate(head_sums, 0)
    mixed_f = (rows_f + head_sum).astype(jnp.bfloat16).astype(jnp.float32)
    ffn_normed = normalize(mixed_f, ffn_gain).astype(jnp.bfloat16)
    table, gate_slot = route_tables(
        expert_ids[0],
        gate_values[0],
        me * per_device + jnp.arange(per_device, dtype=jnp.int32),
        capacity,
    )
    dispatched = jnp.einsum(
        "ect,td->ecd", table, ffn_normed, preferred_element_type=jnp.float32
    ).astype(jnp.bfloat16)
    gate_whole, up_whole, dispatched = lax.optimization_barrier((gate_whole, up_whole, dispatched))
    gate_act = jnp.einsum("ecd,edf->ecf", dispatched, gate_whole, preferred_element_type=jnp.float32)
    up_act = jnp.einsum("ecd,edf->ecf", dispatched, up_whole, preferred_element_type=jnp.float32)
    act = (jax.nn.silu(gate_act) * up_act).astype(jnp.bfloat16)
    down_whole, act = lax.optimization_barrier((down_whole, act))
    devices = lax.axis_size("ep")

    def expert_block(target):
        down_block = lax.dynamic_slice_in_dim(down_whole, target * own_width, own_width, 2)
        output = jnp.einsum("ecf,efd->ecd", act, down_block, preferred_element_type=jnp.float32)
        contrib = (output * gate_slot[..., None]).astype(jnp.bfloat16)
        return jnp.einsum(
            "ect,ecd->td", table, contrib, preferred_element_type=jnp.float32
        ).astype(jnp.bfloat16)

    received = [shifted(expert_block((me + shift) % devices), shift) for shift in range(1, devices)]
    expert_sum = expert_block(me).astype(jnp.float32)
    for piece in received:
        expert_sum = expert_sum + piece.astype(jnp.float32)
    mixed_own = lax.dynamic_slice_in_dim(mixed_f, me * own_width, own_width, 1)
    result = (mixed_own + expert_sum).astype(jnp.bfloat16)
    return (result[None], keys[None], values[None])


def solution(mesh):
    in_specs = (
        P("req", None, "ep"),
        P("req", "ep", None, None),
        P("req", "ep", None, None),
        P(),
        P(),
        P("req", None, None),
        P("req", None, None),
        P(),
        P(),
        P(None, "ep"),
        P(None, "ep"),
        P(None, "ep"),
        P("ep", None),
        P("ep", "req", None),
        P("ep", "req", None),
        P("ep", "req", None),
    )
    out_specs = (P("req", None, "ep"), P("req", "ep", None, None), P("req", "ep", None, None))
    return jax.shard_map(
        on_device, mesh=mesh, in_specs=in_specs, out_specs=out_specs, check_vma=False
    )
```

```python
import jax
import jax.numpy as jnp
from jax import lax
from jax.experimental import pallas as pl
from jax.experimental.pallas import tpu as pltpu
from jax.sharding import PartitionSpec as P

epsilon = 1e-06


def normalize(values, gain):
    return values * lax.rsqrt(jnp.mean(values * values, -1, keepdims=True) + epsilon) * gain


def rotate(values, positions):
    half = values.shape[-1] // 2
    freq = 10000.0 ** (-jnp.arange(half, dtype=jnp.float32) * (2.0 / values.shape[-1]))
    angle = positions.astype(jnp.float32)[:, None] * freq[None, :]
    cosine = jnp.cos(angle)
    sine = jnp.sin(angle)
    first = values[..., :half]
    second = values[..., half:]
    return jnp.concatenate([first * cosine - second * sine, second * cosine + first * sine], -1)


def rounded(values):
    return lax.optimization_barrier(values.astype(jnp.bfloat16)).astype(jnp.float32)


def route_tables(chosen, gate_rows, wanted, capacity):
    hits = chosen[:, :, None] == wanted[None, None, :]
    member = jnp.sum(hits.astype(jnp.int32), 1, dtype=jnp.int32)
    weight = jnp.sum(jnp.where(hits, gate_rows[:, :, None], 0.0), 1)
    place = jnp.cumsum(member, 0, dtype=jnp.int32) - 1
    slots = jnp.arange(capacity, dtype=jnp.int32)
    table = (member.T[:, None, :] == 1) & (place.T[:, None, :] == slots[None, :, None])
    gate_slot = jnp.sum(jnp.where(table, weight.T[:, None, :], 0.0), 2)
    return (table.astype(jnp.bfloat16), gate_slot)


def flash_attend(query, keys, values, key_new, value_new, length, first_token, tokens):
    kv_heads, rows, head_dim = query.shape
    block = key_new.shape[2]
    cached = keys.shape[2] - block
    wide = cached if cached % block == 0 else block
    blocks = 1 + cached // wide

    def cached_blocks(length_ref):
        return (length_ref[0] + wide - 1) // wide

    def kernel(length_ref, q_ref, kc_ref, vc_ref, kn_ref, vn_ref, o_ref, m_sc, l_sc, acc_sc):
        step = pl.program_id(1)
        length = length_ref[0]

        def visit(key_block, value_block, visible, first):
            scores = jnp.dot(q_ref[0], key_block, preferred_element_type=jnp.float32)
            if visible is not None:
                scores = jnp.where(visible, scores, -1e30)
            if first:
                highest = jnp.max(scores, -1, keepdims=True)
            else:
                previous = m_sc[...]
                highest = jnp.maximum(previous, jnp.max(scores, -1, keepdims=True))
            probs = jnp.exp(scores - highest)
            if visible is not None:
                probs = jnp.where(visible, probs, 0.0)
            summed = lax.dot_general(
                probs.astype(jnp.bfloat16),
                value_block,
                (((1,), (1,)), ((), ())),
                preferred_element_type=jnp.float32,
            )
            if first:
                l_sc[...] = jnp.sum(probs, -1, keepdims=True)
                acc_sc[...] = summed
            else:
                correction = jnp.exp(previous - highest)
                l_sc[...] = l_sc[...] * correction + jnp.sum(probs, -1, keepdims=True)
                acc_sc[...] = acc_sc[...] * correction + summed
            m_sc[...] = highest

        @pl.when(step == 0)
        def _():
            shape = (rows, block)
            column = lax.broadcasted_iota(jnp.int32, shape, 1)
            token = first_token + lax.rem(lax.broadcasted_iota(jnp.int32, shape, 0), tokens)
            visit(kn_ref[0], vn_ref[0], column <= token, True)

        column = lax.broadcasted_iota(jnp.int32, (rows, wide), 1)
        start = (step - 1) * wide

        whole = (step > 0) & (start + wide <= length)

        @pl.when(whole)
        def _():
            visit(kc_ref[0], vc_ref[0], None, False)

        @pl.when((step > 0) & jnp.logical_not(whole) & (start < length))
        def _():
            visit(kc_ref[0], vc_ref[0], column + start < length, False)

        @pl.when(step == blocks - 1)
        def _():
            o_ref[0] = (acc_sc[...] / l_sc[...]).astype(o_ref.dtype)

    def cache_map(head, step, length_ref):
        return (head, 0, jnp.clip(step - 1, 0, cached_blocks(length_ref) - 1))

    def fixed_map(head, step, length_ref):
        return (head, 0, 0)

    grid_spec = pltpu.PrefetchScalarGridSpec(
        num_scalar_prefetch=1,
        grid=(kv_heads, blocks),
        in_specs=[
            pl.BlockSpec((1, rows, head_dim), fixed_map),
            pl.BlockSpec((1, head_dim, wide), cache_map),
            pl.BlockSpec((1, head_dim, wide), cache_map),
            pl.BlockSpec((1, head_dim, block), fixed_map),
            pl.BlockSpec((1, head_dim, block), fixed_map),
        ],
        out_specs=pl.BlockSpec((1, rows, head_dim), fixed_map),
        scratch_shapes=[
            pltpu.VMEM((rows, 1), jnp.float32),
            pltpu.VMEM((rows, 1), jnp.float32),
            pltpu.VMEM((rows, head_dim), jnp.float32),
        ],
    )
    flops = 4 * kv_heads * rows * keys.shape[2] * head_dim
    return pl.pallas_call(
        kernel,
        grid_spec=grid_spec,
        out_shape=jax.ShapeDtypeStruct(query.shape, jnp.bfloat16),
        compiler_params=pltpu.CompilerParams(dimension_semantics=("arbitrary", "arbitrary")),
        cost_estimate=pl.CostEstimate(
            flops=flops,
            transcendentals=kv_heads * rows * keys.shape[2],
            bytes_accessed=2 * (query.size + keys.size + values.size + query.size),
        ),
    )(length.reshape(1), query, keys, values, key_new, value_new)


def shifted(values, shift):
    devices = lax.axis_size("ep")
    return lax.ppermute(values, "ep", [(i, (i + shift) % devices) for i in range(devices)])


def gather_columns(values):
    devices = lax.axis_size("ep")
    me = lax.axis_index("ep")
    width = values.shape[-1]
    whole = jnp.zeros(values.shape[:-1] + (width * devices,), values.dtype)
    for shift in range(devices):
        piece = values if shift == 0 else shifted(values, shift)
        source = (me - shift) % devices
        whole = lax.dynamic_update_slice_in_dim(whole, piece, source * width, values.ndim - 1)
    return whole


def sum_over_ep(part):
    devices = lax.axis_size("ep")
    total = part.astype(jnp.float32)
    for shift in range(1, devices):
        total = total + shifted(part, shift).astype(jnp.float32)
    return total


def on_device(
    hidden,
    key_cache,
    value_cache,
    request_order,
    cached_lengths,
    expert_ids,
    gate_values,
    attn_gain,
    ffn_gain,
    w_query,
    w_key,
    w_value,
    w_out,
    expert_gate,
    expert_up,
    expert_down,
):
    own_rows = hidden[0]
    new_rows = own_rows.shape[0]
    own_width = own_rows.shape[1]
    head_dim = key_cache.shape[3]
    kv_local = key_cache.shape[1]
    heads_local = w_query.shape[1] // head_dim
    group = heads_local // kv_local
    per_device = expert_gate.shape[0]
    capacity = 3 * new_rows // 8
    me = lax.axis_index("ep")
    gate_up = lax.all_gather(jnp.stack([expert_gate, expert_up]), "req", axis=2, tiled=True)
    down_whole = lax.all_gather(expert_down, "req", axis=1, tiled=True)
    everyone = jnp.arange(request_order.shape[0], dtype=jnp.int32)
    request = jnp.sum(jnp.where(everyone == lax.axis_index("req"), request_order, 0))
    length = jnp.sum(jnp.where(everyone == request, cached_lengths, 0))
    rows_whole = gather_columns(own_rows)
    rows_f = rows_whole.astype(jnp.float32)
    normed = normalize(rows_f, attn_gain).astype(jnp.bfloat16)
    query = jnp.dot(normed, w_query, preferred_element_type=jnp.float32)
    key_new = jnp.dot(normed, w_key, preferred_element_type=jnp.float32)
    value_new = jnp.dot(normed, w_value, preferred_element_type=jnp.float32)
    positions = length + jnp.arange(new_rows, dtype=jnp.int32)
    query = rotate(
        query.reshape(new_rows, heads_local, head_dim).transpose(1, 0, 2), positions
    ).astype(jnp.bfloat16) * jnp.asarray(head_dim ** (-0.5), jnp.bfloat16)
    key_new = rotate(
        key_new.reshape(new_rows, kv_local, head_dim).transpose(1, 0, 2), positions
    ).astype(jnp.bfloat16)
    value_new = (
        value_new.reshape(new_rows, kv_local, head_dim).transpose(1, 0, 2).astype(jnp.bfloat16)
    )
    zero = jnp.zeros((), jnp.int32)
    keys = lax.dynamic_update_slice(key_cache[0], key_new, (zero, length, zero))
    values = lax.dynamic_update_slice(value_cache[0], value_new, (zero, length, zero))
    half = new_rows // 2
    query = query.reshape(kv_local, group, new_rows, head_dim)
    key_cache_t = jnp.swapaxes(key_cache[0], 1, 2)
    value_cache_t = jnp.swapaxes(value_cache[0], 1, 2)
    key_new_t = jnp.swapaxes(key_new, 1, 2)
    value_new_t = jnp.swapaxes(value_new, 1, 2)
    head_sums = []
    for first in (0, half):
        part_query = query[:, :, first : first + half].reshape(kv_local, group * half, head_dim)
        attended = flash_attend(
            part_query,
            key_cache_t,
            value_cache_t,
            key_new_t,
            value_new_t,
            length,
            first,
            half,
        )
        attended = (
            attended.reshape(heads_local, half, head_dim)
            .transpose(1, 0, 2)
            .reshape(half, heads_local * head_dim)
        )
        head_part = jnp.dot(attended, w_out, preferred_element_type=jnp.float32).astype(
            jnp.bfloat16
        )
        head_sums.append(sum_over_ep(head_part))
    head_sum = jnp.concatenate(head_sums, 0)
    mixed_f = (rows_f + head_sum).astype(jnp.bfloat16).astype(jnp.float32)
    ffn_normed = normalize(mixed_f, ffn_gain).astype(jnp.bfloat16)
    table, gate_slot = route_tables(
        expert_ids[0],
        gate_values[0],
        me * per_device + jnp.arange(per_device, dtype=jnp.int32),
        capacity,
    )
    dispatched = jnp.einsum(
        "ect,td->ecd", table, ffn_normed, preferred_element_type=jnp.float32
    ).astype(jnp.bfloat16)
    gate_up, dispatched = lax.optimization_barrier((gate_up, dispatched))
    both = jnp.einsum("ecd,kedf->kecf", dispatched, gate_up, preferred_element_type=jnp.float32)
    act = (jax.nn.silu(both[0]) * both[1]).astype(jnp.bfloat16)
    down_whole, act = lax.optimization_barrier((down_whole, act))
    devices = lax.axis_size("ep")

    def expert_block(target):
        down_block = lax.dynamic_slice_in_dim(down_whole, target * own_width, own_width, 2)
        output = jnp.einsum("ecf,efd->ecd", act, down_block, preferred_element_type=jnp.float32)
        contrib = (output * gate_slot[..., None]).astype(jnp.bfloat16)
        return jnp.einsum(
            "ect,ecd->td", table, contrib, preferred_element_type=jnp.float32
        ).astype(jnp.bfloat16)

    received = [shifted(expert_block((me + shift) % devices), shift) for shift in range(1, devices)]
    expert_sum = expert_block(me).astype(jnp.float32)
    for piece in received:
        expert_sum = expert_sum + piece.astype(jnp.float32)
    mixed_own = lax.dynamic_slice_in_dim(mixed_f, me * own_width, own_width, 1)
    result = (mixed_own + expert_sum).astype(jnp.bfloat16)
    return (result[None], keys[None], values[None])


def solution(mesh):
    in_specs = (
        P("req", None, "ep"),
        P("req", "ep", None, None),
        P("req", "ep", None, None),
        P(),
        P(),
        P("req", None, None),
        P("req", None, None),
        P(),
        P(),
        P(None, "ep"),
        P(None, "ep"),
        P(None, "ep"),
        P("ep", None),
        P("ep", "req", None),
        P("ep", "req", None),
        P("ep", "req", None),
    )
    out_specs = (P("req", None, "ep"), P("req", "ep", None, None), P("req", "ep", None, None))
    return jax.shard_map(
        on_device, mesh=mesh, in_specs=in_specs, out_specs=out_specs, check_vma=False
    )
```

```python
import jax
import jax.numpy as jnp
from jax import lax
from jax.experimental import pallas as pl
from jax.experimental.pallas import tpu as pltpu
from jax.sharding import PartitionSpec as P

epsilon = 1e-06


def normalize(values, gain):
    return values * lax.rsqrt(jnp.mean(values * values, -1, keepdims=True) + epsilon) * gain


def rotate(values, positions):
    half = values.shape[-1] // 2
    freq = 10000.0 ** (-jnp.arange(half, dtype=jnp.float32) * (2.0 / values.shape[-1]))
    angle = positions.astype(jnp.float32)[:, None] * freq[None, :]
    cosine = jnp.cos(angle)
    sine = jnp.sin(angle)
    first = values[..., :half]
    second = values[..., half:]
    return jnp.concatenate([first * cosine - second * sine, second * cosine + first * sine], -1)


def rounded(values):
    return lax.optimization_barrier(values.astype(jnp.bfloat16)).astype(jnp.float32)


def route_tables(chosen, gate_rows, wanted, capacity):
    hits = chosen[:, :, None] == wanted[None, None, :]
    member = jnp.sum(hits.astype(jnp.int32), 1, dtype=jnp.int32)
    weight = jnp.sum(jnp.where(hits, gate_rows[:, :, None], 0.0), 1)
    place = jnp.cumsum(member, 0, dtype=jnp.int32) - 1
    slots = jnp.arange(capacity, dtype=jnp.int32)
    table = (member.T[:, None, :] == 1) & (place.T[:, None, :] == slots[None, :, None])
    gate_slot = jnp.sum(jnp.where(table, weight.T[:, None, :], 0.0), 2)
    return (table.astype(jnp.bfloat16), gate_slot)


def flash_attend(query, keys, values, key_new, value_new, length, first_token, tokens):
    kv_heads, rows, head_dim = query.shape
    block = key_new.shape[2]
    cached = keys.shape[2] - block
    wide = cached if cached % block == 0 else block
    blocks = 1 + cached // wide

    def cached_blocks(length_ref):
        return (length_ref[0] + wide - 1) // wide

    def kernel(length_ref, q_ref, kc_ref, vc_ref, kn_ref, vn_ref, o_ref, m_sc, l_sc, acc_sc):
        step = pl.program_id(1)
        length = length_ref[0]

        def visit(key_block, value_block, visible, first):
            scores = jnp.dot(q_ref[0], key_block, preferred_element_type=jnp.float32)
            if visible is not None:
                scores = jnp.where(visible, scores, -1e30)
            if first:
                highest = jnp.max(scores, -1, keepdims=True)
            else:
                previous = m_sc[...]
                highest = jnp.maximum(previous, jnp.max(scores, -1, keepdims=True))
            probs = jnp.exp(scores - highest)
            if visible is not None:
                probs = jnp.where(visible, probs, 0.0)
            summed = lax.dot_general(
                probs.astype(jnp.bfloat16),
                value_block,
                (((1,), (1,)), ((), ())),
                preferred_element_type=jnp.float32,
            )
            if first:
                l_sc[...] = jnp.sum(probs, -1, keepdims=True)
                acc_sc[...] = summed
            else:
                correction = jnp.exp(previous - highest)
                l_sc[...] = l_sc[...] * correction + jnp.sum(probs, -1, keepdims=True)
                acc_sc[...] = acc_sc[...] * correction + summed
            m_sc[...] = highest

        @pl.when(step == 0)
        def _():
            shape = (rows, block)
            column = lax.broadcasted_iota(jnp.int32, shape, 1)
            token = first_token + lax.rem(lax.broadcasted_iota(jnp.int32, shape, 0), tokens)
            visit(kn_ref[0], vn_ref[0], column <= token, True)

        column = lax.broadcasted_iota(jnp.int32, (rows, wide), 1)
        start = (step - 1) * wide

        whole = (step > 0) & (start + wide <= length)

        @pl.when(whole)
        def _():
            visit(kc_ref[0], vc_ref[0], None, False)

        @pl.when((step > 0) & jnp.logical_not(whole) & (start < length))
        def _():
            visit(kc_ref[0], vc_ref[0], column + start < length, False)

        @pl.when(step == blocks - 1)
        def _():
            o_ref[0] = (acc_sc[...] / l_sc[...]).astype(o_ref.dtype)

    def cache_map(head, step, length_ref):
        return (head, 0, jnp.clip(step - 1, 0, cached_blocks(length_ref) - 1))

    def fixed_map(head, step, length_ref):
        return (head, 0, 0)

    grid_spec = pltpu.PrefetchScalarGridSpec(
        num_scalar_prefetch=1,
        grid=(kv_heads, blocks),
        in_specs=[
            pl.BlockSpec((1, rows, head_dim), fixed_map),
            pl.BlockSpec((1, head_dim, wide), cache_map),
            pl.BlockSpec((1, head_dim, wide), cache_map),
            pl.BlockSpec((1, head_dim, block), fixed_map),
            pl.BlockSpec((1, head_dim, block), fixed_map),
        ],
        out_specs=pl.BlockSpec((1, rows, head_dim), fixed_map),
        scratch_shapes=[
            pltpu.VMEM((rows, 1), jnp.float32),
            pltpu.VMEM((rows, 1), jnp.float32),
            pltpu.VMEM((rows, head_dim), jnp.float32),
        ],
    )
    flops = 4 * kv_heads * rows * keys.shape[2] * head_dim
    return pl.pallas_call(
        kernel,
        grid_spec=grid_spec,
        out_shape=jax.ShapeDtypeStruct(query.shape, jnp.bfloat16),
        compiler_params=pltpu.CompilerParams(dimension_semantics=("arbitrary", "arbitrary")),
        cost_estimate=pl.CostEstimate(
            flops=flops,
            transcendentals=kv_heads * rows * keys.shape[2],
            bytes_accessed=2 * (query.size + keys.size + values.size + query.size),
        ),
    )(length.reshape(1), query, keys, values, key_new, value_new)


def shifted(values, shift):
    devices = lax.axis_size("ep")
    return lax.ppermute(values, "ep", [(i, (i + shift) % devices) for i in range(devices)])


def gather_columns(values):
    devices = lax.axis_size("ep")
    me = lax.axis_index("ep")
    width = values.shape[-1]
    whole = jnp.zeros(values.shape[:-1] + (width * devices,), values.dtype)
    for shift in range(devices):
        piece = values if shift == 0 else shifted(values, shift)
        source = (me - shift) % devices
        whole = lax.dynamic_update_slice_in_dim(whole, piece, source * width, values.ndim - 1)
    return whole


def sum_over_ep(part):
    devices = lax.axis_size("ep")
    total = part.astype(jnp.float32)
    for shift in range(1, devices):
        total = total + shifted(part, shift).astype(jnp.float32)
    return total


def on_device(
    hidden,
    key_cache,
    value_cache,
    request_order,
    cached_lengths,
    expert_ids,
    gate_values,
    attn_gain,
    ffn_gain,
    w_query,
    w_key,
    w_value,
    w_out,
    expert_gate,
    expert_up,
    expert_down,
):
    own_rows = hidden[0]
    new_rows = own_rows.shape[0]
    own_width = own_rows.shape[1]
    head_dim = key_cache.shape[3]
    kv_local = key_cache.shape[1]
    heads_local = w_query.shape[1] // head_dim
    group = heads_local // kv_local
    per_device = expert_gate.shape[0]
    capacity = 3 * new_rows // 8
    me = lax.axis_index("ep")
    req_devices = lax.axis_size("req")
    down_rows = expert_down.shape[1]
    weights = lax.all_gather(
        jnp.stack([expert_gate, expert_up, expert_down.reshape(expert_gate.shape)]),
        "req",
        axis=2,
        tiled=True,
    )
    gate_up = weights[:2]
    down_whole = (
        weights[2]
        .reshape((per_device, req_devices) + expert_gate.shape[1:])
        .reshape(per_device, req_devices * down_rows, expert_down.shape[2])
    )
    everyone = jnp.arange(request_order.shape[0], dtype=jnp.int32)
    request = jnp.sum(jnp.where(everyone == lax.axis_index("req"), request_order, 0))
    length = jnp.sum(jnp.where(everyone == request, cached_lengths, 0))
    rows_whole = gather_columns(own_rows)
    rows_f = rows_whole.astype(jnp.float32)
    normed = normalize(rows_f, attn_gain).astype(jnp.bfloat16)
    query = jnp.dot(normed, w_query, preferred_element_type=jnp.float32)
    key_new = jnp.dot(normed, w_key, preferred_element_type=jnp.float32)
    value_new = jnp.dot(normed, w_value, preferred_element_type=jnp.float32)
    positions = length + jnp.arange(new_rows, dtype=jnp.int32)
    query = rotate(
        query.reshape(new_rows, heads_local, head_dim).transpose(1, 0, 2), positions
    ).astype(jnp.bfloat16) * jnp.asarray(head_dim ** (-0.5), jnp.bfloat16)
    key_new = rotate(
        key_new.reshape(new_rows, kv_local, head_dim).transpose(1, 0, 2), positions
    ).astype(jnp.bfloat16)
    value_new = (
        value_new.reshape(new_rows, kv_local, head_dim).transpose(1, 0, 2).astype(jnp.bfloat16)
    )
    zero = jnp.zeros((), jnp.int32)
    keys = lax.dynamic_update_slice(key_cache[0], key_new, (zero, length, zero))
    values = lax.dynamic_update_slice(value_cache[0], value_new, (zero, length, zero))
    half = new_rows // 2
    query = query.reshape(kv_local, group, new_rows, head_dim)
    key_cache_t = jnp.swapaxes(key_cache[0], 1, 2)
    value_cache_t = jnp.swapaxes(value_cache[0], 1, 2)
    key_new_t = jnp.swapaxes(key_new, 1, 2)
    value_new_t = jnp.swapaxes(value_new, 1, 2)
    head_sums = []
    for first in (0, half):
        part_query = query[:, :, first : first + half].reshape(kv_local, group * half, head_dim)
        attended = flash_attend(
            part_query,
            key_cache_t,
            value_cache_t,
            key_new_t,
            value_new_t,
            length,
            first,
            half,
        )
        attended = (
            attended.reshape(heads_local, half, head_dim)
            .transpose(1, 0, 2)
            .reshape(half, heads_local * head_dim)
        )
        head_part = jnp.dot(attended, w_out, preferred_element_type=jnp.float32).astype(
            jnp.bfloat16
        )
        head_sums.append(sum_over_ep(head_part))
    head_sum = jnp.concatenate(head_sums, 0)
    mixed_f = (rows_f + head_sum).astype(jnp.bfloat16).astype(jnp.float32)
    ffn_normed = normalize(mixed_f, ffn_gain).astype(jnp.bfloat16)
    table, gate_slot = route_tables(
        expert_ids[0],
        gate_values[0],
        me * per_device + jnp.arange(per_device, dtype=jnp.int32),
        capacity,
    )
    dispatched = jnp.einsum(
        "ect,td->ecd", table, ffn_normed, preferred_element_type=jnp.float32
    ).astype(jnp.bfloat16)
    gate_up, dispatched = lax.optimization_barrier((gate_up, dispatched))
    both = jnp.einsum("ecd,kedf->kecf", dispatched, gate_up, preferred_element_type=jnp.float32)
    act = (jax.nn.silu(both[0]) * both[1]).astype(jnp.bfloat16)
    down_whole, act = lax.optimization_barrier((down_whole, act))
    devices = lax.axis_size("ep")

    def expert_block(target):
        down_block = lax.dynamic_slice_in_dim(down_whole, target * own_width, own_width, 2)
        output = jnp.einsum("ecf,efd->ecd", act, down_block, preferred_element_type=jnp.float32)
        contrib = (output * gate_slot[..., None]).astype(jnp.bfloat16)
        return jnp.einsum(
            "ect,ecd->td", table, contrib, preferred_element_type=jnp.float32
        ).astype(jnp.bfloat16)

    received = [shifted(expert_block((me + shift) % devices), shift) for shift in range(1, devices)]
    expert_sum = expert_block(me).astype(jnp.float32)
    for piece in received:
        expert_sum = expert_sum + piece.astype(jnp.float32)
    mixed_own = lax.dynamic_slice_in_dim(mixed_f, me * own_width, own_width, 1)
    result = (mixed_own + expert_sum).astype(jnp.bfloat16)
    return (result[None], keys[None], values[None])


def solution(mesh):
    in_specs = (
        P("req", None, "ep"),
        P("req", "ep", None, None),
        P("req", "ep", None, None),
        P(),
        P(),
        P("req", None, None),
        P("req", None, None),
        P(),
        P(),
        P(None, "ep"),
        P(None, "ep"),
        P(None, "ep"),
        P("ep", None),
        P("ep", "req", None),
        P("ep", "req", None),
        P("ep", "req", None),
    )
    out_specs = (P("req", None, "ep"), P("req", "ep", None, None), P("req", "ep", None, None))
    return jax.shard_map(
        on_device, mesh=mesh, in_specs=in_specs, out_specs=out_specs, check_vma=False
    )
```

```python
import jax
import jax.numpy as jnp
from jax import lax
from jax.experimental import pallas as pl
from jax.experimental.pallas import tpu as pltpu
from jax.sharding import PartitionSpec as P

epsilon = 1e-06


def normalize(values, gain):
    return values * lax.rsqrt(jnp.mean(values * values, -1, keepdims=True) + epsilon) * gain


def rotate(values, positions):
    half = values.shape[-1] // 2
    freq = 10000.0 ** (-jnp.arange(half, dtype=jnp.float32) * (2.0 / values.shape[-1]))
    angle = positions.astype(jnp.float32)[:, None] * freq[None, :]
    cosine = jnp.cos(angle)
    sine = jnp.sin(angle)
    first = values[..., :half]
    second = values[..., half:]
    return jnp.concatenate([first * cosine - second * sine, second * cosine + first * sine], -1)


def rounded(values):
    return lax.optimization_barrier(values.astype(jnp.bfloat16)).astype(jnp.float32)


def route_tables(chosen, gate_rows, wanted, capacity):
    hits = chosen[:, :, None] == wanted[None, None, :]
    member = jnp.sum(hits.astype(jnp.int32), 1, dtype=jnp.int32)
    weight = jnp.sum(jnp.where(hits, gate_rows[:, :, None], 0.0), 1)
    place = jnp.cumsum(member, 0, dtype=jnp.int32) - 1
    slots = jnp.arange(capacity, dtype=jnp.int32)
    table = (member.T[:, None, :] == 1) & (place.T[:, None, :] == slots[None, :, None])
    gate_slot = jnp.sum(jnp.where(table, weight.T[:, None, :], 0.0), 2)
    return (table.astype(jnp.bfloat16), gate_slot)


def flash_attend(query, keys, values, key_new, value_new, length, first_token, tokens):
    kv_heads, rows, head_dim = query.shape
    block = key_new.shape[2]
    cached = keys.shape[2] - block
    wide = cached if cached % block == 0 else block
    blocks = 1 + cached // wide
    seen = first_token + tokens if (first_token + tokens) % 128 == 0 else block

    def cached_blocks(length_ref):
        return (length_ref[0] + wide - 1) // wide

    def kernel(length_ref, q_ref, kc_ref, vc_ref, kn_ref, vn_ref, o_ref, m_sc, l_sc, acc_sc):
        step = pl.program_id(1)
        length = length_ref[0]

        def visit(key_block, value_block, visible, first):
            scores = jnp.dot(q_ref[0], key_block, preferred_element_type=jnp.float32)
            if visible is not None:
                scores = jnp.where(visible, scores, -1e30)
            if first:
                highest = jnp.max(scores, -1, keepdims=True)
            else:
                previous = m_sc[...]
                highest = jnp.maximum(previous, jnp.max(scores, -1, keepdims=True))
            probs = jnp.exp(scores - highest)
            if visible is not None:
                probs = jnp.where(visible, probs, 0.0)
            summed = lax.dot_general(
                probs.astype(jnp.bfloat16),
                value_block,
                (((1,), (1,)), ((), ())),
                preferred_element_type=jnp.float32,
            )
            if first:
                l_sc[...] = jnp.sum(probs, -1, keepdims=True)
                acc_sc[...] = summed
            else:
                correction = jnp.exp(previous - highest)
                l_sc[...] = l_sc[...] * correction + jnp.sum(probs, -1, keepdims=True)
                acc_sc[...] = acc_sc[...] * correction + summed
            m_sc[...] = highest

        @pl.when(step == 0)
        def _():
            shape = (rows, seen)
            column = lax.broadcasted_iota(jnp.int32, shape, 1)
            token = first_token + lax.rem(lax.broadcasted_iota(jnp.int32, shape, 0), tokens)
            visit(kn_ref[0], vn_ref[0], column <= token, True)

        column = lax.broadcasted_iota(jnp.int32, (rows, wide), 1)
        start = (step - 1) * wide

        whole = (step > 0) & (start + wide <= length)

        @pl.when(whole)
        def _():
            visit(kc_ref[0], vc_ref[0], None, False)

        @pl.when((step > 0) & jnp.logical_not(whole) & (start < length))
        def _():
            visit(kc_ref[0], vc_ref[0], column + start < length, False)

        @pl.when(step == blocks - 1)
        def _():
            o_ref[0] = (acc_sc[...] / l_sc[...]).astype(o_ref.dtype)

    def cache_map(head, step, length_ref):
        return (head, 0, jnp.clip(step - 1, 0, cached_blocks(length_ref) - 1))

    def fixed_map(head, step, length_ref):
        return (head, 0, 0)

    grid_spec = pltpu.PrefetchScalarGridSpec(
        num_scalar_prefetch=1,
        grid=(kv_heads, blocks),
        in_specs=[
            pl.BlockSpec((1, rows, head_dim), fixed_map),
            pl.BlockSpec((1, head_dim, wide), cache_map),
            pl.BlockSpec((1, head_dim, wide), cache_map),
            pl.BlockSpec((1, head_dim, seen), fixed_map),
            pl.BlockSpec((1, head_dim, seen), fixed_map),
        ],
        out_specs=pl.BlockSpec((1, rows, head_dim), fixed_map),
        scratch_shapes=[
            pltpu.VMEM((rows, 1), jnp.float32),
            pltpu.VMEM((rows, 1), jnp.float32),
            pltpu.VMEM((rows, head_dim), jnp.float32),
        ],
    )
    flops = 4 * kv_heads * rows * keys.shape[2] * head_dim
    return pl.pallas_call(
        kernel,
        grid_spec=grid_spec,
        out_shape=jax.ShapeDtypeStruct(query.shape, jnp.bfloat16),
        compiler_params=pltpu.CompilerParams(dimension_semantics=("arbitrary", "arbitrary")),
        cost_estimate=pl.CostEstimate(
            flops=flops,
            transcendentals=kv_heads * rows * keys.shape[2],
            bytes_accessed=2 * (query.size + keys.size + values.size + query.size),
        ),
    )(length.reshape(1), query, keys, values, key_new, value_new)


def shifted(values, shift):
    devices = lax.axis_size("ep")
    return lax.ppermute(values, "ep", [(i, (i + shift) % devices) for i in range(devices)])


def gather_columns(values):
    devices = lax.axis_size("ep")
    me = lax.axis_index("ep")
    width = values.shape[-1]
    whole = jnp.zeros(values.shape[:-1] + (width * devices,), values.dtype)
    for shift in range(devices):
        piece = values if shift == 0 else shifted(values, shift)
        source = (me - shift) % devices
        whole = lax.dynamic_update_slice_in_dim(whole, piece, source * width, values.ndim - 1)
    return whole


def sum_over_ep(part):
    devices = lax.axis_size("ep")
    total = part.astype(jnp.float32)
    for shift in range(1, devices):
        total = total + shifted(part, shift).astype(jnp.float32)
    return total


def on_device(
    hidden,
    key_cache,
    value_cache,
    request_order,
    cached_lengths,
    expert_ids,
    gate_values,
    attn_gain,
    ffn_gain,
    w_query,
    w_key,
    w_value,
    w_out,
    expert_gate,
    expert_up,
    expert_down,
):
    own_rows = hidden[0]
    new_rows = own_rows.shape[0]
    own_width = own_rows.shape[1]
    head_dim = key_cache.shape[3]
    kv_local = key_cache.shape[1]
    heads_local = w_query.shape[1] // head_dim
    group = heads_local // kv_local
    per_device = expert_gate.shape[0]
    capacity = 3 * new_rows // 8
    me = lax.axis_index("ep")
    gate_up = lax.all_gather(jnp.stack([expert_gate, expert_up]), "req", axis=2, tiled=True)
    down_whole = lax.all_gather(expert_down, "req", axis=1, tiled=True)
    everyone = jnp.arange(request_order.shape[0], dtype=jnp.int32)
    request = jnp.sum(jnp.where(everyone == lax.axis_index("req"), request_order, 0))
    length = jnp.sum(jnp.where(everyone == request, cached_lengths, 0))
    rows_whole = gather_columns(own_rows)
    rows_f = rows_whole.astype(jnp.float32)
    normed = normalize(rows_f, attn_gain).astype(jnp.bfloat16)
    query = jnp.dot(normed, w_query, preferred_element_type=jnp.float32)
    key_new = jnp.dot(normed, w_key, preferred_element_type=jnp.float32)
    value_new = jnp.dot(normed, w_value, preferred_element_type=jnp.float32)
    positions = length + jnp.arange(new_rows, dtype=jnp.int32)
    query = rotate(
        query.reshape(new_rows, heads_local, head_dim).transpose(1, 0, 2), positions
    ).astype(jnp.bfloat16) * jnp.asarray(head_dim ** (-0.5), jnp.bfloat16)
    key_new = rotate(
        key_new.reshape(new_rows, kv_local, head_dim).transpose(1, 0, 2), positions
    ).astype(jnp.bfloat16)
    value_new = (
        value_new.reshape(new_rows, kv_local, head_dim).transpose(1, 0, 2).astype(jnp.bfloat16)
    )
    zero = jnp.zeros((), jnp.int32)
    keys = lax.dynamic_update_slice(key_cache[0], key_new, (zero, length, zero))
    values = lax.dynamic_update_slice(value_cache[0], value_new, (zero, length, zero))
    half = new_rows // 2
    query = query.reshape(kv_local, group, new_rows, head_dim)
    key_cache_t = jnp.swapaxes(key_cache[0], 1, 2)
    value_cache_t = jnp.swapaxes(value_cache[0], 1, 2)
    key_new_t = jnp.swapaxes(key_new, 1, 2)
    value_new_t = jnp.swapaxes(value_new, 1, 2)
    head_sums = []
    for first in (0, half):
        part_query = query[:, :, first : first + half].reshape(kv_local, group * half, head_dim)
        attended = flash_attend(
            part_query,
            key_cache_t,
            value_cache_t,
            key_new_t,
            value_new_t,
            length,
            first,
            half,
        )
        attended = (
            attended.reshape(heads_local, half, head_dim)
            .transpose(1, 0, 2)
            .reshape(half, heads_local * head_dim)
        )
        head_part = jnp.dot(attended, w_out, preferred_element_type=jnp.float32).astype(
            jnp.bfloat16
        )
        head_sums.append(sum_over_ep(head_part))
    head_sum = jnp.concatenate(head_sums, 0)
    mixed_f = (rows_f + head_sum).astype(jnp.bfloat16).astype(jnp.float32)
    ffn_normed = normalize(mixed_f, ffn_gain).astype(jnp.bfloat16)
    table, gate_slot = route_tables(
        expert_ids[0],
        gate_values[0],
        me * per_device + jnp.arange(per_device, dtype=jnp.int32),
        capacity,
    )
    dispatched = jnp.einsum(
        "ect,td->ecd", table, ffn_normed, preferred_element_type=jnp.float32
    ).astype(jnp.bfloat16)
    gate_up, dispatched = lax.optimization_barrier((gate_up, dispatched))
    both = jnp.einsum("ecd,kedf->kecf", dispatched, gate_up, preferred_element_type=jnp.float32)
    act = (jax.nn.silu(both[0]) * both[1]).astype(jnp.bfloat16)
    down_whole, act = lax.optimization_barrier((down_whole, act))
    devices = lax.axis_size("ep")

    def expert_block(target):
        down_block = lax.dynamic_slice_in_dim(down_whole, target * own_width, own_width, 2)
        output = jnp.einsum("ecf,efd->ecd", act, down_block, preferred_element_type=jnp.float32)
        contrib = (output * gate_slot[..., None]).astype(jnp.bfloat16)
        return jnp.einsum(
            "ect,ecd->td", table, contrib, preferred_element_type=jnp.float32
        ).astype(jnp.bfloat16)

    received = [shifted(expert_block((me + shift) % devices), shift) for shift in range(1, devices)]
    expert_sum = expert_block(me).astype(jnp.float32)
    for piece in received:
        expert_sum = expert_sum + piece.astype(jnp.float32)
    mixed_own = lax.dynamic_slice_in_dim(mixed_f, me * own_width, own_width, 1)
    result = (mixed_own + expert_sum).astype(jnp.bfloat16)
    return (result[None], keys[None], values[None])


def solution(mesh):
    in_specs = (
        P("req", None, "ep"),
        P("req", "ep", None, None),
        P("req", "ep", None, None),
        P(),
        P(),
        P("req", None, None),
        P("req", None, None),
        P(),
        P(),
        P(None, "ep"),
        P(None, "ep"),
        P(None, "ep"),
        P("ep", None),
        P("ep", "req", None),
        P("ep", "req", None),
        P("ep", "req", None),
    )
    out_specs = (P("req", None, "ep"), P("req", "ep", None, None), P("req", "ep", None, None))
    return jax.shard_map(
        on_device, mesh=mesh, in_specs=in_specs, out_specs=out_specs, check_vma=False
    )
```
